128 devices in a mesh: det: 8 (over x, core), tm: 16 (over z, y).
Axes of the slice: x: 4, y: 4, z: 4, core: 2. Of those that a mesh axis runs over, the one named last changes fastest.
Arguments:
- samples: float32 [32, 1024, 128], P('det', 'tm'), may hold values from -6 to 6
- pointing: bfloat16 [32, 1024, 128, 128], P('det', 'tm'), may hold values from -0.25 to 0.25
- pix_block: int32 [32, 1024], P('det', 'tm'), may hold values from 0 to 8191, as said below
- det_weight: float32 [32], P('det'), may hold values from 0.5 to 2
- start_map: float32 [128, 8192], P(('det', 'tm')), may hold values from -6 to 6
- legendre: bfloat16 [1024, 6144, 128], P(('det', 'tm')), may hold values from -0.5 to 0.5
- prior_gain: float32 [6144], replicated, may hold values from 0.3 to 3
- m_values: int32 [1024], replicated, may hold values from 0 to 4095, as said below
- cycle_offset: int32 [128], P(('det', 'tm')), may hold values from 0 to 8191
Outputs:
- final_map: float32 [128, 8192], P(('det', 'tm'))
The draws below stay inside these ranges and needn't reach their ends.
Inputs may be any that keep to these rules, and one draw needn't show every extreme that they name: `m_values`: strictly increasing; entry k lies in k * 4 to (k + 1) * 4 - 1, the first is 0 and the last is 4095. `pix_block`: the cycle owner of block b is the device holding cycle b // 64 of the map; among the 4 x 64 sample blocks of one device, at most 8 name blocks of any one owner, and on every device some owner gets exactly 8.
All inputs are finite; a program needn't handle non-finite values.
Results may differ from the reference program's by a relative error of at most 0.0042.
Values may be sent and summed in bfloat16 or wider, within the bound.
No kernel may reach another device: no remote copies, remote signals or barrier semaphores. Data moves between devices by JAX's collectives and lax.ppermute only.
A program may use at most 128 MiB of HBM per device.

```python
import math
import jax
import jax.numpy as jnp
from jax import lax

RLEN = 8192
L = 6144
ITERS = 2
CAP = 8
DET_DEV = 4
TB_DEV = 64
NRING = 128
NPB = 8192
M = 1024
STRIDE = 4
DETS = 32
TIMEB = 1024


def draw_m_values(key, part):
    jitter = jax.random.randint(key, (M,), 0, STRIDE, dtype=jnp.int32)
    jitter = jitter.at[0].set(0).at[M - 1].set(STRIDE - 1)
    return jnp.arange(M, dtype=jnp.int32) * STRIDE + jitter


def draw_pix_block(key, part):
    det_groups = DETS // DET_DEV
    time_groups = TIMEB // TB_DEV
    owners = det_groups * time_groups
    per_device = DET_DEV * TB_DEV
    per_owner = NPB // owners
    hot_count = max(1, per_device // (4 * CAP))
    key_rank = jax.random.fold_in(key, 11)
    key_noise = jax.random.fold_in(key, 12)
    key_order = jax.random.fold_in(key, 13)
    key_within = jax.random.fold_in(key, 14)
    rank_keys = jax.random.split(key_rank, owners)
    owner_rank = jax.vmap(lambda k: jax.random.permutation(k, owners))(rank_keys)
    boost = jnp.where(owner_rank < hot_count, 8192, 0).astype(jnp.int32)
    noise = jax.random.randint(key_noise, (owners, owners, CAP), 0, 4096, dtype=jnp.int32)
    score = (noise + boost[:, :, None]).reshape(owners, owners * CAP)
    slot_index = jnp.arange(owners * CAP, dtype=jnp.int32)[None, :]
    distinct = score * (owners * CAP) + slot_index
    top_scores, chosen = lax.top_k(distinct, per_device)
    target = chosen.astype(jnp.int32) // CAP
    order_keys = jax.random.split(key_order, owners)
    order = jax.vmap(lambda k: jax.random.permutation(k, per_device))(order_keys)
    target = jnp.take_along_axis(target, order, axis=1)
    within = jax.random.randint(key_within, (owners, per_device), 0, per_owner, dtype=jnp.int32)
    blocks = target * per_owner + within
    blocks = blocks.reshape(det_groups, time_groups, DET_DEV, TB_DEV)
    return blocks.transpose(0, 2, 1, 3).reshape(DETS, TIMEB)


def touch_ends(drawn, rng, least, largest):
    index_at = [jax.random.randint(jax.random.fold_in(rng, axis), (), 0, length) for axis, length in enumerate(drawn.shape)]
    widest = drawn.shape.index(max(drawn.shape))
    neighbour = index_at[:widest] + [(index_at[widest] + 1) % drawn.shape[widest]] + index_at[widest + 1:]
    return drawn.at[tuple(index_at)].set(least).at[tuple(neighbour)].set(largest)


def level_of(key, dims, pieces, smallest, top_value):
    def one(position, blocks):
        steps = jax.random.uniform(jax.random.fold_in(jax.random.fold_in(key, 6), position), (blocks,), jnp.float32, smallest / len(pieces), top_value / len(pieces))
        return jnp.repeat(jnp.exp(steps), dims[position] // blocks).reshape((-1,) + (1,) * (len(dims) - position - 1))

    level = one(*pieces[0])
    for cut in pieces[1:]:
        level = level * one(*cut)
    return level


def bell_draw(rng, shape, scale, most, pieces=(), kind=jnp.bfloat16):
    array = jax.random.normal(rng, shape, jnp.float32) * scale
    if len(pieces) > 0:
        array = level_of(rng, shape, pieces, -0.22, 0.18) * array
    return jnp.clip(array, min=-most, max=most).astype(kind)


def setup_inputs(seed: int = 0) -> dict:
    streams_of = jax.random.split(jax.random.key(seed), 10)
    return {
        "samples": bell_draw(streams_of[0], (DETS, TIMEB, 128), 1.0, 6.0, ((0, 8), (1, 16)), jnp.float32),
        "pointing": bell_draw(streams_of[1], (DETS, TIMEB, 128, 128), 512 ** -0.5, 0.25, ((0, 8), (1, 16))),
        "pix_block": draw_pix_block(jax.random.fold_in(streams_of[9], 71), 0),
        "det_weight": jnp.clip(jnp.exp(math.log(2.0) - 1.3862944 * jax.random.uniform(streams_of[3], (DETS,), jnp.float32) ** level_of(streams_of[3], (DETS,), ((0, 8),), -0.2, 0.2)), 0.5, 2.0),
        "start_map": bell_draw(streams_of[4], (NRING, RLEN), 1.0, 6.0, ((0, 128),), jnp.float32),
        "legendre": bell_draw(streams_of[5], (M, L, NRING), NRING ** -0.5, 0.5, ((0, 128),)),
        "prior_gain": jnp.clip(jnp.exp(jax.random.uniform(streams_of[6], (L,), jnp.float32, math.log(0.3), math.log(3.0))), 0.3, 3.0),
        "m_values": draw_m_values(jax.random.fold_in(streams_of[9], 71), 0),
        "cycle_offset": touch_ends(jax.random.randint(streams_of[8], (NRING,), 0, RLEN), jax.random.fold_in(streams_of[8], 1), 0, RLEN - 1).astype(jnp.int32),
    }


def harmonic_filter(field, legendre, prior_gain, m_values, cycle_offset):
    cycles, length = field.shape
    count = m_values.shape[0]
    degrees = legendre.shape[1]
    spectrum = jnp.fft.fft(field, axis=1)[:, m_values]
    phases = (m_values[None, :] * cycle_offset[:, None] % length).astype(jnp.float32) * (2.0 * math.pi / length)
    cos_phase = jnp.cos(phases)
    sin_phase = jnp.sin(phases)
    norm_factor = 1.0 / math.sqrt(length)
    coef_re = ((jnp.real(spectrum) * cos_phase + jnp.imag(spectrum) * sin_phase) * norm_factor).astype(jnp.bfloat16)
    coef_im = ((jnp.imag(spectrum) * cos_phase - jnp.real(spectrum) * sin_phase) * norm_factor).astype(jnp.bfloat16)
    columns = jnp.stack([coef_re.T, coef_im.T], axis=1)
    degree = jnp.arange(degrees, dtype=jnp.int32)

    def per_mode(packed):
        table, m_value, column = packed
        table_wide = table.astype(jnp.float32)
        analysed = jnp.einsum('lr,cr->cl', table_wide, column.astype(jnp.float32))
        scaled = jnp.where(degree[None, :] >= m_value, analysed * prior_gain[None, :], 0.0).astype(jnp.bfloat16)
        return jnp.einsum('lr,cl->cr', table_wide, scaled.astype(jnp.float32))
    synth = lax.map(per_mode, (legendre, m_values, columns)) * math.sqrt(cycles / degrees)
    back_re = synth[:, 0, :].T
    back_im = synth[:, 1, :].T
    mode_weight = jnp.where(m_values == 0, 1.0, 2.0)[None, :]
    harm_re = mode_weight * (back_re * cos_phase - back_im * sin_phase)
    harm_im = mode_weight * (back_re * sin_phase + back_im * cos_phase)
    full_spec = jnp.zeros((cycles, length), dtype=spectrum.dtype).at[:, m_values].set(harm_re + 1j * harm_im)
    return jnp.real(jnp.fft.ifft(full_spec, axis=1)) * (length / math.sqrt(2.0 * count))

def reference(samples, pointing, pix_block, det_weight, start_map, legendre, prior_gain, m_values, cycle_offset):
    cycles, length = start_map.shape
    per_cycle = length // 128
    nblocks = cycles * per_cycle
    flat_pix = pix_block.reshape(-1)
    hit_terms = jnp.broadcast_to(det_weight[:, None], pix_block.shape).reshape(-1)
    hit_weight = jnp.zeros((nblocks,), jnp.float32).at[flat_pix].add(hit_terms)
    divisor = jnp.repeat(1.0 + 0.25 * hit_weight.reshape(cycles, per_cycle), 128, axis=1)
    current = start_map
    for iteration in range(ITERS):
        map_half = current.astype(jnp.bfloat16).reshape(nblocks, 128)

        def bin_detector(packed):
            point, pixels, weight, signal = packed
            point_wide = point.astype(jnp.float32)
            picked = map_half[pixels].astype(jnp.float32)
            predicted = jnp.einsum('tsp,tp->ts', point_wide, picked)
            weighted_resid = (weight * (signal - predicted)).astype(jnp.bfloat16)
            return jnp.einsum('tsp,ts->tp', point_wide, weighted_resid.astype(jnp.float32))
        binned_terms = lax.map(bin_detector, (pointing, pix_block, det_weight, samples))
        binned = jnp.zeros((nblocks, 128), jnp.float32).at[flat_pix].add(binned_terms.reshape(-1, 128))
        filtered = harmonic_filter(current, legendre, prior_gain, m_values, cycle_offset)
        current = current + (binned.reshape(cycles, length) - filtered) / divisor
    return current
```

```python
import math

import jax
import jax.numpy as jnp
from jax import lax
from jax.sharding import PartitionSpec as P

ITERS = 2


highest = lax.Precision.HIGHEST


def phase_pair(first_len, second_len, length, sign):
    first = jnp.arange(first_len, dtype=jnp.int32)[:, None]
    second = jnp.arange(second_len, dtype=jnp.int32)[None, :]
    phases = (first * second % length).astype(jnp.float32) * (sign * 2.0 * math.pi / length)
    return (jnp.cos(phases), jnp.sin(phases))


def forward_cycles(field):
    cycles, length = field.shape
    outer_len = length // 128
    shaped = field.reshape(cycles, outer_len, 128)
    cos_outer, sin_outer = phase_pair(outer_len, outer_len, outer_len, -1.0)
    part_re = jnp.einsum("mj,rjk->rmk", cos_outer, shaped, precision=highest)
    part_im = jnp.einsum("mj,rjk->rmk", sin_outer, shaped, precision=highest)
    cos_twist, sin_twist = phase_pair(outer_len, 128, length, -1.0)
    twist_re = part_re * cos_twist - part_im * sin_twist
    twist_im = part_re * sin_twist + part_im * cos_twist
    cos_inner, sin_inner = phase_pair(128, 128, 128, -1.0)
    spec_re = jnp.einsum("rmk,kn->rmn", twist_re, cos_inner, precision=highest) - jnp.einsum(
        "rmk,kn->rmn", twist_im, sin_inner, precision=highest
    )
    spec_im = jnp.einsum("rmk,kn->rmn", twist_re, sin_inner, precision=highest) + jnp.einsum(
        "rmk,kn->rmn", twist_im, cos_inner, precision=highest
    )
    return (spec_re.reshape(cycles, length), spec_im.reshape(cycles, length))


def inverse_cycles(spec_re, spec_im):
    cycles, length = spec_re.shape
    outer_len = length // 128
    shaped_re = spec_re.reshape(cycles, outer_len, 128)
    shaped_im = spec_im.reshape(cycles, outer_len, 128)
    cos_inner, sin_inner = phase_pair(128, 128, 128, 1.0)
    inner_re = jnp.einsum("rmn,nk->rmk", shaped_re, cos_inner, precision=highest) - jnp.einsum(
        "rmn,nk->rmk", shaped_im, sin_inner, precision=highest
    )
    inner_im = jnp.einsum("rmn,nk->rmk", shaped_re, sin_inner, precision=highest) + jnp.einsum(
        "rmn,nk->rmk", shaped_im, cos_inner, precision=highest
    )
    cos_twist, sin_twist = phase_pair(outer_len, 128, length, 1.0)
    twist_re = inner_re * cos_twist - inner_im * sin_twist
    twist_im = inner_re * sin_twist + inner_im * cos_twist
    cos_outer, sin_outer = phase_pair(outer_len, outer_len, outer_len, 1.0)
    field = jnp.einsum("jm,rmk->rjk", cos_outer, twist_re, precision=highest) - jnp.einsum(
        "jm,rmk->rjk", sin_outer, twist_im, precision=highest
    )
    return field.reshape(cycles, length)


def legendre_filter(owned, legendre, prior_gain, m_own):
    count_here, degrees, total_cycles = legendre.shape
    block_rows = min(512, degrees)

    def one_block(index, running):
        start = index * block_rows
        table = lax.dynamic_slice_in_dim(legendre, start, block_rows, 1)
        analysed = jnp.einsum("mlr,cmr->cml", table, owned, preferred_element_type=jnp.float32)
        degree = start + jnp.arange(block_rows, dtype=jnp.int32)
        keep_rows = degree[None, :] >= m_own[:, None]
        gain_block = lax.dynamic_slice_in_dim(prior_gain, start, block_rows)
        scaled = jnp.where(keep_rows[None], analysed * gain_block, 0.0).astype(jnp.bfloat16)
        return running + jnp.einsum(
            "mlr,cml->cmr", table, scaled, preferred_element_type=jnp.float32
        )

    first_block = 0
    initial = jnp.zeros(owned.shape, jnp.float32)
    summed = lax.fori_loop(first_block, degrees // block_rows, one_block, initial)
    return summed * math.sqrt(total_cycles / degrees)


CAP = 8


def spectrum_out(field, m_values, cycle_offset):
    cycles_here, length = field.shape
    outer_len = length // 128
    spectrum_slot = m_values % outer_len * 128 + m_values // outer_len
    spec_re, spec_im = forward_cycles(field)
    pick_re = spec_re[:, spectrum_slot]
    pick_im = spec_im[:, spectrum_slot]
    phases = (m_values[None, :] * cycle_offset[:, None] % length).astype(jnp.float32) * (
        2.0 * math.pi / length
    )
    cos_phase = jnp.cos(phases)
    sin_phase = jnp.sin(phases)
    norm_factor = 1.0 / math.sqrt(length)
    coef_re = (pick_re * cos_phase + pick_im * sin_phase) * norm_factor
    coef_im = (pick_im * cos_phase - pick_re * sin_phase) * norm_factor
    return coef_re, coef_im, cos_phase, sin_phase


def spectrum_back(back_re, back_im, cos_phase, sin_phase, m_values, length):
    cycles_here = back_re.shape[0]
    count = m_values.shape[0]
    outer_len = length // 128
    spectrum_slot = m_values % outer_len * 128 + m_values // outer_len
    mode_weight = jnp.where(m_values == 0, 1.0, 2.0).astype(jnp.float32)[None, :]
    harm_re = mode_weight * (back_re * cos_phase - back_im * sin_phase)
    harm_im = mode_weight * (back_re * sin_phase + back_im * cos_phase)
    full_re = jnp.zeros((cycles_here, length), jnp.float32).at[:, spectrum_slot].set(harm_re)
    full_im = jnp.zeros((cycles_here, length), jnp.float32).at[:, spectrum_slot].set(harm_im)
    return inverse_cycles(full_re, full_im) / math.sqrt(2.0 * count)


def on_device(
    samples,
    pointing,
    pix_block,
    det_weight,
    start_map,
    legendre,
    prior_gain,
    m_values,
    cycle_offset,
):
    axes = ("det", "tm")
    cycles_here, length = start_map.shape
    per_cycle = length // 128
    owners = lax.axis_size(axes)
    total_cycles = cycles_here * owners
    blocks_here = cycles_here * per_cycle
    count_here = legendre.shape[0]
    owner_index = lax.axis_index(axes)
    m_own = lax.dynamic_slice_in_dim(m_values, owner_index * count_here, count_here)
    slots = owners * CAP

    flat_pix = pix_block.reshape(-1)
    nloc = flat_pix.shape[0]
    owner_of = flat_pix // blocks_here
    within = flat_pix % blocks_here
    order = jnp.arange(nloc, dtype=jnp.int32)
    same = (owner_of[:, None] == owner_of[None, :]) & (order[None, :] < order[:, None])
    rank = jnp.sum(same.astype(jnp.int32), axis=1)
    slot = owner_of * CAP + rank
    weight_of = jnp.broadcast_to(det_weight[:, None], pix_block.shape).reshape(-1)
    index_send = jnp.zeros((slots,), jnp.float32).at[slot].set(within.astype(jnp.float32))
    weight_send = jnp.zeros((slots,), jnp.float32).at[slot].set(weight_of)
    info = jnp.stack([index_send, weight_send], axis=1).reshape(owners, CAP * 2)
    info_recv = lax.all_to_all(info, axes, 0, 0, tiled=True).reshape(slots, 2)
    want = info_recv[:, 0].astype(jnp.int32)
    want_hot = (want[None, :] == jnp.arange(blocks_here, dtype=jnp.int32)[:, None]).astype(jnp.float32)
    hit_weight = jnp.sum(want_hot * info_recv[None, :, 1], axis=1).reshape(cycles_here, per_cycle)
    divisor = jnp.repeat(1.0 + 0.25 * hit_weight, 128, axis=1)

    current = start_map
    for iteration in range(ITERS):
        map_half = current.astype(jnp.bfloat16).reshape(blocks_here, 128)
        rows_out = map_half[want].reshape(owners, CAP * 128)
        coef_re, coef_im, cos_phase, sin_phase = spectrum_out(current, m_values, cycle_offset)
        outward = jnp.stack([coef_re.T, coef_im.T]).astype(jnp.bfloat16)
        outward = outward.reshape(2, owners, count_here, cycles_here).transpose(1, 0, 2, 3)
        send_a = jnp.concatenate(
            [rows_out, outward.reshape(owners, 2 * count_here * cycles_here)], axis=1
        )
        recv_a = lax.all_to_all(send_a, axes, 0, 0, tiled=True)
        rows_in = recv_a[:, : CAP * 128].reshape(slots, 128)
        owned = recv_a[:, CAP * 128 :].reshape(owners, 2, count_here, cycles_here)
        owned = owned.transpose(1, 2, 0, 3).reshape(2, count_here, total_cycles)

        picked = rows_in[slot].reshape(pix_block.shape + (128,))
        predicted = jnp.einsum(
            "dtsp,dtp->dts", pointing, picked, preferred_element_type=jnp.float32
        )
        weighted_resid = (det_weight[:, None, None] * (samples - predicted)).astype(jnp.bfloat16)
        binned_terms = jnp.einsum(
            "dtsp,dts->dtp", pointing, weighted_resid, preferred_element_type=jnp.float32
        )
        binned_send = jnp.zeros((slots, 128), jnp.float32).at[slot].set(binned_terms.reshape(-1, 128))

        synth = legendre_filter(owned, legendre, prior_gain, m_own)
        synth_send = synth.reshape(2, count_here, owners, cycles_here).transpose(2, 0, 1, 3)
        send_b = jnp.concatenate(
            [binned_send.reshape(owners, CAP * 128), synth_send.reshape(owners, -1)], axis=1
        )
        recv_b = lax.all_to_all(send_b, axes, 0, 0, tiled=True)
        binned_in = recv_b[:, : CAP * 128].reshape(slots, 128)
        binned = jnp.dot(want_hot, binned_in, precision=highest).reshape(cycles_here, length)
        returned = recv_b[:, CAP * 128 :].reshape(owners, 2, count_here, cycles_here)
        returned = returned.transpose(1, 0, 2, 3).reshape(2, owners * count_here, cycles_here)
        filtered = spectrum_back(
            returned[0].T, returned[1].T, cos_phase, sin_phase, m_values, length
        )
        current = current + (binned - filtered) / divisor
    return current


def solution(mesh):
    placed = (
        P("det", "tm", None),
        P("det", "tm", None, None),
        P("det", "tm"),
        P("det"),
        P(("det", "tm"), None),
        P(("det", "tm"), None, None),
        P(),
        P(),
        P(("det", "tm")),
    )
    return jax.shard_map(
        on_device, mesh=mesh, in_specs=placed, out_specs=P(("det", "tm"), None), check_vma=False
    )
```

```python
import math

import jax
import jax.numpy as jnp
from jax import lax
from jax.sharding import PartitionSpec as P

ITERS = 2


highest = lax.Precision.HIGHEST


def phase_pair(first_len, second_len, length, sign):
    first = jnp.arange(first_len, dtype=jnp.int32)[:, None]
    second = jnp.arange(second_len, dtype=jnp.int32)[None, :]
    phases = (first * second % length).astype(jnp.float32) * (sign * 2.0 * math.pi / length)
    return (jnp.cos(phases), jnp.sin(phases))


def forward_cycles(field):
    cycles, length = field.shape
    outer_len = length // 128
    shaped = field.reshape(cycles, outer_len, 128)
    cos_outer, sin_outer = phase_pair(outer_len, outer_len, outer_len, -1.0)
    part_re = jnp.einsum("mj,rjk->rmk", cos_outer, shaped, precision=highest)
    part_im = jnp.einsum("mj,rjk->rmk", sin_outer, shaped, precision=highest)
    cos_twist, sin_twist = phase_pair(outer_len, 128, length, -1.0)
    twist_re = part_re * cos_twist - part_im * sin_twist
    twist_im = part_re * sin_twist + part_im * cos_twist
    cos_inner, sin_inner = phase_pair(128, 128, 128, -1.0)
    spec_re = jnp.einsum("rmk,kn->rmn", twist_re, cos_inner, precision=highest) - jnp.einsum(
        "rmk,kn->rmn", twist_im, sin_inner, precision=highest
    )
    spec_im = jnp.einsum("rmk,kn->rmn", twist_re, sin_inner, precision=highest) + jnp.einsum(
        "rmk,kn->rmn", twist_im, cos_inner, precision=highest
    )
    return (spec_re.reshape(cycles, length), spec_im.reshape(cycles, length))


def inverse_cycles(spec_re, spec_im):
    cycles, length = spec_re.shape
    outer_len = length // 128
    shaped_re = spec_re.reshape(cycles, outer_len, 128)
    shaped_im = spec_im.reshape(cycles, outer_len, 128)
    cos_inner, sin_inner = phase_pair(128, 128, 128, 1.0)
    inner_re = jnp.einsum("rmn,nk->rmk", shaped_re, cos_inner, precision=highest) - jnp.einsum(
        "rmn,nk->rmk", shaped_im, sin_inner, precision=highest
    )
    inner_im = jnp.einsum("rmn,nk->rmk", shaped_re, sin_inner, precision=highest) + jnp.einsum(
        "rmn,nk->rmk", shaped_im, cos_inner, precision=highest
    )
    cos_twist, sin_twist = phase_pair(outer_len, 128, length, 1.0)
    twist_re = inner_re * cos_twist - inner_im * sin_twist
    twist_im = inner_re * sin_twist + inner_im * cos_twist
    cos_outer, sin_outer = phase_pair(outer_len, outer_len, outer_len, 1.0)
    field = jnp.einsum("jm,rmk->rjk", cos_outer, twist_re, precision=highest) - jnp.einsum(
        "jm,rmk->rjk", sin_outer, twist_im, precision=highest
    )
    return field.reshape(cycles, length)


def legendre_filter(owned, legendre, prior_gain, m_own):
    count_here, degrees, total_cycles = legendre.shape
    block_rows = min(512, degrees)

    def one_block(index, running):
        start = index * block_rows
        table = lax.dynamic_slice_in_dim(legendre, start, block_rows, 1)
        analysed = jnp.einsum("mlr,cmr->cml", table, owned, preferred_element_type=jnp.float32)
        degree = start + jnp.arange(block_rows, dtype=jnp.int32)
        keep_rows = degree[None, :] >= m_own[:, None]
        gain_block = lax.dynamic_slice_in_dim(prior_gain, start, block_rows)
        scaled = jnp.where(keep_rows[None], analysed * gain_block, 0.0).astype(jnp.bfloat16)
        return running + jnp.einsum(
            "mlr,cml->cmr", table, scaled, preferred_element_type=jnp.float32
        )

    first_block = 0
    initial = jnp.zeros(owned.shape, jnp.float32)
    summed = lax.fori_loop(first_block, degrees // block_rows, one_block, initial)
    return summed * math.sqrt(total_cycles / degrees)


CAP = 8


STRIDE = 4


def order_pick(m_values):
    count = m_values.shape[0]
    offset = m_values - STRIDE * jnp.arange(count, dtype=jnp.int32)
    return offset[:, None] == jnp.arange(STRIDE, dtype=jnp.int32)[None, :]


def spectrum_out(field, m_values, cycle_offset):
    cycles_here, length = field.shape
    count = m_values.shape[0]
    spec_re, spec_im = forward_cycles(field)
    outer_len = length // 128
    spec_re = spec_re.reshape(cycles_here, outer_len, 128).transpose(0, 2, 1)
    spec_im = spec_im.reshape(cycles_here, outer_len, 128).transpose(0, 2, 1)
    pick = order_pick(m_values)[None]
    band = count * STRIDE
    spec_re = spec_re.reshape(cycles_here, length)[:, :band].reshape(cycles_here, count, STRIDE)
    spec_im = spec_im.reshape(cycles_here, length)[:, :band].reshape(cycles_here, count, STRIDE)
    pick_re = jnp.sum(jnp.where(pick, spec_re, 0.0), axis=2)
    pick_im = jnp.sum(jnp.where(pick, spec_im, 0.0), axis=2)
    phases = (m_values[None, :] * cycle_offset[:, None] % length).astype(jnp.float32) * (
        2.0 * math.pi / length
    )
    cos_phase = jnp.cos(phases)
    sin_phase = jnp.sin(phases)
    norm_factor = 1.0 / math.sqrt(length)
    coef_re = (pick_re * cos_phase + pick_im * sin_phase) * norm_factor
    coef_im = (pick_im * cos_phase - pick_re * sin_phase) * norm_factor
    return coef_re, coef_im, cos_phase, sin_phase


def spectrum_back(back_re, back_im, cos_phase, sin_phase, m_values, length):
    cycles_here = back_re.shape[0]
    count = m_values.shape[0]
    outer_len = length // 128
    mode_weight = jnp.where(m_values == 0, 1.0, 2.0).astype(jnp.float32)[None, :]
    harm_re = mode_weight * (back_re * cos_phase - back_im * sin_phase)
    harm_im = mode_weight * (back_re * sin_phase + back_im * cos_phase)
    pick = order_pick(m_values)[None]
    rest = ((0, 0), (0, length - count * STRIDE))
    full_re = jnp.where(pick, harm_re[:, :, None], 0.0).reshape(cycles_here, count * STRIDE)
    full_im = jnp.where(pick, harm_im[:, :, None], 0.0).reshape(cycles_here, count * STRIDE)
    full_re = jnp.pad(full_re, rest).reshape(cycles_here, 128, outer_len)
    full_im = jnp.pad(full_im, rest).reshape(cycles_here, 128, outer_len)
    full_re = full_re.transpose(0, 2, 1).reshape(cycles_here, length)
    full_im = full_im.transpose(0, 2, 1).reshape(cycles_here, length)
    return inverse_cycles(full_re, full_im) / math.sqrt(2.0 * count)


def on_device(
    samples,
    pointing,
    pix_block,
    det_weight,
    start_map,
    legendre,
    prior_gain,
    m_values,
    cycle_offset,
):
    axes = ("det", "tm")
    cycles_here, length = start_map.shape
    per_cycle = length // 128
    owners = lax.axis_size(axes)
    total_cycles = cycles_here * owners
    blocks_here = cycles_here * per_cycle
    count_here = legendre.shape[0]
    owner_index = lax.axis_index(axes)
    m_own = lax.dynamic_slice_in_dim(m_values, owner_index * count_here, count_here)
    slots = owners * CAP

    flat_pix = pix_block.reshape(-1)
    nloc = flat_pix.shape[0]
    owner_of = flat_pix // blocks_here
    within = flat_pix % blocks_here
    order = jnp.arange(nloc, dtype=jnp.int32)
    same = (owner_of[:, None] == owner_of[None, :]) & (order[None, :] < order[:, None])
    rank = jnp.sum(same.astype(jnp.int32), axis=1)
    slot = owner_of * CAP + rank
    weight_of = jnp.broadcast_to(det_weight[:, None], pix_block.shape).reshape(-1)
    index_send = jnp.zeros((slots,), jnp.float32).at[slot].set(within.astype(jnp.float32))
    weight_send = jnp.zeros((slots,), jnp.float32).at[slot].set(weight_of)
    info = jnp.stack([index_send, weight_send], axis=1).reshape(owners, CAP * 2)
    info_recv = lax.all_to_all(info, axes, 0, 0, tiled=True).reshape(slots, 2)
    want = info_recv[:, 0].astype(jnp.int32)
    want_hot = (want[None, :] == jnp.arange(blocks_here, dtype=jnp.int32)[:, None]).astype(jnp.float32)
    hit_weight = jnp.sum(want_hot * info_recv[None, :, 1], axis=1).reshape(cycles_here, per_cycle)
    divisor = jnp.repeat(1.0 + 0.25 * hit_weight, 128, axis=1)

    current = start_map
    for iteration in range(ITERS):
        map_half = current.astype(jnp.bfloat16).reshape(blocks_here, 128)
        rows_out = map_half[want].reshape(owners, CAP * 128)
        coef_re, coef_im, cos_phase, sin_phase = spectrum_out(current, m_values, cycle_offset)
        outward = jnp.stack([coef_re.T, coef_im.T]).astype(jnp.bfloat16)
        outward = outward.reshape(2, owners, count_here, cycles_here).transpose(1, 0, 2, 3)
        send_a = jnp.concatenate(
            [rows_out, outward.reshape(owners, 2 * count_here * cycles_here)], axis=1
        )
        recv_a = lax.all_to_all(send_a, axes, 0, 0, tiled=True)
        rows_in = recv_a[:, : CAP * 128].reshape(slots, 128)
        owned = recv_a[:, CAP * 128 :].reshape(owners, 2, count_here, cycles_here)
        owned = owned.transpose(1, 2, 0, 3).reshape(2, count_here, total_cycles)

        picked = rows_in[slot].reshape(pix_block.shape + (128,))
        predicted = jnp.einsum(
            "dtsp,dtp->dts", pointing, picked, preferred_element_type=jnp.float32
        )
        weighted_resid = (det_weight[:, None, None] * (samples - predicted)).astype(jnp.bfloat16)
        binned_terms = jnp.einsum(
            "dtsp,dts->dtp", pointing, weighted_resid, preferred_element_type=jnp.float32
        )
        binned_send = jnp.zeros((slots, 128), jnp.float32).at[slot].set(binned_terms.reshape(-1, 128))

        synth = legendre_filter(owned, legendre, prior_gain, m_own)
        synth_send = synth.reshape(2, count_here, owners, cycles_here).transpose(2, 0, 1, 3)
        send_b = jnp.concatenate(
            [binned_send.reshape(owners, CAP * 128), synth_send.reshape(owners, -1)], axis=1
        )
        recv_b = lax.all_to_all(send_b, axes, 0, 0, tiled=True)
        binned_in = recv_b[:, : CAP * 128].reshape(slots, 128)
        binned = jnp.dot(want_hot, binned_in, precision=highest).reshape(cycles_here, length)
        returned = recv_b[:, CAP * 128 :].reshape(owners, 2, count_here, cycles_here)
        returned = returned.transpose(1, 0, 2, 3).reshape(2, owners * count_here, cycles_here)
        filtered = spectrum_back(
            returned[0].T, returned[1].T, cos_phase, sin_phase, m_values, length
        )
        current = current + (binned - filtered) / divisor
    return current


def solution(mesh):
    placed = (
        P("det", "tm", None),
        P("det", "tm", None, None),
        P("det", "tm"),
        P("det"),
        P(("det", "tm"), None),
        P(("det", "tm"), None, None),
        P(),
        P(),
        P(("det", "tm")),
    )
    return jax.shard_map(
        on_device, mesh=mesh, in_specs=placed, out_specs=P(("det", "tm"), None), check_vma=False
    )
```

```python
import math

import functools

import jax
import jax.numpy as jnp
from jax import lax
from jax.experimental import pallas as pl
from jax.experimental.pallas import tpu as pltpu
from jax.sharding import PartitionSpec as P

ITERS = 2


highest = lax.Precision.HIGHEST


def phase_pair(first_len, second_len, length, sign):
    first = jnp.arange(first_len, dtype=jnp.int32)[:, None]
    second = jnp.arange(second_len, dtype=jnp.int32)[None, :]
    phases = (first * second % length).astype(jnp.float32) * (sign * 2.0 * math.pi / length)
    return (jnp.cos(phases), jnp.sin(phases))


def forward_cycles(field):
    cycles, length = field.shape
    outer_len = length // 128
    shaped = field.reshape(cycles, outer_len, 128)
    cos_outer, sin_outer = phase_pair(outer_len, outer_len, outer_len, -1.0)
    part_re = jnp.einsum("mj,rjk->rmk", cos_outer, shaped, precision=highest)
    part_im = jnp.einsum("mj,rjk->rmk", sin_outer, shaped, precision=highest)
    cos_twist, sin_twist = phase_pair(outer_len, 128, length, -1.0)
    twist_re = part_re * cos_twist - part_im * sin_twist
    twist_im = part_re * sin_twist + part_im * cos_twist
    cos_inner, sin_inner = phase_pair(128, 128, 128, -1.0)
    spec_re = jnp.einsum("rmk,kn->rmn", twist_re, cos_inner, precision=highest) - jnp.einsum(
        "rmk,kn->rmn", twist_im, sin_inner, precision=highest
    )
    spec_im = jnp.einsum("rmk,kn->rmn", twist_re, sin_inner, precision=highest) + jnp.einsum(
        "rmk,kn->rmn", twist_im, cos_inner, precision=highest
    )
    return (spec_re.reshape(cycles, length), spec_im.reshape(cycles, length))


def inverse_cycles(spec_re, spec_im):
    cycles, length = spec_re.shape
    outer_len = length // 128
    shaped_re = spec_re.reshape(cycles, outer_len, 128)
    shaped_im = spec_im.reshape(cycles, outer_len, 128)
    cos_inner, sin_inner = phase_pair(128, 128, 128, 1.0)
    inner_re = jnp.einsum("rmn,nk->rmk", shaped_re, cos_inner, precision=highest) - jnp.einsum(
        "rmn,nk->rmk", shaped_im, sin_inner, precision=highest
    )
    inner_im = jnp.einsum("rmn,nk->rmk", shaped_re, sin_inner, precision=highest) + jnp.einsum(
        "rmn,nk->rmk", shaped_im, cos_inner, precision=highest
    )
    cos_twist, sin_twist = phase_pair(outer_len, 128, length, 1.0)
    twist_re = inner_re * cos_twist - inner_im * sin_twist
    twist_im = inner_re * sin_twist + inner_im * cos_twist
    cos_outer, sin_outer = phase_pair(outer_len, outer_len, outer_len, 1.0)
    field = jnp.einsum("jm,rmk->rjk", cos_outer, twist_re, precision=highest) - jnp.einsum(
        "jm,rmk->rjk", sin_outer, twist_im, precision=highest
    )
    return field.reshape(cycles, length)


def legendre_filter(owned, legendre, prior_gain, m_own):
    count_here, degrees, total_cycles = legendre.shape
    block_rows = min(512, degrees)

    def one_block(index, running):
        start = index * block_rows
        table = lax.dynamic_slice_in_dim(legendre, start, block_rows, 1)
        analysed = jnp.einsum("mlr,cmr->cml", table, owned, preferred_element_type=jnp.float32)
        degree = start + jnp.arange(block_rows, dtype=jnp.int32)
        keep_rows = degree[None, :] >= m_own[:, None]
        gain_block = lax.dynamic_slice_in_dim(prior_gain, start, block_rows)
        scaled = jnp.where(keep_rows[None], analysed * gain_block, 0.0).astype(jnp.bfloat16)
        return running + jnp.einsum(
            "mlr,cml->cmr", table, scaled, preferred_element_type=jnp.float32
        )

    first_block = 0
    initial = jnp.zeros(owned.shape, jnp.float32)
    summed = lax.fori_loop(first_block, degrees // block_rows, one_block, initial)
    return summed * math.sqrt(total_cycles / degrees)


ROWS = 16


def legendre_body(m_ref, coef_ref, gain_ref, tab_ref, out_ref, *, scale):
    k = pl.program_id(0)
    tab = tab_ref[0]
    coef = coef_ref[0]
    analysed = lax.dot_general(
        coef, tab, (((1,), (1,)), ((), ())), preferred_element_type=jnp.float32
    )
    degree = lax.broadcasted_iota(jnp.int32, analysed.shape, 1)
    keep = degree >= m_ref[k]
    scaled = jnp.where(keep, analysed * gain_ref[...], 0.0).astype(jnp.bfloat16)
    synth = jnp.dot(scaled, tab, preferred_element_type=jnp.float32)
    out_ref[0] = synth * scale


def legendre_pallas(owned, legendre, prior_gain, m_own):
    count_here, degrees, total_cycles = legendre.shape
    coef = jnp.zeros((count_here, ROWS, total_cycles), jnp.bfloat16)
    coef = coef.at[:, :2, :].set(owned.transpose(1, 0, 2))
    gain = prior_gain.reshape(1, degrees)
    grid_spec = pltpu.PrefetchScalarGridSpec(
        num_scalar_prefetch=1,
        grid=(count_here,),
        in_specs=[
            pl.BlockSpec((1, ROWS, total_cycles), lambda k, m: (k, 0, 0)),
            pl.BlockSpec((1, degrees), lambda k, m: (0, 0)),
            pl.BlockSpec((1, degrees, total_cycles), lambda k, m: (k, 0, 0)),
        ],
        out_specs=pl.BlockSpec((1, ROWS, total_cycles), lambda k, m: (k, 0, 0)),
    )
    out = pl.pallas_call(
        functools.partial(legendre_body, scale=math.sqrt(total_cycles / degrees)),
        grid_spec=grid_spec,
        out_shape=jax.ShapeDtypeStruct((count_here, ROWS, total_cycles), jnp.float32),
    )(m_own, coef, gain, legendre)
    return out[:, :2, :].transpose(1, 0, 2)


CAP = 8


STRIDE = 4


def order_pick(m_values):
    count = m_values.shape[0]
    offset = m_values - STRIDE * jnp.arange(count, dtype=jnp.int32)
    return offset[:, None] == jnp.arange(STRIDE, dtype=jnp.int32)[None, :]


def spectrum_out(field, m_values, cycle_offset):
    cycles_here, length = field.shape
    count = m_values.shape[0]
    spec_re, spec_im = forward_cycles(field)
    outer_len = length // 128
    spec_re = spec_re.reshape(cycles_here, outer_len, 128).transpose(0, 2, 1)
    spec_im = spec_im.reshape(cycles_here, outer_len, 128).transpose(0, 2, 1)
    pick = order_pick(m_values)[None]
    band = count * STRIDE
    spec_re = spec_re.reshape(cycles_here, length)[:, :band].reshape(cycles_here, count, STRIDE)
    spec_im = spec_im.reshape(cycles_here, length)[:, :band].reshape(cycles_here, count, STRIDE)
    pick_re = jnp.sum(jnp.where(pick, spec_re, 0.0), axis=2)
    pick_im = jnp.sum(jnp.where(pick, spec_im, 0.0), axis=2)
    phases = (m_values[None, :] * cycle_offset[:, None] % length).astype(jnp.float32) * (
        2.0 * math.pi / length
    )
    cos_phase = jnp.cos(phases)
    sin_phase = jnp.sin(phases)
    norm_factor = 1.0 / math.sqrt(length)
    coef_re = (pick_re * cos_phase + pick_im * sin_phase) * norm_factor
    coef_im = (pick_im * cos_phase - pick_re * sin_phase) * norm_factor
    return coef_re, coef_im, cos_phase, sin_phase


def spectrum_back(back_re, back_im, cos_phase, sin_phase, m_values, length):
    cycles_here = back_re.shape[0]
    count = m_values.shape[0]
    outer_len = length // 128
    mode_weight = jnp.where(m_values == 0, 1.0, 2.0).astype(jnp.float32)[None, :]
    harm_re = mode_weight * (back_re * cos_phase - back_im * sin_phase)
    harm_im = mode_weight * (back_re * sin_phase + back_im * cos_phase)
    pick = order_pick(m_values)[None]
    rest = ((0, 0), (0, length - count * STRIDE))
    full_re = jnp.where(pick, harm_re[:, :, None], 0.0).reshape(cycles_here, count * STRIDE)
    full_im = jnp.where(pick, harm_im[:, :, None], 0.0).reshape(cycles_here, count * STRIDE)
    full_re = jnp.pad(full_re, rest).reshape(cycles_here, 128, outer_len)
    full_im = jnp.pad(full_im, rest).reshape(cycles_here, 128, outer_len)
    full_re = full_re.transpose(0, 2, 1).reshape(cycles_here, length)
    full_im = full_im.transpose(0, 2, 1).reshape(cycles_here, length)
    return inverse_cycles(full_re, full_im) / math.sqrt(2.0 * count)


def on_device(
    samples,
    pointing,
    pix_block,
    det_weight,
    start_map,
    legendre,
    prior_gain,
    m_values,
    cycle_offset,
):
    axes = ("det", "tm")
    cycles_here, length = start_map.shape
    per_cycle = length // 128
    owners = lax.axis_size(axes)
    total_cycles = cycles_here * owners
    blocks_here = cycles_here * per_cycle
    count_here = legendre.shape[0]
    owner_index = lax.axis_index(axes)
    m_own = lax.dynamic_slice_in_dim(m_values, owner_index * count_here, count_here)
    slots = owners * CAP

    flat_pix = pix_block.reshape(-1)
    nloc = flat_pix.shape[0]
    owner_of = flat_pix // blocks_here
    within = flat_pix % blocks_here
    order = jnp.arange(nloc, dtype=jnp.int32)
    same = (owner_of[:, None] == owner_of[None, :]) & (order[None, :] < order[:, None])
    rank = jnp.sum(same.astype(jnp.int32), axis=1)
    slot = owner_of * CAP + rank
    weight_of = jnp.broadcast_to(det_weight[:, None], pix_block.shape).reshape(-1)
    index_send = jnp.zeros((slots,), jnp.float32).at[slot].set(within.astype(jnp.float32))
    weight_send = jnp.zeros((slots,), jnp.float32).at[slot].set(weight_of)
    info = jnp.stack([index_send, weight_send], axis=1).reshape(owners, CAP * 2)
    info_recv = lax.all_to_all(info, axes, 0, 0, tiled=True).reshape(slots, 2)
    want = info_recv[:, 0].astype(jnp.int32)
    want_hot = (want[None, :] == jnp.arange(blocks_here, dtype=jnp.int32)[:, None]).astype(jnp.float32)
    hit_weight = jnp.sum(want_hot * info_recv[None, :, 1], axis=1).reshape(cycles_here, per_cycle)
    divisor = jnp.repeat(1.0 + 0.25 * hit_weight, 128, axis=1)

    current = start_map
    for iteration in range(ITERS):
        map_half = current.astype(jnp.bfloat16).reshape(blocks_here, 128)
        rows_out = map_half[want].reshape(owners, CAP * 128)
        coef_re, coef_im, cos_phase, sin_phase = spectrum_out(current, m_values, cycle_offset)
        outward = jnp.stack([coef_re.T, coef_im.T]).astype(jnp.bfloat16)
        outward = outward.reshape(2, owners, count_here, cycles_here).transpose(1, 0, 2, 3)
        send_a = jnp.concatenate(
            [rows_out, outward.reshape(owners, 2 * count_here * cycles_here)], axis=1
        )
        recv_a = lax.all_to_all(send_a, axes, 0, 0, tiled=True)
        rows_in = recv_a[:, : CAP * 128].reshape(slots, 128)
        owned = recv_a[:, CAP * 128 :].reshape(owners, 2, count_here, cycles_here)
        owned = owned.transpose(1, 2, 0, 3).reshape(2, count_here, total_cycles)

        picked = rows_in[slot].reshape(pix_block.shape + (128,))
        predicted = jnp.einsum(
            "dtsp,dtp->dts", pointing, picked, preferred_element_type=jnp.float32
        )
        weighted_resid = (det_weight[:, None, None] * (samples - predicted)).astype(jnp.bfloat16)
        binned_terms = jnp.einsum(
            "dtsp,dts->dtp", pointing, weighted_resid, preferred_element_type=jnp.float32
        )
        binned_send = jnp.zeros((slots, 128), jnp.float32).at[slot].set(binned_terms.reshape(-1, 128))

        synth = legendre_pallas(owned, legendre, prior_gain, m_own)
        synth_send = synth.reshape(2, count_here, owners, cycles_here).transpose(2, 0, 1, 3)
        send_b = jnp.concatenate(
            [binned_send.reshape(owners, CAP * 128), synth_send.reshape(owners, -1)], axis=1
        )
        recv_b = lax.all_to_all(send_b, axes, 0, 0, tiled=True)
        binned_in = recv_b[:, : CAP * 128].reshape(slots, 128)
        binned = jnp.dot(want_hot, binned_in, precision=highest).reshape(cycles_here, length)
        returned = recv_b[:, CAP * 128 :].reshape(owners, 2, count_here, cycles_here)
        returned = returned.transpose(1, 0, 2, 3).reshape(2, owners * count_here, cycles_here)
        filtered = spectrum_back(
            returned[0].T, returned[1].T, cos_phase, sin_phase, m_values, length
        )
        current = current + (binned - filtered) / divisor
    return current


def solution(mesh):
    placed = (
        P("det", "tm", None),
        P("det", "tm", None, None),
        P("det", "tm"),
        P("det"),
        P(("det", "tm"), None),
        P(("det", "tm"), None, None),
        P(),
        P(),
        P(("det", "tm")),
    )
    return jax.shard_map(
        on_device, mesh=mesh, in_specs=placed, out_specs=P(("det", "tm"), None), check_vma=False
    )
```

```python
import math

import functools

import jax
import jax.numpy as jnp
from jax import lax
from jax.experimental import pallas as pl
from jax.experimental.pallas import tpu as pltpu
from jax.sharding import PartitionSpec as P

ITERS = 2


highest = lax.Precision.HIGHEST


def phase_pair(first_len, second_len, length, sign):
    first = jnp.arange(first_len, dtype=jnp.int32)[:, None]
    second = jnp.arange(second_len, dtype=jnp.int32)[None, :]
    phases = (first * second % length).astype(jnp.float32) * (sign * 2.0 * math.pi / length)
    return (jnp.cos(phases), jnp.sin(phases))


def forward_cycles(field):
    cycles, length = field.shape
    outer_len = length // 128
    shaped = field.reshape(cycles, outer_len, 128)
    cos_outer, sin_outer = phase_pair(outer_len, outer_len, outer_len, -1.0)
    part_re = jnp.einsum("mj,rjk->rmk", cos_outer, shaped, precision=highest)
    part_im = jnp.einsum("mj,rjk->rmk", sin_outer, shaped, precision=highest)
    cos_twist, sin_twist = phase_pair(outer_len, 128, length, -1.0)
    twist_re = part_re * cos_twist - part_im * sin_twist
    twist_im = part_re * sin_twist + part_im * cos_twist
    cos_inner, sin_inner = phase_pair(128, 128, 128, -1.0)
    spec_re = jnp.einsum("rmk,kn->rmn", twist_re, cos_inner, precision=highest) - jnp.einsum(
        "rmk,kn->rmn", twist_im, sin_inner, precision=highest
    )
    spec_im = jnp.einsum("rmk,kn->rmn", twist_re, sin_inner, precision=highest) + jnp.einsum(
        "rmk,kn->rmn", twist_im, cos_inner, precision=highest
    )
    return (spec_re.reshape(cycles, length), spec_im.reshape(cycles, length))


def inverse_cycles(spec_re, spec_im):
    cycles, length = spec_re.shape
    outer_len = length // 128
    shaped_re = spec_re.reshape(cycles, outer_len, 128)
    shaped_im = spec_im.reshape(cycles, outer_len, 128)
    cos_inner, sin_inner = phase_pair(128, 128, 128, 1.0)
    inner_re = jnp.einsum("rmn,nk->rmk", shaped_re, cos_inner, precision=highest) - jnp.einsum(
        "rmn,nk->rmk", shaped_im, sin_inner, precision=highest
    )
    inner_im = jnp.einsum("rmn,nk->rmk", shaped_re, sin_inner, precision=highest) + jnp.einsum(
        "rmn,nk->rmk", shaped_im, cos_inner, precision=highest
    )
    cos_twist, sin_twist = phase_pair(outer_len, 128, length, 1.0)
    twist_re = inner_re * cos_twist - inner_im * sin_twist
    twist_im = inner_re * sin_twist + inner_im * cos_twist
    cos_outer, sin_outer = phase_pair(outer_len, outer_len, outer_len, 1.0)
    field = jnp.einsum("jm,rmk->rjk", cos_outer, twist_re, precision=highest) - jnp.einsum(
        "jm,rmk->rjk", sin_outer, twist_im, precision=highest
    )
    return field.reshape(cycles, length)


def legendre_filter(owned, legendre, prior_gain, m_own):
    count_here, degrees, total_cycles = legendre.shape
    block_rows = min(512, degrees)

    def one_block(index, running):
        start = index * block_rows
        table = lax.dynamic_slice_in_dim(legendre, start, block_rows, 1)
        analysed = jnp.einsum("mlr,cmr->cml", table, owned, preferred_element_type=jnp.float32)
        degree = start + jnp.arange(block_rows, dtype=jnp.int32)
        keep_rows = degree[None, :] >= m_own[:, None]
        gain_block = lax.dynamic_slice_in_dim(prior_gain, start, block_rows)
        scaled = jnp.where(keep_rows[None], analysed * gain_block, 0.0).astype(jnp.bfloat16)
        return running + jnp.einsum(
            "mlr,cml->cmr", table, scaled, preferred_element_type=jnp.float32
        )

    first_block = 0
    initial = jnp.zeros(owned.shape, jnp.float32)
    summed = lax.fori_loop(first_block, degrees // block_rows, one_block, initial)
    return summed * math.sqrt(total_cycles / degrees)


ROWS = 16


def legendre_body(m_ref, coef_ref, gain_ref, tab_ref, out_ref, *, scale):
    k = pl.program_id(0)
    tab = tab_ref[0]
    coef = coef_ref[0]
    analysed = lax.dot_general(
        coef, tab, (((1,), (1,)), ((), ())), preferred_element_type=jnp.float32
    )
    degree = lax.broadcasted_iota(jnp.int32, analysed.shape, 1)
    keep = degree >= m_ref[k]
    scaled = jnp.where(keep, analysed * gain_ref[...], 0.0).astype(jnp.bfloat16)
    synth = jnp.dot(scaled, tab, preferred_element_type=jnp.float32)
    out_ref[0] = synth * scale


def legendre_pallas(owned, legendre, prior_gain, m_own):
    count_here, degrees, total_cycles = legendre.shape
    coef = jnp.zeros((count_here, ROWS, total_cycles), jnp.bfloat16)
    coef = coef.at[:, :2, :].set(owned.transpose(1, 0, 2))
    gain = prior_gain.reshape(1, degrees)
    grid_spec = pltpu.PrefetchScalarGridSpec(
        num_scalar_prefetch=1,
        grid=(count_here,),
        in_specs=[
            pl.BlockSpec((1, ROWS, total_cycles), lambda k, m: (k, 0, 0)),
            pl.BlockSpec((1, degrees), lambda k, m: (0, 0)),
            pl.BlockSpec((1, degrees, total_cycles), lambda k, m: (k, 0, 0)),
        ],
        out_specs=pl.BlockSpec((1, ROWS, total_cycles), lambda k, m: (k, 0, 0)),
    )
    out = pl.pallas_call(
        functools.partial(legendre_body, scale=math.sqrt(total_cycles / degrees)),
        grid_spec=grid_spec,
        out_shape=jax.ShapeDtypeStruct((count_here, ROWS, total_cycles), jnp.float32),
    )(m_own, coef, gain, legendre)
    return out[:, :2, :].transpose(1, 0, 2)


CAP = 8


STRIDE = 4


def order_pick(m_values):
    count = m_values.shape[0]
    offset = m_values - STRIDE * jnp.arange(count, dtype=jnp.int32)
    return offset[:, None] == jnp.arange(STRIDE, dtype=jnp.int32)[None, :]


def spectrum_out(field, m_values, cycle_offset):
    cycles_here, length = field.shape
    count = m_values.shape[0]
    spec_re, spec_im = forward_cycles(field)
    outer_len = length // 128
    spec_re = spec_re.reshape(cycles_here, outer_len, 128).transpose(0, 2, 1)
    spec_im = spec_im.reshape(cycles_here, outer_len, 128).transpose(0, 2, 1)
    pick = order_pick(m_values)[None]
    band = count * STRIDE
    spec_re = spec_re.reshape(cycles_here, length)[:, :band].reshape(cycles_here, count, STRIDE)
    spec_im = spec_im.reshape(cycles_here, length)[:, :band].reshape(cycles_here, count, STRIDE)
    pick_re = jnp.sum(jnp.where(pick, spec_re, 0.0), axis=2)
    pick_im = jnp.sum(jnp.where(pick, spec_im, 0.0), axis=2)
    phases = (m_values[None, :] * cycle_offset[:, None] % length).astype(jnp.float32) * (
        2.0 * math.pi / length
    )
    cos_phase = jnp.cos(phases)
    sin_phase = jnp.sin(phases)
    norm_factor = 1.0 / math.sqrt(length)
    coef_re = (pick_re * cos_phase + pick_im * sin_phase) * norm_factor
    coef_im = (pick_im * cos_phase - pick_re * sin_phase) * norm_factor
    return coef_re, coef_im, cos_phase, sin_phase


def spectrum_back(back_re, back_im, cos_phase, sin_phase, m_values, length):
    cycles_here = back_re.shape[0]
    count = m_values.shape[0]
    outer_len = length // 128
    mode_weight = jnp.where(m_values == 0, 1.0, 2.0).astype(jnp.float32)[None, :]
    harm_re = mode_weight * (back_re * cos_phase - back_im * sin_phase)
    harm_im = mode_weight * (back_re * sin_phase + back_im * cos_phase)
    pick = order_pick(m_values)[None]
    rest = ((0, 0), (0, length - count * STRIDE))
    full_re = jnp.where(pick, harm_re[:, :, None], 0.0).reshape(cycles_here, count * STRIDE)
    full_im = jnp.where(pick, harm_im[:, :, None], 0.0).reshape(cycles_here, count * STRIDE)
    full_re = jnp.pad(full_re, rest).reshape(cycles_here, 128, outer_len)
    full_im = jnp.pad(full_im, rest).reshape(cycles_here, 128, outer_len)
    full_re = full_re.transpose(0, 2, 1).reshape(cycles_here, length)
    full_im = full_im.transpose(0, 2, 1).reshape(cycles_here, length)
    return inverse_cycles(full_re, full_im) / math.sqrt(2.0 * count)


def on_device(
    samples,
    pointing,
    pix_block,
    det_weight,
    start_map,
    legendre,
    prior_gain,
    m_values,
    cycle_offset,
):
    axes = ("det", "tm")
    cycles_here, length = start_map.shape
    per_cycle = length // 128
    owners = lax.axis_size(axes)
    total_cycles = cycles_here * owners
    blocks_here = cycles_here * per_cycle
    count_here = legendre.shape[0]
    owner_index = lax.axis_index(axes)
    m_own = lax.dynamic_slice_in_dim(m_values, owner_index * count_here, count_here)
    slots = owners * CAP

    flat_pix = pix_block.reshape(-1)
    nloc = flat_pix.shape[0]
    owner_of = flat_pix // blocks_here
    within = flat_pix % blocks_here
    order = jnp.arange(nloc, dtype=jnp.int32)
    same = (owner_of[:, None] == owner_of[None, :]) & (order[None, :] < order[:, None])
    rank = jnp.sum(same.astype(jnp.int32), axis=1)
    slot = owner_of * CAP + rank
    weight_of = jnp.broadcast_to(det_weight[:, None], pix_block.shape).reshape(-1)
    info = jnp.stack([within.astype(jnp.float32), weight_of], axis=1)
    info = jnp.zeros((slots, 2), jnp.float32).at[slot].set(info).reshape(owners, CAP * 2)
    info_recv = lax.all_to_all(info, axes, 0, 0, tiled=True).reshape(slots, 2)
    want = info_recv[:, 0].astype(jnp.int32)
    want_hot = (want[None, :] == jnp.arange(blocks_here, dtype=jnp.int32)[:, None]).astype(jnp.float32)
    hit_weight = jnp.sum(want_hot * info_recv[None, :, 1], axis=1).reshape(cycles_here, per_cycle)
    divisor = jnp.repeat(1.0 + 0.25 * hit_weight, 128, axis=1)
    want_pick = want_hot.T.astype(jnp.bfloat16)

    current = start_map
    for iteration in range(ITERS):
        map_half = current.astype(jnp.bfloat16).reshape(blocks_here, 128)
        rows_out = jnp.dot(want_pick, map_half, preferred_element_type=jnp.float32)
        rows_out = rows_out.astype(jnp.bfloat16).reshape(owners, CAP * 128)
        coef_re, coef_im, cos_phase, sin_phase = spectrum_out(current, m_values, cycle_offset)
        outward = jnp.stack([coef_re.T, coef_im.T]).astype(jnp.bfloat16)
        outward = outward.reshape(2, owners, count_here, cycles_here).transpose(1, 0, 2, 3)
        send_a = jnp.concatenate(
            [rows_out, outward.reshape(owners, 2 * count_here * cycles_here)], axis=1
        )
        recv_a = lax.all_to_all(send_a, axes, 0, 0, tiled=True)
        rows_in = recv_a[:, : CAP * 128].reshape(slots, 128)
        owned = recv_a[:, CAP * 128 :].reshape(owners, 2, count_here, cycles_here)
        owned = owned.transpose(1, 2, 0, 3).reshape(2, count_here, total_cycles)

        picked = rows_in[slot].reshape(pix_block.shape + (128,))
        predicted = jnp.einsum(
            "dtsp,dtp->dts", pointing, picked, preferred_element_type=jnp.float32
        )
        weighted_resid = (det_weight[:, None, None] * (samples - predicted)).astype(jnp.bfloat16)
        binned_terms = jnp.einsum(
            "dtsp,dts->dtp", pointing, weighted_resid, preferred_element_type=jnp.float32
        )
        binned_send = jnp.zeros((slots, 128), jnp.float32).at[slot].set(binned_terms.reshape(-1, 128))

        synth = legendre_pallas(owned, legendre, prior_gain, m_own)
        synth_send = synth.reshape(2, count_here, owners, cycles_here).transpose(2, 0, 1, 3)
        send_b = jnp.concatenate(
            [binned_send.reshape(owners, CAP * 128), synth_send.reshape(owners, -1)], axis=1
        )
        recv_b = lax.all_to_all(send_b, axes, 0, 0, tiled=True)
        binned_in = recv_b[:, : CAP * 128].reshape(slots, 128)
        binned = jnp.dot(want_hot, binned_in, precision=highest).reshape(cycles_here, length)
        returned = recv_b[:, CAP * 128 :].reshape(owners, 2, count_here, cycles_here)
        returned = returned.transpose(1, 0, 2, 3).reshape(2, owners * count_here, cycles_here)
        filtered = spectrum_back(
            returned[0].T, returned[1].T, cos_phase, sin_phase, m_values, length
        )
        current = current + (binned - filtered) / divisor
    return current


def solution(mesh):
    placed = (
        P("det", "tm", None),
        P("det", "tm", None, None),
        P("det", "tm"),
        P("det"),
        P(("det", "tm"), None),
        P(("det", "tm"), None, None),
        P(),
        P(),
        P(("det", "tm")),
    )
    return jax.shard_map(
        on_device, mesh=mesh, in_specs=placed, out_specs=P(("det", "tm"), None), check_vma=False
    )
```

```python
import math

import functools

import jax
import jax.numpy as jnp
from jax import lax
from jax.experimental import pallas as pl
from jax.experimental.pallas import tpu as pltpu
from jax.sharding import PartitionSpec as P

ITERS = 2


highest = lax.Precision.HIGHEST


def phase_pair(first_len, second_len, length, sign):
    first = jnp.arange(first_len, dtype=jnp.int32)[:, None]
    second = jnp.arange(second_len, dtype=jnp.int32)[None, :]
    phases = (first * second % length).astype(jnp.float32) * (sign * 2.0 * math.pi / length)
    return (jnp.cos(phases), jnp.sin(phases))


def forward_cycles(field):
    cycles, length = field.shape
    outer_len = length // 128
    shaped = field.reshape(cycles, outer_len, 128)
    cos_outer, sin_outer = phase_pair(outer_len, outer_len, outer_len, -1.0)
    part_re = jnp.einsum("mj,rjk->rmk", cos_outer, shaped, precision=highest)
    part_im = jnp.einsum("mj,rjk->rmk", sin_outer, shaped, precision=highest)
    cos_twist, sin_twist = phase_pair(outer_len, 128, length, -1.0)
    twist_re = part_re * cos_twist - part_im * sin_twist
    twist_im = part_re * sin_twist + part_im * cos_twist
    cos_inner, sin_inner = phase_pair(128, 128, 128, -1.0)
    spec_re = jnp.einsum("rmk,kn->rmn", twist_re, cos_inner, precision=highest) - jnp.einsum(
        "rmk,kn->rmn", twist_im, sin_inner, precision=highest
    )
    spec_im = jnp.einsum("rmk,kn->rmn", twist_re, sin_inner, precision=highest) + jnp.einsum(
        "rmk,kn->rmn", twist_im, cos_inner, precision=highest
    )
    return (spec_re.reshape(cycles, length), spec_im.reshape(cycles, length))


def inverse_cycles(spec_re, spec_im):
    cycles, length = spec_re.shape
    outer_len = length // 128
    shaped_re = spec_re.reshape(cycles, outer_len, 128)
    shaped_im = spec_im.reshape(cycles, outer_len, 128)
    cos_inner, sin_inner = phase_pair(128, 128, 128, 1.0)
    inner_re = jnp.einsum("rmn,nk->rmk", shaped_re, cos_inner, precision=highest) - jnp.einsum(
        "rmn,nk->rmk", shaped_im, sin_inner, precision=highest
    )
    inner_im = jnp.einsum("rmn,nk->rmk", shaped_re, sin_inner, precision=highest) + jnp.einsum(
        "rmn,nk->rmk", shaped_im, cos_inner, precision=highest
    )
    cos_twist, sin_twist = phase_pair(outer_len, 128, length, 1.0)
    twist_re = inner_re * cos_twist - inner_im * sin_twist
    twist_im = inner_re * sin_twist + inner_im * cos_twist
    cos_outer, sin_outer = phase_pair(outer_len, outer_len, outer_len, 1.0)
    field = jnp.einsum("jm,rmk->rjk", cos_outer, twist_re, precision=highest) - jnp.einsum(
        "jm,rmk->rjk", sin_outer, twist_im, precision=highest
    )
    return field.reshape(cycles, length)


def legendre_filter(owned, legendre, prior_gain, m_own):
    count_here, degrees, total_cycles = legendre.shape
    block_rows = min(512, degrees)

    def one_block(index, running):
        start = index * block_rows
        table = lax.dynamic_slice_in_dim(legendre, start, block_rows, 1)
        analysed = jnp.einsum("mlr,cmr->cml", table, owned, preferred_element_type=jnp.float32)
        degree = start + jnp.arange(block_rows, dtype=jnp.int32)
        keep_rows = degree[None, :] >= m_own[:, None]
        gain_block = lax.dynamic_slice_in_dim(prior_gain, start, block_rows)
        scaled = jnp.where(keep_rows[None], analysed * gain_block, 0.0).astype(jnp.bfloat16)
        return running + jnp.einsum(
            "mlr,cml->cmr", table, scaled, preferred_element_type=jnp.float32
        )

    first_block = 0
    initial = jnp.zeros(owned.shape, jnp.float32)
    summed = lax.fori_loop(first_block, degrees // block_rows, one_block, initial)
    return summed * math.sqrt(total_cycles / degrees)


ROWS = 16


def legendre_body(m_ref, coef_ref, gain_ref, tab_ref, out_ref, *, scale):
    k = pl.program_id(0)
    tab = tab_ref[0]
    coef = coef_ref[0]
    analysed = lax.dot_general(
        coef, tab, (((1,), (1,)), ((), ())), preferred_element_type=jnp.float32
    )
    degree = lax.broadcasted_iota(jnp.int32, analysed.shape, 1)
    keep = degree >= m_ref[k]
    scaled = jnp.where(keep, analysed * gain_ref[...], 0.0).astype(jnp.bfloat16)
    synth = jnp.dot(scaled, tab, preferred_element_type=jnp.float32)
    out_ref[0] = synth * scale


def legendre_pallas(owned, legendre, prior_gain, m_own):
    count_here, degrees, total_cycles = legendre.shape
    coef = jnp.zeros((count_here, ROWS, total_cycles), jnp.bfloat16)
    coef = coef.at[:, :2, :].set(owned.transpose(1, 0, 2))
    gain = prior_gain.reshape(1, degrees)
    grid_spec = pltpu.PrefetchScalarGridSpec(
        num_scalar_prefetch=1,
        grid=(count_here,),
        in_specs=[
            pl.BlockSpec((1, ROWS, total_cycles), lambda k, m: (k, 0, 0)),
            pl.BlockSpec((1, degrees), lambda k, m: (0, 0)),
            pl.BlockSpec((1, degrees, total_cycles), lambda k, m: (k, 0, 0)),
        ],
        out_specs=pl.BlockSpec((1, ROWS, total_cycles), lambda k, m: (k, 0, 0)),
    )
    out = pl.pallas_call(
        functools.partial(legendre_body, scale=math.sqrt(total_cycles / degrees)),
        grid_spec=grid_spec,
        out_shape=jax.ShapeDtypeStruct((count_here, ROWS, total_cycles), jnp.float32),
    )(m_own, coef, gain, legendre)
    return out[:, :2, :].transpose(1, 0, 2)


CAP = 8


STRIDE = 4


def order_pick(m_values):
    count = m_values.shape[0]
    offset = m_values - STRIDE * jnp.arange(count, dtype=jnp.int32)
    return offset[:, None] == jnp.arange(STRIDE, dtype=jnp.int32)[None, :]


def spectrum_out(field, m_values, cycle_offset):
    cycles_here, length = field.shape
    count = m_values.shape[0]
    spec_re, spec_im = forward_cycles(field)
    outer_len = length // 128
    spec_re = spec_re.reshape(cycles_here, outer_len, 128).transpose(0, 2, 1)
    spec_im = spec_im.reshape(cycles_here, outer_len, 128).transpose(0, 2, 1)
    pick = order_pick(m_values)[None]
    band = count * STRIDE
    spec_re = spec_re.reshape(cycles_here, length)[:, :band].reshape(cycles_here, count, STRIDE)
    spec_im = spec_im.reshape(cycles_here, length)[:, :band].reshape(cycles_here, count, STRIDE)
    pick_re = jnp.sum(jnp.where(pick, spec_re, 0.0), axis=2)
    pick_im = jnp.sum(jnp.where(pick, spec_im, 0.0), axis=2)
    phases = (m_values[None, :] * cycle_offset[:, None] % length).astype(jnp.float32) * (
        2.0 * math.pi / length
    )
    cos_phase = jnp.cos(phases)
    sin_phase = jnp.sin(phases)
    norm_factor = 1.0 / math.sqrt(length)
    coef_re = (pick_re * cos_phase + pick_im * sin_phase) * norm_factor
    coef_im = (pick_im * cos_phase - pick_re * sin_phase) * norm_factor
    return coef_re, coef_im, cos_phase, sin_phase


def spectrum_back(back_re, back_im, cos_phase, sin_phase, m_values, length):
    cycles_here = back_re.shape[0]
    count = m_values.shape[0]
    outer_len = length // 128
    mode_weight = jnp.where(m_values == 0, 1.0, 2.0).astype(jnp.float32)[None, :]
    harm_re = mode_weight * (back_re * cos_phase - back_im * sin_phase)
    harm_im = mode_weight * (back_re * sin_phase + back_im * cos_phase)
    pick = order_pick(m_values)[None]
    rest = ((0, 0), (0, length - count * STRIDE))
    full_re = jnp.where(pick, harm_re[:, :, None], 0.0).reshape(cycles_here, count * STRIDE)
    full_im = jnp.where(pick, harm_im[:, :, None], 0.0).reshape(cycles_here, count * STRIDE)
    full_re = jnp.pad(full_re, rest).reshape(cycles_here, 128, outer_len)
    full_im = jnp.pad(full_im, rest).reshape(cycles_here, 128, outer_len)
    full_re = full_re.transpose(0, 2, 1).reshape(cycles_here, length)
    full_im = full_im.transpose(0, 2, 1).reshape(cycles_here, length)
    return inverse_cycles(full_re, full_im) / math.sqrt(2.0 * count)


def on_device(
    samples,
    pointing,
    pix_block,
    det_weight,
    start_map,
    legendre,
    prior_gain,
    m_values,
    cycle_offset,
):
    axes = ("det", "tm")
    cycles_here, length = start_map.shape
    per_cycle = length // 128
    owners = lax.axis_size(axes)
    total_cycles = cycles_here * owners
    blocks_here = cycles_here * per_cycle
    count_here = legendre.shape[0]
    owner_index = lax.axis_index(axes)
    m_own = lax.dynamic_slice_in_dim(m_values, owner_index * count_here, count_here)
    slots = owners * CAP

    flat_pix = pix_block.reshape(-1)
    nloc = flat_pix.shape[0]
    owner_of = flat_pix // blocks_here
    within = flat_pix % blocks_here
    order = jnp.arange(nloc, dtype=jnp.int32)
    same = (owner_of[:, None] == owner_of[None, :]) & (order[None, :] < order[:, None])
    rank = jnp.sum(same.astype(jnp.int32), axis=1)
    slot = owner_of * CAP + rank
    weight_of = jnp.broadcast_to(det_weight[:, None], pix_block.shape).reshape(-1)
    info = jnp.stack([within.astype(jnp.float32), weight_of], axis=1)
    info = jnp.zeros((slots, 2), jnp.float32).at[slot].set(info).reshape(owners, CAP * 2)
    coef_width = 2 * count_here * cycles_here

    def coef_out(field):
        coef_re, coef_im, cos_phase, sin_phase = spectrum_out(field, m_values, cycle_offset)
        outward = jnp.stack([coef_re.T, coef_im.T]).astype(jnp.bfloat16)
        outward = outward.reshape(2, owners, count_here, cycles_here).transpose(1, 0, 2, 3)
        return outward.reshape(owners, coef_width), cos_phase, sin_phase

    def coef_in(part):
        owned = part.reshape(owners, 2, count_here, cycles_here).astype(jnp.bfloat16)
        return owned.transpose(1, 2, 0, 3).reshape(2, count_here, total_cycles)

    first_out, cos_phase, sin_phase = coef_out(start_map)
    info = jnp.concatenate([info, first_out.astype(jnp.float32)], axis=1)
    info_recv = lax.all_to_all(info, axes, 0, 0, tiled=True)
    first_owned = coef_in(info_recv[:, CAP * 2 :])
    info_recv = info_recv[:, : CAP * 2].reshape(slots, 2)
    want = info_recv[:, 0].astype(jnp.int32)
    want_hot = (want[None, :] == jnp.arange(blocks_here, dtype=jnp.int32)[:, None]).astype(jnp.float32)
    hit_weight = jnp.sum(want_hot * info_recv[None, :, 1], axis=1).reshape(cycles_here, per_cycle)
    divisor = jnp.repeat(1.0 + 0.25 * hit_weight, 128, axis=1)
    want_pick = want_hot.T.astype(jnp.bfloat16)

    current = start_map
    for iteration in range(ITERS):
        map_half = current.astype(jnp.bfloat16).reshape(blocks_here, 128)
        rows_out = jnp.dot(want_pick, map_half, preferred_element_type=jnp.float32)
        rows_out = rows_out.astype(jnp.bfloat16).reshape(owners, CAP * 128)
        if iteration == 0:
            rows_in = lax.all_to_all(rows_out, axes, 0, 0, tiled=True).reshape(slots, 128)
            owned = first_owned
        else:
            outward, cos_phase, sin_phase = coef_out(current)
            send_a = jnp.concatenate([rows_out, outward], axis=1)
            recv_a = lax.all_to_all(send_a, axes, 0, 0, tiled=True)
            rows_in = recv_a[:, : CAP * 128].reshape(slots, 128)
            owned = coef_in(recv_a[:, CAP * 128 :])

        picked = rows_in[slot].reshape(pix_block.shape + (128,))
        predicted = jnp.einsum(
            "dtsp,dtp->dts", pointing, picked, preferred_element_type=jnp.float32
        )
        weighted_resid = (det_weight[:, None, None] * (samples - predicted)).astype(jnp.bfloat16)
        binned_terms = jnp.einsum(
            "dtsp,dts->dtp", pointing, weighted_resid, preferred_element_type=jnp.float32
        )
        binned_send = jnp.zeros((slots, 128), jnp.float32).at[slot].set(binned_terms.reshape(-1, 128))

        synth = legendre_pallas(owned, legendre, prior_gain, m_own)
        synth_send = synth.reshape(2, count_here, owners, cycles_here).transpose(2, 0, 1, 3)
        send_b = jnp.concatenate(
            [binned_send.reshape(owners, CAP * 128), synth_send.reshape(owners, -1)], axis=1
        )
        recv_b = lax.all_to_all(send_b, axes, 0, 0, tiled=True)
        binned_in = recv_b[:, : CAP * 128].reshape(slots, 128)
        binned = jnp.dot(want_hot, binned_in, precision=highest).reshape(cycles_here, length)
        returned = recv_b[:, CAP * 128 :].reshape(owners, 2, count_here, cycles_here)
        returned = returned.transpose(1, 0, 2, 3).reshape(2, owners * count_here, cycles_here)
        filtered = spectrum_back(
            returned[0].T, returned[1].T, cos_phase, sin_phase, m_values, length
        )
        current = current + (binned - filtered) / divisor
    return current


def solution(mesh):
    placed = (
        P("det", "tm", None),
        P("det", "tm", None, None),
        P("det", "tm"),
        P("det"),
        P(("det", "tm"), None),
        P(("det", "tm"), None, None),
        P(),
        P(),
        P(("det", "tm")),
    )
    return jax.shard_map(
        on_device, mesh=mesh, in_specs=placed, out_specs=P(("det", "tm"), None), check_vma=False
    )
```

```python
import math

import functools

import jax
import jax.numpy as jnp
from jax import lax
from jax.experimental import pallas as pl
from jax.experimental.pallas import tpu as pltpu
from jax.sharding import PartitionSpec as P

ITERS = 2


highest = lax.Precision.HIGHEST


def phase_pair(first_len, second_len, length, sign):
    first = jnp.arange(first_len, dtype=jnp.int32)[:, None]
    second = jnp.arange(second_len, dtype=jnp.int32)[None, :]
    phases = (first * second % length).astype(jnp.float32) * (sign * 2.0 * math.pi / length)
    return (jnp.cos(phases), jnp.sin(phases))


def forward_cycles(field):
    cycles, length = field.shape
    outer_len = length // 128
    shaped = field.reshape(cycles, outer_len, 128)
    cos_outer, sin_outer = phase_pair(outer_len, outer_len, outer_len, -1.0)
    part_re = jnp.einsum("mj,rjk->rmk", cos_outer, shaped, precision=highest)
    part_im = jnp.einsum("mj,rjk->rmk", sin_outer, shaped, precision=highest)
    cos_twist, sin_twist = phase_pair(outer_len, 128, length, -1.0)
    twist_re = part_re * cos_twist - part_im * sin_twist
    twist_im = part_re * sin_twist + part_im * cos_twist
    cos_inner, sin_inner = phase_pair(128, 128, 128, -1.0)
    spec_re = jnp.einsum("rmk,kn->rmn", twist_re, cos_inner, precision=highest) - jnp.einsum(
        "rmk,kn->rmn", twist_im, sin_inner, precision=highest
    )
    spec_im = jnp.einsum("rmk,kn->rmn", twist_re, sin_inner, precision=highest) + jnp.einsum(
        "rmk,kn->rmn", twist_im, cos_inner, precision=highest
    )
    return (spec_re.reshape(cycles, length), spec_im.reshape(cycles, length))


def inverse_cycles(spec_re, spec_im):
    cycles, length = spec_re.shape
    outer_len = length // 128
    shaped_re = spec_re.reshape(cycles, outer_len, 128)
    shaped_im = spec_im.reshape(cycles, outer_len, 128)
    cos_inner, sin_inner = phase_pair(128, 128, 128, 1.0)
    inner_re = jnp.einsum("rmn,nk->rmk", shaped_re, cos_inner, precision=highest) - jnp.einsum(
        "rmn,nk->rmk", shaped_im, sin_inner, precision=highest
    )
    inner_im = jnp.einsum("rmn,nk->rmk", shaped_re, sin_inner, precision=highest) + jnp.einsum(
        "rmn,nk->rmk", shaped_im, cos_inner, precision=highest
    )
    cos_twist, sin_twist = phase_pair(outer_len, 128, length, 1.0)
    twist_re = inner_re * cos_twist - inner_im * sin_twist
    twist_im = inner_re * sin_twist + inner_im * cos_twist
    cos_outer, sin_outer = phase_pair(outer_len, outer_len, outer_len, 1.0)
    field = jnp.einsum("jm,rmk->rjk", cos_outer, twist_re, precision=highest) - jnp.einsum(
        "jm,rmk->rjk", sin_outer, twist_im, precision=highest
    )
    return field.reshape(cycles, length)


def legendre_filter(owned, legendre, prior_gain, m_own):
    count_here, degrees, total_cycles = legendre.shape
    block_rows = min(512, degrees)

    def one_block(index, running):
        start = index * block_rows
        table = lax.dynamic_slice_in_dim(legendre, start, block_rows, 1)
        analysed = jnp.einsum("mlr,cmr->cml", table, owned, preferred_element_type=jnp.float32)
        degree = start + jnp.arange(block_rows, dtype=jnp.int32)
        keep_rows = degree[None, :] >= m_own[:, None]
        gain_block = lax.dynamic_slice_in_dim(prior_gain, start, block_rows)
        scaled = jnp.where(keep_rows[None], analysed * gain_block, 0.0).astype(jnp.bfloat16)
        return running + jnp.einsum(
            "mlr,cml->cmr", table, scaled, preferred_element_type=jnp.float32
        )

    first_block = 0
    initial = jnp.zeros(owned.shape, jnp.float32)
    summed = lax.fori_loop(first_block, degrees // block_rows, one_block, initial)
    return summed * math.sqrt(total_cycles / degrees)


ROWS = 16


def legendre_body(m_ref, coef_ref, gain_ref, tab_ref, out_ref, *, scale):
    k = pl.program_id(0)
    tab = tab_ref[0]
    coef = coef_ref[0]
    analysed = lax.dot_general(
        coef, tab, (((1,), (1,)), ((), ())), preferred_element_type=jnp.float32
    )
    degree = lax.broadcasted_iota(jnp.int32, analysed.shape, 1)
    keep = degree >= m_ref[k]
    scaled = jnp.where(keep, analysed * gain_ref[...], 0.0).astype(jnp.bfloat16)
    synth = jnp.dot(scaled, tab, preferred_element_type=jnp.float32)
    out_ref[0] = synth * scale


def legendre_pallas(owned, legendre, prior_gain, m_own):
    count_here, degrees, total_cycles = legendre.shape
    coef = jnp.zeros((count_here, ROWS, total_cycles), jnp.bfloat16)
    coef = coef.at[:, :2, :].set(owned.transpose(1, 0, 2))
    gain = prior_gain.reshape(1, degrees)
    grid_spec = pltpu.PrefetchScalarGridSpec(
        num_scalar_prefetch=1,
        grid=(count_here,),
        in_specs=[
            pl.BlockSpec((1, ROWS, total_cycles), lambda k, m: (k, 0, 0)),
            pl.BlockSpec((1, degrees), lambda k, m: (0, 0)),
            pl.BlockSpec((1, degrees, total_cycles), lambda k, m: (k, 0, 0)),
        ],
        out_specs=pl.BlockSpec((1, ROWS, total_cycles), lambda k, m: (k, 0, 0)),
    )
    out = pl.pallas_call(
        functools.partial(legendre_body, scale=math.sqrt(total_cycles / degrees)),
        grid_spec=grid_spec,
        out_shape=jax.ShapeDtypeStruct((count_here, ROWS, total_cycles), jnp.float32),
    )(m_own, coef, gain, legendre)
    return out[:, :2, :].transpose(1, 0, 2)


def pointing_body(w_ref, p_ref, x_ref, s_ref, out_ref, *, tblk, nsamp):
    d = pl.program_id(0)
    point = p_ref[0].reshape(tblk * nsamp, p_ref.shape[3])
    picked = x_ref[0]
    every = lax.dot_general(
        picked, point, (((1,), (1,)), ((), ())), preferred_element_type=jnp.float32
    )
    row = lax.broadcasted_iota(jnp.int32, every.shape, 0)
    col = lax.broadcasted_iota(jnp.int32, every.shape, 1)
    mine = row == col // nsamp
    predicted = jnp.sum(jnp.where(mine, every, 0.0), axis=0, keepdims=True)
    resid = (w_ref[d] * (s_ref[0] - predicted)).astype(jnp.bfloat16)
    spread = jnp.where(mine, jnp.broadcast_to(resid, every.shape), jnp.zeros_like(resid))
    out_ref[0] = jnp.dot(spread, point, preferred_element_type=jnp.float32)


def pointing_pallas(pointing, picked, samples, det_weight):
    dets, times, nsamp, npix = pointing.shape
    tblk = times
    samples_row = samples.reshape(dets, 1, times * nsamp)
    grid_spec = pltpu.PrefetchScalarGridSpec(
        num_scalar_prefetch=1,
        grid=(dets, times // tblk),
        in_specs=[
            pl.BlockSpec((1, tblk, nsamp, npix), lambda d, t, w: (d, t, 0, 0)),
            pl.BlockSpec((1, tblk, npix), lambda d, t, w: (d, t, 0)),
            pl.BlockSpec((1, 1, tblk * nsamp), lambda d, t, w: (d, 0, t)),
        ],
        out_specs=pl.BlockSpec((1, tblk, npix), lambda d, t, w: (d, t, 0)),
    )
    return pl.pallas_call(
        functools.partial(pointing_body, tblk=tblk, nsamp=nsamp),
        grid_spec=grid_spec,
        out_shape=jax.ShapeDtypeStruct((dets, times, npix), jnp.float32),
    )(det_weight, pointing, picked, samples_row)


CAP = 8


STRIDE = 4


def order_pick(m_values):
    count = m_values.shape[0]
    offset = m_values - STRIDE * jnp.arange(count, dtype=jnp.int32)
    return offset[:, None] == jnp.arange(STRIDE, dtype=jnp.int32)[None, :]


def spectrum_out(field, m_values, cycle_offset):
    cycles_here, length = field.shape
    count = m_values.shape[0]
    spec_re, spec_im = forward_cycles(field)
    outer_len = length // 128
    spec_re = spec_re.reshape(cycles_here, outer_len, 128).transpose(0, 2, 1)
    spec_im = spec_im.reshape(cycles_here, outer_len, 128).transpose(0, 2, 1)
    pick = order_pick(m_values)[None]
    band = count * STRIDE
    spec_re = spec_re.reshape(cycles_here, length)[:, :band].reshape(cycles_here, count, STRIDE)
    spec_im = spec_im.reshape(cycles_here, length)[:, :band].reshape(cycles_here, count, STRIDE)
    pick_re = jnp.sum(jnp.where(pick, spec_re, 0.0), axis=2)
    pick_im = jnp.sum(jnp.where(pick, spec_im, 0.0), axis=2)
    phases = (m_values[None, :] * cycle_offset[:, None] % length).astype(jnp.float32) * (
        2.0 * math.pi / length
    )
    cos_phase = jnp.cos(phases)
    sin_phase = jnp.sin(phases)
    norm_factor = 1.0 / math.sqrt(length)
    coef_re = (pick_re * cos_phase + pick_im * sin_phase) * norm_factor
    coef_im = (pick_im * cos_phase - pick_re * sin_phase) * norm_factor
    return coef_re, coef_im, cos_phase, sin_phase


def spectrum_back(back_re, back_im, cos_phase, sin_phase, m_values, length):
    cycles_here = back_re.shape[0]
    count = m_values.shape[0]
    outer_len = length // 128
    mode_weight = jnp.where(m_values == 0, 1.0, 2.0).astype(jnp.float32)[None, :]
    harm_re = mode_weight * (back_re * cos_phase - back_im * sin_phase)
    harm_im = mode_weight * (back_re * sin_phase + back_im * cos_phase)
    pick = order_pick(m_values)[None]
    rest = ((0, 0), (0, length - count * STRIDE))
    full_re = jnp.where(pick, harm_re[:, :, None], 0.0).reshape(cycles_here, count * STRIDE)
    full_im = jnp.where(pick, harm_im[:, :, None], 0.0).reshape(cycles_here, count * STRIDE)
    full_re = jnp.pad(full_re, rest).reshape(cycles_here, 128, outer_len)
    full_im = jnp.pad(full_im, rest).reshape(cycles_here, 128, outer_len)
    full_re = full_re.transpose(0, 2, 1).reshape(cycles_here, length)
    full_im = full_im.transpose(0, 2, 1).reshape(cycles_here, length)
    return inverse_cycles(full_re, full_im) / math.sqrt(2.0 * count)


def on_device(
    samples,
    pointing,
    pix_block,
    det_weight,
    start_map,
    legendre,
    prior_gain,
    m_values,
    cycle_offset,
):
    axes = ("det", "tm")
    cycles_here, length = start_map.shape
    per_cycle = length // 128
    owners = lax.axis_size(axes)
    total_cycles = cycles_here * owners
    blocks_here = cycles_here * per_cycle
    count_here = legendre.shape[0]
    owner_index = lax.axis_index(axes)
    m_own = lax.dynamic_slice_in_dim(m_values, owner_index * count_here, count_here)
    slots = owners * CAP

    flat_pix = pix_block.reshape(-1)
    nloc = flat_pix.shape[0]
    owner_of = flat_pix // blocks_here
    within = flat_pix % blocks_here
    order = jnp.arange(nloc, dtype=jnp.int32)
    same = (owner_of[:, None] == owner_of[None, :]) & (order[None, :] < order[:, None])
    rank = jnp.sum(same.astype(jnp.int32), axis=1)
    slot = owner_of * CAP + rank
    weight_of = jnp.broadcast_to(det_weight[:, None], pix_block.shape).reshape(-1)
    info = jnp.stack([within.astype(jnp.float32), weight_of], axis=1)
    info = jnp.zeros((slots, 2), jnp.float32).at[slot].set(info).reshape(owners, CAP * 2)
    coef_width = 2 * count_here * cycles_here

    def coef_out(field):
        coef_re, coef_im, cos_phase, sin_phase = spectrum_out(field, m_values, cycle_offset)
        outward = jnp.stack([coef_re.T, coef_im.T]).astype(jnp.bfloat16)
        outward = outward.reshape(2, owners, count_here, cycles_here).transpose(1, 0, 2, 3)
        return outward.reshape(owners, coef_width), cos_phase, sin_phase

    def coef_in(part):
        owned = part.reshape(owners, 2, count_here, cycles_here).astype(jnp.bfloat16)
        return owned.transpose(1, 2, 0, 3).reshape(2, count_here, total_cycles)

    first_out, cos_phase, sin_phase = coef_out(start_map)
    info = jnp.concatenate([info, first_out.astype(jnp.float32)], axis=1)
    info_recv = lax.all_to_all(info, axes, 0, 0, tiled=True)
    first_owned = coef_in(info_recv[:, CAP * 2 :])
    info_recv = info_recv[:, : CAP * 2].reshape(slots, 2)
    want = info_recv[:, 0].astype(jnp.int32)
    want_hot = (want[None, :] == jnp.arange(blocks_here, dtype=jnp.int32)[:, None]).astype(jnp.float32)
    hit_weight = jnp.sum(want_hot * info_recv[None, :, 1], axis=1).reshape(cycles_here, per_cycle)
    divisor = jnp.repeat(1.0 + 0.25 * hit_weight, 128, axis=1)
    want_pick = want_hot.T.astype(jnp.bfloat16)

    current = start_map
    for iteration in range(ITERS):
        map_half = current.astype(jnp.bfloat16).reshape(blocks_here, 128)
        rows_out = jnp.dot(want_pick, map_half, preferred_element_type=jnp.float32)
        rows_out = rows_out.astype(jnp.bfloat16).reshape(owners, CAP * 128)
        if iteration == 0:
            rows_in = lax.all_to_all(rows_out, axes, 0, 0, tiled=True).reshape(slots, 128)
            owned = first_owned
        else:
            outward, cos_phase, sin_phase = coef_out(current)
            send_a = jnp.concatenate([rows_out, outward], axis=1)
            recv_a = lax.all_to_all(send_a, axes, 0, 0, tiled=True)
            rows_in = recv_a[:, : CAP * 128].reshape(slots, 128)
            owned = coef_in(recv_a[:, CAP * 128 :])

        picked = rows_in[slot].reshape(pix_block.shape + (128,))
        binned_terms = pointing_pallas(pointing, picked, samples, det_weight)
        binned_send = jnp.zeros((slots, 128), jnp.float32).at[slot].set(binned_terms.reshape(-1, 128))

        synth = legendre_pallas(owned, legendre, prior_gain, m_own)
        synth_send = synth.reshape(2, count_here, owners, cycles_here).transpose(2, 0, 1, 3)
        send_b = jnp.concatenate(
            [binned_send.reshape(owners, CAP * 128), synth_send.reshape(owners, -1)], axis=1
        )
        recv_b = lax.all_to_all(send_b, axes, 0, 0, tiled=True)
        binned_in = recv_b[:, : CAP * 128].reshape(slots, 128)
        binned = jnp.dot(want_hot, binned_in, precision=highest).reshape(cycles_here, length)
        returned = recv_b[:, CAP * 128 :].reshape(owners, 2, count_here, cycles_here)
        returned = returned.transpose(1, 0, 2, 3).reshape(2, owners * count_here, cycles_here)
        filtered = spectrum_back(
            returned[0].T, returned[1].T, cos_phase, sin_phase, m_values, length
        )
        current = current + (binned - filtered) / divisor
    return current


def solution(mesh):
    placed = (
        P("det", "tm", None),
        P("det", "tm", None, None),
        P("det", "tm"),
        P("det"),
        P(("det", "tm"), None),
        P(("det", "tm"), None, None),
        P(),
        P(),
        P(("det", "tm")),
    )
    return jax.shard_map(
        on_device, mesh=mesh, in_specs=placed, out_specs=P(("det", "tm"), None), check_vma=False
    )
```

```python
import math

import functools

import jax
import jax.numpy as jnp
from jax import lax
from jax.experimental import pallas as pl
from jax.experimental.pallas import tpu as pltpu
from jax.sharding import PartitionSpec as P

ITERS = 2


highest = lax.Precision.HIGHEST


def phase_pair(first_len, second_len, length, sign):
    first = jnp.arange(first_len, dtype=jnp.int32)[:, None]
    second = jnp.arange(second_len, dtype=jnp.int32)[None, :]
    phases = (first * second % length).astype(jnp.float32) * (sign * 2.0 * math.pi / length)
    return (jnp.cos(phases), jnp.sin(phases))


def forward_cycles(field):
    cycles, length = field.shape
    outer_len = length // 128
    shaped = field.reshape(cycles, outer_len, 128)
    cos_outer, sin_outer = phase_pair(outer_len, outer_len, outer_len, -1.0)
    part_re = jnp.einsum("mj,rjk->rmk", cos_outer, shaped, precision=highest)
    part_im = jnp.einsum("mj,rjk->rmk", sin_outer, shaped, precision=highest)
    cos_twist, sin_twist = phase_pair(outer_len, 128, length, -1.0)
    twist_re = part_re * cos_twist - part_im * sin_twist
    twist_im = part_re * sin_twist + part_im * cos_twist
    cos_inner, sin_inner = phase_pair(128, 128, 128, -1.0)
    spec_re = jnp.einsum("rmk,kn->rmn", twist_re, cos_inner, precision=highest) - jnp.einsum(
        "rmk,kn->rmn", twist_im, sin_inner, precision=highest
    )
    spec_im = jnp.einsum("rmk,kn->rmn", twist_re, sin_inner, precision=highest) + jnp.einsum(
        "rmk,kn->rmn", twist_im, cos_inner, precision=highest
    )
    return (spec_re.reshape(cycles, length), spec_im.reshape(cycles, length))


def inverse_cycles(spec_re, spec_im):
    cycles, length = spec_re.shape
    outer_len = length // 128
    shaped_re = spec_re.reshape(cycles, outer_len, 128)
    shaped_im = spec_im.reshape(cycles, outer_len, 128)
    cos_inner, sin_inner = phase_pair(128, 128, 128, 1.0)
    inner_re = jnp.einsum("rmn,nk->rmk", shaped_re, cos_inner, precision=highest) - jnp.einsum(
        "rmn,nk->rmk", shaped_im, sin_inner, precision=highest
    )
    inner_im = jnp.einsum("rmn,nk->rmk", shaped_re, sin_inner, precision=highest) + jnp.einsum(
        "rmn,nk->rmk", shaped_im, cos_inner, precision=highest
    )
    cos_twist, sin_twist = phase_pair(outer_len, 128, length, 1.0)
    twist_re = inner_re * cos_twist - inner_im * sin_twist
    twist_im = inner_re * sin_twist + inner_im * cos_twist
    cos_outer, sin_outer = phase_pair(outer_len, outer_len, outer_len, 1.0)
    field = jnp.einsum("jm,rmk->rjk", cos_outer, twist_re, precision=highest) - jnp.einsum(
        "jm,rmk->rjk", sin_outer, twist_im, precision=highest
    )
    return field.reshape(cycles, length)


def legendre_filter(owned, legendre, prior_gain, m_own):
    count_here, degrees, total_cycles = legendre.shape
    block_rows = min(512, degrees)

    def one_block(index, running):
        start = index * block_rows
        table = lax.dynamic_slice_in_dim(legendre, start, block_rows, 1)
        analysed = jnp.einsum("mlr,cmr->cml", table, owned, preferred_element_type=jnp.float32)
        degree = start + jnp.arange(block_rows, dtype=jnp.int32)
        keep_rows = degree[None, :] >= m_own[:, None]
        gain_block = lax.dynamic_slice_in_dim(prior_gain, start, block_rows)
        scaled = jnp.where(keep_rows[None], analysed * gain_block, 0.0).astype(jnp.bfloat16)
        return running + jnp.einsum(
            "mlr,cml->cmr", table, scaled, preferred_element_type=jnp.float32
        )

    first_block = 0
    initial = jnp.zeros(owned.shape, jnp.float32)
    summed = lax.fori_loop(first_block, degrees // block_rows, one_block, initial)
    return summed * math.sqrt(total_cycles / degrees)


ROWS = 16


def legendre_body(m_ref, coef_ref, gain_ref, tab_ref, out_ref, *, scale):
    k = pl.program_id(0)
    tab = tab_ref[0]
    coef = coef_ref[0]
    analysed = lax.dot_general(
        coef, tab, (((1,), (1,)), ((), ())), preferred_element_type=jnp.float32
    )
    degree = lax.broadcasted_iota(jnp.int32, analysed.shape, 1)
    keep = degree >= m_ref[k]
    scaled = jnp.where(keep, analysed * gain_ref[...], 0.0).astype(jnp.bfloat16)
    synth = jnp.dot(scaled, tab, preferred_element_type=jnp.float32)
    out_ref[0] = synth * scale


def legendre_pallas(owned, legendre, prior_gain, m_own):
    count_here, degrees, total_cycles = legendre.shape
    coef = jnp.zeros((count_here, ROWS, total_cycles), jnp.bfloat16)
    coef = coef.at[:, :2, :].set(owned.transpose(1, 0, 2))
    gain = prior_gain.reshape(1, degrees)
    grid_spec = pltpu.PrefetchScalarGridSpec(
        num_scalar_prefetch=1,
        grid=(count_here,),
        in_specs=[
            pl.BlockSpec((1, ROWS, total_cycles), lambda k, m: (k, 0, 0)),
            pl.BlockSpec((1, degrees), lambda k, m: (0, 0)),
            pl.BlockSpec((1, degrees, total_cycles), lambda k, m: (k, 0, 0)),
        ],
        out_specs=pl.BlockSpec((1, ROWS, total_cycles), lambda k, m: (k, 0, 0)),
    )
    out = pl.pallas_call(
        functools.partial(legendre_body, scale=math.sqrt(total_cycles / degrees)),
        grid_spec=grid_spec,
        out_shape=jax.ShapeDtypeStruct((count_here, ROWS, total_cycles), jnp.float32),
    )(m_own, coef, gain, legendre)
    return out[:, :2, :].transpose(1, 0, 2)


def pointing_body(w_ref, p_ref, x_ref, s_ref, out_ref, *, tblk, nsamp):
    d = pl.program_id(0)
    point = p_ref[0].reshape(tblk * nsamp, p_ref.shape[3])
    picked = x_ref[0]
    every = lax.dot_general(
        picked, point, (((1,), (1,)), ((), ())), preferred_element_type=jnp.float32
    )
    row = lax.broadcasted_iota(jnp.int32, every.shape, 0)
    col = lax.broadcasted_iota(jnp.int32, every.shape, 1)
    mine = row == col // nsamp
    predicted = jnp.sum(jnp.where(mine, every, 0.0), axis=0, keepdims=True)
    resid = (w_ref[d] * (s_ref[0] - predicted)).astype(jnp.bfloat16)
    spread = jnp.where(mine, jnp.broadcast_to(resid, every.shape), jnp.zeros_like(resid))
    out_ref[0] = jnp.dot(spread, point, preferred_element_type=jnp.float32)


def pointing_pallas(pointing, picked, samples, det_weight):
    dets, times, nsamp, npix = pointing.shape
    tblk = times
    samples_row = samples.reshape(dets, 1, times * nsamp)
    grid_spec = pltpu.PrefetchScalarGridSpec(
        num_scalar_prefetch=1,
        grid=(dets, times // tblk),
        in_specs=[
            pl.BlockSpec((1, tblk, nsamp, npix), lambda d, t, w: (d, t, 0, 0)),
            pl.BlockSpec((1, tblk, npix), lambda d, t, w: (d, t, 0)),
            pl.BlockSpec((1, 1, tblk * nsamp), lambda d, t, w: (d, 0, t)),
        ],
        out_specs=pl.BlockSpec((1, tblk, npix), lambda d, t, w: (d, t, 0)),
    )
    return pl.pallas_call(
        functools.partial(pointing_body, tblk=tblk, nsamp=nsamp),
        grid_spec=grid_spec,
        out_shape=jax.ShapeDtypeStruct((dets, times, npix), jnp.float32),
    )(det_weight, pointing, picked, samples_row)


CAP = 8


STRIDE = 4


def order_pick(m_values):
    count = m_values.shape[0]
    offset = m_values - STRIDE * jnp.arange(count, dtype=jnp.int32)
    return offset[:, None] == jnp.arange(STRIDE, dtype=jnp.int32)[None, :]


def spectrum_out(field, m_values, cycle_offset):
    cycles_here, length = field.shape
    count = m_values.shape[0]
    spec_re, spec_im = forward_cycles(field)
    outer_len = length // 128
    spec_re = spec_re.reshape(cycles_here, outer_len, 128).transpose(0, 2, 1)
    spec_im = spec_im.reshape(cycles_here, outer_len, 128).transpose(0, 2, 1)
    pick = order_pick(m_values)[None]
    band = count * STRIDE
    spec_re = spec_re.reshape(cycles_here, length)[:, :band].reshape(cycles_here, count, STRIDE)
    spec_im = spec_im.reshape(cycles_here, length)[:, :band].reshape(cycles_here, count, STRIDE)
    pick_re = jnp.sum(jnp.where(pick, spec_re, 0.0), axis=2)
    pick_im = jnp.sum(jnp.where(pick, spec_im, 0.0), axis=2)
    phases = (m_values[None, :] * cycle_offset[:, None] % length).astype(jnp.float32) * (
        2.0 * math.pi / length
    )
    cos_phase = jnp.cos(phases)
    sin_phase = jnp.sin(phases)
    norm_factor = 1.0 / math.sqrt(length)
    coef_re = (pick_re * cos_phase + pick_im * sin_phase) * norm_factor
    coef_im = (pick_im * cos_phase - pick_re * sin_phase) * norm_factor
    return coef_re, coef_im, cos_phase, sin_phase


def spectrum_back(back_re, back_im, cos_phase, sin_phase, m_values, length):
    cycles_here = back_re.shape[0]
    count = m_values.shape[0]
    outer_len = length // 128
    mode_weight = jnp.where(m_values == 0, 1.0, 2.0).astype(jnp.float32)[None, :]
    harm_re = mode_weight * (back_re * cos_phase - back_im * sin_phase)
    harm_im = mode_weight * (back_re * sin_phase + back_im * cos_phase)
    pick = order_pick(m_values)[None]
    rest = ((0, 0), (0, length - count * STRIDE))
    full_re = jnp.where(pick, harm_re[:, :, None], 0.0).reshape(cycles_here, count * STRIDE)
    full_im = jnp.where(pick, harm_im[:, :, None], 0.0).reshape(cycles_here, count * STRIDE)
    full_re = jnp.pad(full_re, rest).reshape(cycles_here, 128, outer_len)
    full_im = jnp.pad(full_im, rest).reshape(cycles_here, 128, outer_len)
    full_re = full_re.transpose(0, 2, 1).reshape(cycles_here, length)
    full_im = full_im.transpose(0, 2, 1).reshape(cycles_here, length)
    return inverse_cycles(full_re, full_im) / math.sqrt(2.0 * count)


def on_device(
    samples,
    pointing,
    pix_block,
    det_weight,
    start_map,
    legendre,
    prior_gain,
    m_values,
    cycle_offset,
):
    axes = ("det", "tm")
    cycles_here, length = start_map.shape
    per_cycle = length // 128
    owners = lax.axis_size(axes)
    total_cycles = cycles_here * owners
    blocks_here = cycles_here * per_cycle
    count_here = legendre.shape[0]
    owner_index = lax.axis_index(axes)
    m_own = lax.dynamic_slice_in_dim(m_values, owner_index * count_here, count_here)
    slots = owners * CAP

    flat_pix = pix_block.reshape(-1)
    nloc = flat_pix.shape[0]
    owner_of = flat_pix // blocks_here
    within = flat_pix % blocks_here
    order = jnp.arange(nloc, dtype=jnp.int32)
    same = (owner_of[:, None] == owner_of[None, :]) & (order[None, :] < order[:, None])
    rank = jnp.sum(same.astype(jnp.int32), axis=1)
    slot = owner_of * CAP + rank
    slot_hot = (slot[:, None] == jnp.arange(slots, dtype=jnp.int32)[None, :]).astype(jnp.bfloat16)
    weight_of = jnp.broadcast_to(det_weight[:, None], pix_block.shape).reshape(-1)
    info = jnp.stack([within.astype(jnp.float32), weight_of], axis=1)
    info = jnp.zeros((slots, 2), jnp.float32).at[slot].set(info).reshape(owners, CAP * 2)
    coef_width = 2 * count_here * cycles_here

    def coef_out(field):
        coef_re, coef_im, cos_phase, sin_phase = spectrum_out(field, m_values, cycle_offset)
        outward = jnp.stack([coef_re.T, coef_im.T]).astype(jnp.bfloat16)
        outward = outward.reshape(2, owners, count_here, cycles_here).transpose(1, 0, 2, 3)
        return outward.reshape(owners, coef_width), cos_phase, sin_phase

    def coef_in(part):
        owned = part.reshape(owners, 2, count_here, cycles_here).astype(jnp.bfloat16)
        return owned.transpose(1, 2, 0, 3).reshape(2, count_here, total_cycles)

    first_out, cos_phase, sin_phase = coef_out(start_map)
    info = jnp.concatenate([info, first_out.astype(jnp.float32)], axis=1)
    info_recv = lax.all_to_all(info, axes, 0, 0, tiled=True)
    first_owned = coef_in(info_recv[:, CAP * 2 :])
    info_recv = info_recv[:, : CAP * 2].reshape(slots, 2)
    want = info_recv[:, 0].astype(jnp.int32)
    want_hot = (want[None, :] == jnp.arange(blocks_here, dtype=jnp.int32)[:, None]).astype(jnp.float32)
    hit_weight = jnp.sum(want_hot * info_recv[None, :, 1], axis=1).reshape(cycles_here, per_cycle)
    divisor = jnp.repeat(1.0 + 0.25 * hit_weight, 128, axis=1)
    want_pick = want_hot.T.astype(jnp.bfloat16)
    want_sum = want_hot.astype(jnp.bfloat16)

    current = start_map
    for iteration in range(ITERS):
        map_half = current.astype(jnp.bfloat16).reshape(blocks_here, 128)
        rows_out = jnp.dot(want_pick, map_half, preferred_element_type=jnp.float32)
        rows_out = rows_out.astype(jnp.bfloat16).reshape(owners, CAP * 128)
        if iteration == 0:
            rows_in = lax.all_to_all(rows_out, axes, 0, 0, tiled=True).reshape(slots, 128)
            owned = first_owned
        else:
            outward, cos_phase, sin_phase = coef_out(current)
            send_a = jnp.concatenate([rows_out, outward], axis=1)
            recv_a = lax.all_to_all(send_a, axes, 0, 0, tiled=True)
            rows_in = recv_a[:, : CAP * 128].reshape(slots, 128)
            owned = coef_in(recv_a[:, CAP * 128 :])

        picked = jnp.dot(slot_hot, rows_in, preferred_element_type=jnp.float32)
        picked = picked.astype(jnp.bfloat16).reshape(pix_block.shape + (128,))
        binned_terms = pointing_pallas(pointing, picked, samples, det_weight)
        binned_half = binned_terms.reshape(-1, 128).astype(jnp.bfloat16)
        binned_send = jnp.dot(slot_hot.T, binned_half, preferred_element_type=jnp.float32)

        synth = legendre_pallas(owned, legendre, prior_gain, m_own)
        synth_send = synth.reshape(2, count_here, owners, cycles_here).transpose(2, 0, 1, 3)
        synth_send = synth_send.reshape(owners, -1)
        synth_hi = synth_send.astype(jnp.bfloat16)
        synth_lo = (synth_send - synth_hi.astype(jnp.float32)).astype(jnp.bfloat16)
        send_b = jnp.concatenate(
            [binned_send.astype(jnp.bfloat16).reshape(owners, CAP * 128), synth_hi, synth_lo],
            axis=1,
        )
        recv_b = lax.all_to_all(send_b, axes, 0, 0, tiled=True)
        binned_in = recv_b[:, : CAP * 128].reshape(slots, 128)
        binned = jnp.dot(want_sum, binned_in, preferred_element_type=jnp.float32)
        binned = binned.reshape(cycles_here, length)
        returned = recv_b[:, CAP * 128 :].astype(jnp.float32)
        returned = returned[:, :coef_width] + returned[:, coef_width:]
        returned = returned.reshape(owners, 2, count_here, cycles_here)
        returned = returned.transpose(1, 0, 2, 3).reshape(2, owners * count_here, cycles_here)
        filtered = spectrum_back(
            returned[0].T, returned[1].T, cos_phase, sin_phase, m_values, length
        )
        current = current + (binned - filtered) / divisor
    return current


def solution(mesh):
    placed = (
        P("det", "tm", None),
        P("det", "tm", None, None),
        P("det", "tm"),
        P("det"),
        P(("det", "tm"), None),
        P(("det", "tm"), None, None),
        P(),
        P(),
        P(("det", "tm")),
    )
    return jax.shard_map(
        on_device, mesh=mesh, in_specs=placed, out_specs=P(("det", "tm"), None), check_vma=False
    )
```

```python
import math

import functools

import jax
import jax.numpy as jnp
from jax import lax
from jax.experimental import pallas as pl
from jax.experimental.pallas import tpu as pltpu
from jax.sharding import PartitionSpec as P

ITERS = 2


highest = lax.Precision.HIGHEST


def phase_pair(first_len, second_len, length, sign):
    first = jnp.arange(first_len, dtype=jnp.int32)[:, None]
    second = jnp.arange(second_len, dtype=jnp.int32)[None, :]
    phases = (first * second % length).astype(jnp.float32) * (sign * 2.0 * math.pi / length)
    return (jnp.cos(phases), jnp.sin(phases))


def forward_cycles(field):
    cycles, length = field.shape
    outer_len = length // 128
    shaped = field.reshape(cycles, outer_len, 128)
    cos_outer, sin_outer = phase_pair(outer_len, outer_len, outer_len, -1.0)
    part_re = jnp.einsum("mj,rjk->rmk", cos_outer, shaped, precision=highest)
    part_im = jnp.einsum("mj,rjk->rmk", sin_outer, shaped, precision=highest)
    cos_twist, sin_twist = phase_pair(outer_len, 128, length, -1.0)
    twist_re = part_re * cos_twist - part_im * sin_twist
    twist_im = part_re * sin_twist + part_im * cos_twist
    cos_inner, sin_inner = phase_pair(128, 128, 128, -1.0)
    spec_re = jnp.einsum("rmk,kn->rmn", twist_re, cos_inner, precision=highest) - jnp.einsum(
        "rmk,kn->rmn", twist_im, sin_inner, precision=highest
    )
    spec_im = jnp.einsum("rmk,kn->rmn", twist_re, sin_inner, precision=highest) + jnp.einsum(
        "rmk,kn->rmn", twist_im, cos_inner, precision=highest
    )
    return (spec_re.reshape(cycles, length), spec_im.reshape(cycles, length))


def inverse_cycles(spec_re, spec_im):
    cycles, length = spec_re.shape
    outer_len = length // 128
    shaped_re = spec_re.reshape(cycles, outer_len, 128)
    shaped_im = spec_im.reshape(cycles, outer_len, 128)
    cos_inner, sin_inner = phase_pair(128, 128, 128, 1.0)
    inner_re = jnp.einsum("rmn,nk->rmk", shaped_re, cos_inner, precision=highest) - jnp.einsum(
        "rmn,nk->rmk", shaped_im, sin_inner, precision=highest
    )
    inner_im = jnp.einsum("rmn,nk->rmk", shaped_re, sin_inner, precision=highest) + jnp.einsum(
        "rmn,nk->rmk", shaped_im, cos_inner, precision=highest
    )
    cos_twist, sin_twist = phase_pair(outer_len, 128, length, 1.0)
    twist_re = inner_re * cos_twist - inner_im * sin_twist
    twist_im = inner_re * sin_twist + inner_im * cos_twist
    cos_outer, sin_outer = phase_pair(outer_len, outer_len, outer_len, 1.0)
    field = jnp.einsum("jm,rmk->rjk", cos_outer, twist_re, precision=highest) - jnp.einsum(
        "jm,rmk->rjk", sin_outer, twist_im, precision=highest
    )
    return field.reshape(cycles, length)


def forward_band(field, band):
    cycles, length = field.shape
    outer_len = length // 128
    band_cols = band // outer_len
    shaped = field.reshape(cycles, outer_len, 128)
    cos_outer, sin_outer = phase_pair(outer_len, outer_len, outer_len, -1.0)
    part = jnp.einsum(
        "mj,rjk->rmk", jnp.concatenate([cos_outer, sin_outer], axis=0), shaped, precision=highest
    )
    part_re, part_im = part[:, :outer_len], part[:, outer_len:]
    cos_twist, sin_twist = phase_pair(outer_len, 128, length, -1.0)
    twist = jnp.concatenate(
        [part_re * cos_twist - part_im * sin_twist, part_re * sin_twist + part_im * cos_twist],
        axis=2,
    )
    cos_inner, sin_inner = phase_pair(128, band_cols, 128, -1.0)
    inner = jnp.concatenate(
        [jnp.concatenate([cos_inner, sin_inner], axis=1),
         jnp.concatenate([-sin_inner, cos_inner], axis=1)],
        axis=0,
    )
    spec = jnp.einsum("rmk,kn->rmn", twist, inner, precision=highest)
    return spec[:, :, :band_cols], spec[:, :, band_cols:]


def inverse_band(spec_re, spec_im, length):
    cycles, outer_len, band_cols = spec_re.shape
    cos_inner, sin_inner = phase_pair(band_cols, 128, 128, 1.0)
    inner = jnp.concatenate(
        [jnp.concatenate([cos_inner, sin_inner], axis=1),
         jnp.concatenate([-sin_inner, cos_inner], axis=1)],
        axis=0,
    )
    inner_out = jnp.einsum(
        "rmn,nk->rmk", jnp.concatenate([spec_re, spec_im], axis=2), inner, precision=highest
    )
    inner_re, inner_im = inner_out[:, :, :128], inner_out[:, :, 128:]
    cos_twist, sin_twist = phase_pair(outer_len, 128, length, 1.0)
    twist = jnp.concatenate(
        [inner_re * cos_twist - inner_im * sin_twist, inner_re * sin_twist + inner_im * cos_twist],
        axis=1,
    )
    cos_outer, sin_outer = phase_pair(outer_len, outer_len, outer_len, 1.0)
    outer = jnp.concatenate([cos_outer, -sin_outer], axis=1)
    field = jnp.einsum("jm,rmk->rjk", outer, twist, precision=highest)
    return field.reshape(cycles, length)


def legendre_filter(owned, legendre, prior_gain, m_own):
    count_here, degrees, total_cycles = legendre.shape
    block_rows = min(512, degrees)

    def one_block(index, running):
        start = index * block_rows
        table = lax.dynamic_slice_in_dim(legendre, start, block_rows, 1)
        analysed = jnp.einsum("mlr,cmr->cml", table, owned, preferred_element_type=jnp.float32)
        degree = start + jnp.arange(block_rows, dtype=jnp.int32)
        keep_rows = degree[None, :] >= m_own[:, None]
        gain_block = lax.dynamic_slice_in_dim(prior_gain, start, block_rows)
        scaled = jnp.where(keep_rows[None], analysed * gain_block, 0.0).astype(jnp.bfloat16)
        return running + jnp.einsum(
            "mlr,cml->cmr", table, scaled, preferred_element_type=jnp.float32
        )

    first_block = 0
    initial = jnp.zeros(owned.shape, jnp.float32)
    summed = lax.fori_loop(first_block, degrees // block_rows, one_block, initial)
    return summed * math.sqrt(total_cycles / degrees)


ROWS = 16


def legendre_body(m_ref, coef_ref, gain_ref, tab_ref, out_ref, *, scale):
    k = pl.program_id(0)
    tab = tab_ref[0]
    coef = coef_ref[0]
    analysed = lax.dot_general(
        coef, tab, (((1,), (1,)), ((), ())), preferred_element_type=jnp.float32
    )
    degree = lax.broadcasted_iota(jnp.int32, analysed.shape, 1)
    keep = degree >= m_ref[k]
    scaled = jnp.where(keep, analysed * gain_ref[...], 0.0).astype(jnp.bfloat16)
    synth = jnp.dot(scaled, tab, preferred_element_type=jnp.float32)
    out_ref[0] = synth * scale


def legendre_pallas(owned, legendre, prior_gain, m_own):
    count_here, degrees, total_cycles = legendre.shape
    coef = jnp.zeros((count_here, ROWS, total_cycles), jnp.bfloat16)
    coef = coef.at[:, :2, :].set(owned.transpose(1, 0, 2))
    gain = prior_gain.reshape(1, degrees)
    grid_spec = pltpu.PrefetchScalarGridSpec(
        num_scalar_prefetch=1,
        grid=(count_here,),
        in_specs=[
            pl.BlockSpec((1, ROWS, total_cycles), lambda k, m: (k, 0, 0)),
            pl.BlockSpec((1, degrees), lambda k, m: (0, 0)),
            pl.BlockSpec((1, degrees, total_cycles), lambda k, m: (k, 0, 0)),
        ],
        out_specs=pl.BlockSpec((1, ROWS, total_cycles), lambda k, m: (k, 0, 0)),
    )
    out = pl.pallas_call(
        functools.partial(legendre_body, scale=math.sqrt(total_cycles / degrees)),
        grid_spec=grid_spec,
        out_shape=jax.ShapeDtypeStruct((count_here, ROWS, total_cycles), jnp.float32),
    )(m_own, coef, gain, legendre)
    return out[:, :2, :].transpose(1, 0, 2)


def pointing_body(w_ref, p_ref, x_ref, s_ref, out_ref, *, tblk, nsamp):
    d = pl.program_id(0)
    point = p_ref[0].reshape(tblk * nsamp, p_ref.shape[3])
    picked = x_ref[0]
    every = lax.dot_general(
        picked, point, (((1,), (1,)), ((), ())), preferred_element_type=jnp.float32
    )
    row = lax.broadcasted_iota(jnp.int32, every.shape, 0)
    col = lax.broadcasted_iota(jnp.int32, every.shape, 1)
    mine = row == col // nsamp
    predicted = jnp.sum(jnp.where(mine, every, 0.0), axis=0, keepdims=True)
    resid = (w_ref[d] * (s_ref[0] - predicted)).astype(jnp.bfloat16)
    spread = jnp.where(mine, jnp.broadcast_to(resid, every.shape), jnp.zeros_like(resid))
    out_ref[0] = jnp.dot(spread, point, preferred_element_type=jnp.float32)


def pointing_pallas(pointing, picked, samples, det_weight):
    dets, times, nsamp, npix = pointing.shape
    tblk = times
    samples_row = samples.reshape(dets, 1, times * nsamp)
    grid_spec = pltpu.PrefetchScalarGridSpec(
        num_scalar_prefetch=1,
        grid=(dets, times // tblk),
        in_specs=[
            pl.BlockSpec((1, tblk, nsamp, npix), lambda d, t, w: (d, t, 0, 0)),
            pl.BlockSpec((1, tblk, npix), lambda d, t, w: (d, t, 0)),
            pl.BlockSpec((1, 1, tblk * nsamp), lambda d, t, w: (d, 0, t)),
        ],
        out_specs=pl.BlockSpec((1, tblk, npix), lambda d, t, w: (d, t, 0)),
    )
    return pl.pallas_call(
        functools.partial(pointing_body, tblk=tblk, nsamp=nsamp),
        grid_spec=grid_spec,
        out_shape=jax.ShapeDtypeStruct((dets, times, npix), jnp.float32),
    )(det_weight, pointing, picked, samples_row)


CAP = 8


STRIDE = 4


def order_pick(m_values):
    count = m_values.shape[0]
    offset = m_values - STRIDE * jnp.arange(count, dtype=jnp.int32)
    return offset[:, None] == jnp.arange(STRIDE, dtype=jnp.int32)[None, :]


def spectrum_out(field, m_values, cycle_offset):
    cycles_here, length = field.shape
    count = m_values.shape[0]
    band = count * STRIDE
    spec_re, spec_im = forward_band(field, band)
    spec_re = spec_re.transpose(0, 2, 1).reshape(cycles_here, count, STRIDE)
    spec_im = spec_im.transpose(0, 2, 1).reshape(cycles_here, count, STRIDE)
    pick = order_pick(m_values)[None]
    pick_re = jnp.sum(jnp.where(pick, spec_re, 0.0), axis=2)
    pick_im = jnp.sum(jnp.where(pick, spec_im, 0.0), axis=2)
    phases = (m_values[None, :] * cycle_offset[:, None] % length).astype(jnp.float32) * (
        2.0 * math.pi / length
    )
    cos_phase = jnp.cos(phases)
    sin_phase = jnp.sin(phases)
    norm_factor = 1.0 / math.sqrt(length)
    coef_re = (pick_re * cos_phase + pick_im * sin_phase) * norm_factor
    coef_im = (pick_im * cos_phase - pick_re * sin_phase) * norm_factor
    return coef_re, coef_im, cos_phase, sin_phase


def spectrum_back(back_re, back_im, cos_phase, sin_phase, m_values, length):
    cycles_here = back_re.shape[0]
    count = m_values.shape[0]
    outer_len = length // 128
    mode_weight = jnp.where(m_values == 0, 1.0, 2.0).astype(jnp.float32)[None, :]
    harm_re = mode_weight * (back_re * cos_phase - back_im * sin_phase)
    harm_im = mode_weight * (back_re * sin_phase + back_im * cos_phase)
    pick = order_pick(m_values)[None]
    band_cols = count * STRIDE // outer_len
    full_re = jnp.where(pick, harm_re[:, :, None], 0.0).reshape(cycles_here, band_cols, outer_len)
    full_im = jnp.where(pick, harm_im[:, :, None], 0.0).reshape(cycles_here, band_cols, outer_len)
    full_re = full_re.transpose(0, 2, 1)
    full_im = full_im.transpose(0, 2, 1)
    return inverse_band(full_re, full_im, length) / math.sqrt(2.0 * count)


def on_device(
    samples,
    pointing,
    pix_block,
    det_weight,
    start_map,
    legendre,
    prior_gain,
    m_values,
    cycle_offset,
):
    axes = ("det", "tm")
    cycles_here, length = start_map.shape
    per_cycle = length // 128
    owners = lax.axis_size(axes)
    total_cycles = cycles_here * owners
    blocks_here = cycles_here * per_cycle
    count_here = legendre.shape[0]
    owner_index = lax.axis_index(axes)
    m_own = lax.dynamic_slice_in_dim(m_values, owner_index * count_here, count_here)
    slots = owners * CAP

    flat_pix = pix_block.reshape(-1)
    nloc = flat_pix.shape[0]
    owner_of = flat_pix // blocks_here
    within = flat_pix % blocks_here
    order = jnp.arange(nloc, dtype=jnp.int32)
    same = (owner_of[:, None] == owner_of[None, :]) & (order[None, :] < order[:, None])
    rank = jnp.sum(same.astype(jnp.int32), axis=1)
    slot = owner_of * CAP + rank
    weight_of = jnp.broadcast_to(det_weight[:, None], pix_block.shape).reshape(-1)
    info = jnp.stack([within.astype(jnp.float32), weight_of], axis=1)
    info = jnp.zeros((slots, 2), jnp.float32).at[slot].set(info).reshape(owners, CAP * 2)
    coef_width = 2 * count_here * cycles_here

    def coef_out(field):
        coef_re, coef_im, cos_phase, sin_phase = spectrum_out(field, m_values, cycle_offset)
        outward = jnp.stack([coef_re.T, coef_im.T]).astype(jnp.bfloat16)
        outward = outward.reshape(2, owners, count_here, cycles_here).transpose(1, 0, 2, 3)
        return outward.reshape(owners, coef_width), cos_phase, sin_phase

    def coef_in(part):
        owned = part.reshape(owners, 2, count_here, cycles_here).astype(jnp.bfloat16)
        return owned.transpose(1, 2, 0, 3).reshape(2, count_here, total_cycles)

    first_out, cos_phase, sin_phase = coef_out(start_map)
    info = jnp.concatenate([info, first_out.astype(jnp.float32)], axis=1)
    info_recv = lax.all_to_all(info, axes, 0, 0, tiled=True)
    first_owned = coef_in(info_recv[:, CAP * 2 :])
    info_recv = info_recv[:, : CAP * 2].reshape(slots, 2)
    want = info_recv[:, 0].astype(jnp.int32)
    want_hot = (want[None, :] == jnp.arange(blocks_here, dtype=jnp.int32)[:, None]).astype(jnp.float32)
    hit_weight = jnp.sum(want_hot * info_recv[None, :, 1], axis=1).reshape(cycles_here, per_cycle)
    divisor = jnp.repeat(1.0 + 0.25 * hit_weight, 128, axis=1)
    want_pick = want_hot.T.astype(jnp.bfloat16)

    current = start_map
    for iteration in range(ITERS):
        map_half = current.astype(jnp.bfloat16).reshape(blocks_here, 128)
        rows_out = jnp.dot(want_pick, map_half, preferred_element_type=jnp.float32)
        rows_out = rows_out.astype(jnp.bfloat16).reshape(owners, CAP * 128)
        if iteration == 0:
            rows_in = lax.all_to_all(rows_out, axes, 0, 0, tiled=True).reshape(slots, 128)
            owned = first_owned
        else:
            outward, cos_phase, sin_phase = coef_out(current)
            send_a = jnp.concatenate([rows_out, outward], axis=1)
            recv_a = lax.all_to_all(send_a, axes, 0, 0, tiled=True)
            rows_in = recv_a[:, : CAP * 128].reshape(slots, 128)
            owned = coef_in(recv_a[:, CAP * 128 :])

        picked = rows_in[slot].reshape(pix_block.shape + (128,))
        binned_terms = pointing_pallas(pointing, picked, samples, det_weight)
        binned_send = jnp.zeros((slots, 128), jnp.float32).at[slot].set(binned_terms.reshape(-1, 128))

        synth = legendre_pallas(owned, legendre, prior_gain, m_own)
        synth_send = synth.reshape(2, count_here, owners, cycles_here).transpose(2, 0, 1, 3)
        send_b = jnp.concatenate(
            [binned_send.reshape(owners, CAP * 128), synth_send.reshape(owners, -1)], axis=1
        )
        recv_b = lax.all_to_all(send_b, axes, 0, 0, tiled=True)
        binned_in = recv_b[:, : CAP * 128].reshape(slots, 128)
        binned = jnp.dot(want_hot, binned_in, precision=highest).reshape(cycles_here, length)
        returned = recv_b[:, CAP * 128 :].reshape(owners, 2, count_here, cycles_here)
        returned = returned.transpose(1, 0, 2, 3).reshape(2, owners * count_here, cycles_here)
        filtered = spectrum_back(
            returned[0].T, returned[1].T, cos_phase, sin_phase, m_values, length
        )
        current = current + (binned - filtered) / divisor
    return current


def solution(mesh):
    placed = (
        P("det", "tm", None),
        P("det", "tm", None, None),
        P("det", "tm"),
        P("det"),
        P(("det", "tm"), None),
        P(("det", "tm"), None, None),
        P(),
        P(),
        P(("det", "tm")),
    )
    return jax.shard_map(
        on_device, mesh=mesh, in_specs=placed, out_specs=P(("det", "tm"), None), check_vma=False
    )
```

```python
import math

import functools

import jax
import jax.numpy as jnp
from jax import lax
from jax.experimental import pallas as pl
from jax.experimental.pallas import tpu as pltpu
from jax.sharding import PartitionSpec as P

ITERS = 2


highest = lax.Precision.HIGHEST


def phase_pair(first_len, second_len, length, sign):
    first = jnp.arange(first_len, dtype=jnp.int32)[:, None]
    second = jnp.arange(second_len, dtype=jnp.int32)[None, :]
    phases = (first * second % length).astype(jnp.float32) * (sign * 2.0 * math.pi / length)
    return (jnp.cos(phases), jnp.sin(phases))


def forward_cycles(field):
    cycles, length = field.shape
    outer_len = length // 128
    shaped = field.reshape(cycles, outer_len, 128)
    cos_outer, sin_outer = phase_pair(outer_len, outer_len, outer_len, -1.0)
    part_re = jnp.einsum("mj,rjk->rmk", cos_outer, shaped, precision=highest)
    part_im = jnp.einsum("mj,rjk->rmk", sin_outer, shaped, precision=highest)
    cos_twist, sin_twist = phase_pair(outer_len, 128, length, -1.0)
    twist_re = part_re * cos_twist - part_im * sin_twist
    twist_im = part_re * sin_twist + part_im * cos_twist
    cos_inner, sin_inner = phase_pair(128, 128, 128, -1.0)
    spec_re = jnp.einsum("rmk,kn->rmn", twist_re, cos_inner, precision=highest) - jnp.einsum(
        "rmk,kn->rmn", twist_im, sin_inner, precision=highest
    )
    spec_im = jnp.einsum("rmk,kn->rmn", twist_re, sin_inner, precision=highest) + jnp.einsum(
        "rmk,kn->rmn", twist_im, cos_inner, precision=highest
    )
    return (spec_re.reshape(cycles, length), spec_im.reshape(cycles, length))


def inverse_cycles(spec_re, spec_im):
    cycles, length = spec_re.shape
    outer_len = length // 128
    shaped_re = spec_re.reshape(cycles, outer_len, 128)
    shaped_im = spec_im.reshape(cycles, outer_len, 128)
    cos_inner, sin_inner = phase_pair(128, 128, 128, 1.0)
    inner_re = jnp.einsum("rmn,nk->rmk", shaped_re, cos_inner, precision=highest) - jnp.einsum(
        "rmn,nk->rmk", shaped_im, sin_inner, precision=highest
    )
    inner_im = jnp.einsum("rmn,nk->rmk", shaped_re, sin_inner, precision=highest) + jnp.einsum(
        "rmn,nk->rmk", shaped_im, cos_inner, precision=highest
    )
    cos_twist, sin_twist = phase_pair(outer_len, 128, length, 1.0)
    twist_re = inner_re * cos_twist - inner_im * sin_twist
    twist_im = inner_re * sin_twist + inner_im * cos_twist
    cos_outer, sin_outer = phase_pair(outer_len, outer_len, outer_len, 1.0)
    field = jnp.einsum("jm,rmk->rjk", cos_outer, twist_re, precision=highest) - jnp.einsum(
        "jm,rmk->rjk", sin_outer, twist_im, precision=highest
    )
    return field.reshape(cycles, length)


def forward_band(field, band):
    cycles, length = field.shape
    outer_len = length // 128
    band_cols = band // outer_len
    shaped = field.reshape(cycles, outer_len, 128)
    cos_outer, sin_outer = phase_pair(outer_len, outer_len, outer_len, -1.0)
    part = jnp.einsum(
        "mj,rjk->rmk", jnp.concatenate([cos_outer, sin_outer], axis=0), shaped, precision=highest
    )
    part_re, part_im = part[:, :outer_len], part[:, outer_len:]
    cos_twist, sin_twist = phase_pair(outer_len, 128, length, -1.0)
    twist = jnp.concatenate(
        [part_re * cos_twist - part_im * sin_twist, part_re * sin_twist + part_im * cos_twist],
        axis=2,
    )
    cos_inner, sin_inner = phase_pair(128, band_cols, 128, -1.0)
    inner = jnp.concatenate(
        [jnp.concatenate([cos_inner, sin_inner], axis=1),
         jnp.concatenate([-sin_inner, cos_inner], axis=1)],
        axis=0,
    )
    spec = jnp.einsum("rmk,kn->rmn", twist, inner, precision=highest)
    return spec[:, :, :band_cols], spec[:, :, band_cols:]


def inverse_band(spec_re, spec_im, length):
    cycles, outer_len, band_cols = spec_re.shape
    cos_inner, sin_inner = phase_pair(band_cols, 128, 128, 1.0)
    inner = jnp.concatenate(
        [jnp.concatenate([cos_inner, sin_inner], axis=1),
         jnp.concatenate([-sin_inner, cos_inner], axis=1)],
        axis=0,
    )
    inner_out = jnp.einsum(
        "rmn,nk->rmk", jnp.concatenate([spec_re, spec_im], axis=2), inner, precision=highest
    )
    inner_re, inner_im = inner_out[:, :, :128], inner_out[:, :, 128:]
    cos_twist, sin_twist = phase_pair(outer_len, 128, length, 1.0)
    twist = jnp.concatenate(
        [inner_re * cos_twist - inner_im * sin_twist, inner_re * sin_twist + inner_im * cos_twist],
        axis=1,
    )
    cos_outer, sin_outer = phase_pair(outer_len, outer_len, outer_len, 1.0)
    outer = jnp.concatenate([cos_outer, -sin_outer], axis=1)
    field = jnp.einsum("jm,rmk->rjk", outer, twist, precision=highest)
    return field.reshape(cycles, length)


def legendre_filter(owned, legendre, prior_gain, m_own):
    count_here, degrees, total_cycles = legendre.shape
    block_rows = min(512, degrees)

    def one_block(index, running):
        start = index * block_rows
        table = lax.dynamic_slice_in_dim(legendre, start, block_rows, 1)
        analysed = jnp.einsum("mlr,cmr->cml", table, owned, preferred_element_type=jnp.float32)
        degree = start + jnp.arange(block_rows, dtype=jnp.int32)
        keep_rows = degree[None, :] >= m_own[:, None]
        gain_block = lax.dynamic_slice_in_dim(prior_gain, start, block_rows)
        scaled = jnp.where(keep_rows[None], analysed * gain_block, 0.0).astype(jnp.bfloat16)
        return running + jnp.einsum(
            "mlr,cml->cmr", table, scaled, preferred_element_type=jnp.float32
        )

    first_block = 0
    initial = jnp.zeros(owned.shape, jnp.float32)
    summed = lax.fori_loop(first_block, degrees // block_rows, one_block, initial)
    return summed * math.sqrt(total_cycles / degrees)


ROWS = 16


def legendre_body(base_ref, m_ref, coef_ref, gain_ref, tab_ref, out_ref, *, scale):
    k = pl.program_id(0)
    tab = tab_ref[0]
    coef = coef_ref[0]
    analysed = lax.dot_general(
        coef, tab, (((1,), (1,)), ((), ())), preferred_element_type=jnp.float32
    )
    degree = lax.broadcasted_iota(jnp.int32, analysed.shape, 1)
    keep = degree >= m_ref[base_ref[0] + k]
    scaled = jnp.where(keep, analysed * gain_ref[...], 0.0).astype(jnp.bfloat16)
    synth = jnp.dot(scaled, tab, preferred_element_type=jnp.float32)
    out_ref[0] = synth * scale


def legendre_pallas(owned, legendre, prior_gain, m_values, first):
    count_here, degrees, total_cycles = legendre.shape
    coef = jnp.zeros((count_here, ROWS, total_cycles), jnp.bfloat16)
    coef = coef.at[:, :2, :].set(owned.transpose(1, 0, 2))
    gain = prior_gain.reshape(1, degrees)
    grid_spec = pltpu.PrefetchScalarGridSpec(
        num_scalar_prefetch=2,
        grid=(count_here,),
        in_specs=[
            pl.BlockSpec((1, ROWS, total_cycles), lambda k, b, m: (k, 0, 0)),
            pl.BlockSpec((1, degrees), lambda k, b, m: (0, 0)),
            pl.BlockSpec((1, degrees, total_cycles), lambda k, b, m: (k, 0, 0)),
        ],
        out_specs=pl.BlockSpec((1, ROWS, total_cycles), lambda k, b, m: (k, 0, 0)),
    )
    out = pl.pallas_call(
        functools.partial(legendre_body, scale=math.sqrt(total_cycles / degrees)),
        grid_spec=grid_spec,
        out_shape=jax.ShapeDtypeStruct((count_here, ROWS, total_cycles), jnp.float32),
    )(first, m_values, coef, gain, legendre)
    return out[:, :2, :].transpose(1, 0, 2)


def pointing_body(w_ref, p_ref, x_ref, s_ref, out_ref, *, tblk, nsamp):
    d = pl.program_id(0)
    point = p_ref[0].reshape(tblk * nsamp, p_ref.shape[3])
    picked = x_ref[0]
    every = lax.dot_general(
        picked, point, (((1,), (1,)), ((), ())), preferred_element_type=jnp.float32
    )
    row = lax.broadcasted_iota(jnp.int32, every.shape, 0)
    col = lax.broadcasted_iota(jnp.int32, every.shape, 1)
    mine = row == col // nsamp
    predicted = jnp.sum(jnp.where(mine, every, 0.0), axis=0, keepdims=True)
    resid = (w_ref[d] * (s_ref[0] - predicted)).astype(jnp.bfloat16)
    spread = jnp.where(mine, jnp.broadcast_to(resid, every.shape), jnp.zeros_like(resid))
    out_ref[0] = jnp.dot(spread, point, preferred_element_type=jnp.float32)


def pointing_pallas(pointing, picked, samples, det_weight):
    dets, times, nsamp, npix = pointing.shape
    tblk = times
    samples_row = samples.reshape(dets, 1, times * nsamp)
    grid_spec = pltpu.PrefetchScalarGridSpec(
        num_scalar_prefetch=1,
        grid=(dets, times // tblk),
        in_specs=[
            pl.BlockSpec((1, tblk, nsamp, npix), lambda d, t, w: (d, t, 0, 0)),
            pl.BlockSpec((1, tblk, npix), lambda d, t, w: (d, t, 0)),
            pl.BlockSpec((1, 1, tblk * nsamp), lambda d, t, w: (d, 0, t)),
        ],
        out_specs=pl.BlockSpec((1, tblk, npix), lambda d, t, w: (d, t, 0)),
    )
    return pl.pallas_call(
        functools.partial(pointing_body, tblk=tblk, nsamp=nsamp),
        grid_spec=grid_spec,
        out_shape=jax.ShapeDtypeStruct((dets, times, npix), jnp.float32),
    )(det_weight, pointing, picked, samples_row)


CAP = 8


STRIDE = 4


def order_pick(m_values):
    count = m_values.shape[0]
    offset = m_values - STRIDE * jnp.arange(count, dtype=jnp.int32)
    return offset[:, None] == jnp.arange(STRIDE, dtype=jnp.int32)[None, :]


def spectrum_out(field, m_values, cycle_offset):
    cycles_here, length = field.shape
    count = m_values.shape[0]
    band = count * STRIDE
    spec_re, spec_im = forward_band(field, band)
    spec_re = spec_re.transpose(0, 2, 1).reshape(cycles_here, count, STRIDE)
    spec_im = spec_im.transpose(0, 2, 1).reshape(cycles_here, count, STRIDE)
    pick = order_pick(m_values)[None]
    pick_re = jnp.sum(jnp.where(pick, spec_re, 0.0), axis=2)
    pick_im = jnp.sum(jnp.where(pick, spec_im, 0.0), axis=2)
    phases = (m_values[None, :] * cycle_offset[:, None] % length).astype(jnp.float32) * (
        2.0 * math.pi / length
    )
    cos_phase = jnp.cos(phases)
    sin_phase = jnp.sin(phases)
    norm_factor = 1.0 / math.sqrt(length)
    coef_re = (pick_re * cos_phase + pick_im * sin_phase) * norm_factor
    coef_im = (pick_im * cos_phase - pick_re * sin_phase) * norm_factor
    return coef_re, coef_im, cos_phase, sin_phase


def spectrum_back(back_re, back_im, cos_phase, sin_phase, m_values, length):
    cycles_here = back_re.shape[0]
    count = m_values.shape[0]
    outer_len = length // 128
    mode_weight = jnp.where(m_values == 0, 1.0, 2.0).astype(jnp.float32)[None, :]
    harm_re = mode_weight * (back_re * cos_phase - back_im * sin_phase)
    harm_im = mode_weight * (back_re * sin_phase + back_im * cos_phase)
    pick = order_pick(m_values)[None]
    band_cols = count * STRIDE // outer_len
    full_re = jnp.where(pick, harm_re[:, :, None], 0.0).reshape(cycles_here, band_cols, outer_len)
    full_im = jnp.where(pick, harm_im[:, :, None], 0.0).reshape(cycles_here, band_cols, outer_len)
    full_re = full_re.transpose(0, 2, 1)
    full_im = full_im.transpose(0, 2, 1)
    return inverse_band(full_re, full_im, length) / math.sqrt(2.0 * count)


def on_device(
    samples,
    pointing,
    pix_block,
    det_weight,
    start_map,
    legendre,
    prior_gain,
    m_values,
    cycle_offset,
):
    axes = ("det", "tm")
    cycles_here, length = start_map.shape
    per_cycle = length // 128
    owners = lax.axis_size(axes)
    total_cycles = cycles_here * owners
    blocks_here = cycles_here * per_cycle
    count_here = legendre.shape[0]
    owner_index = lax.axis_index(axes)
    first_order = jnp.full((1,), owner_index * count_here, jnp.int32)
    slots = owners * CAP

    flat_pix = pix_block.reshape(-1)
    nloc = flat_pix.shape[0]
    owner_of = flat_pix // blocks_here
    within = flat_pix % blocks_here
    order = jnp.arange(nloc, dtype=jnp.int32)
    same = (owner_of[:, None] == owner_of[None, :]) & (order[None, :] < order[:, None])
    rank = jnp.sum(same.astype(jnp.int32), axis=1)
    slot = owner_of * CAP + rank
    slot_hot = slot[:, None] == jnp.arange(slots, dtype=jnp.int32)[None, :]
    weight_of = jnp.broadcast_to(det_weight[:, None], pix_block.shape).reshape(-1)
    info = jnp.stack([within.astype(jnp.float32), weight_of], axis=1)
    info = jnp.zeros((slots, 2), jnp.float32).at[slot].set(info).reshape(owners, CAP * 2)
    coef_width = 2 * count_here * cycles_here

    def coef_out(field):
        coef_re, coef_im, cos_phase, sin_phase = spectrum_out(field, m_values, cycle_offset)
        outward = jnp.stack([coef_re.T, coef_im.T]).astype(jnp.bfloat16)
        outward = outward.reshape(2, owners, count_here, cycles_here).transpose(1, 0, 2, 3)
        return outward.reshape(owners, coef_width), cos_phase, sin_phase

    def coef_in(part):
        owned = part.reshape(owners, 2, count_here, cycles_here).astype(jnp.bfloat16)
        return owned.transpose(1, 2, 0, 3).reshape(2, count_here, total_cycles)

    first_out, cos_phase, sin_phase = coef_out(start_map)
    info = jnp.concatenate([info, first_out.astype(jnp.float32)], axis=1)
    info_recv = lax.all_to_all(info, axes, 0, 0, tiled=True)
    first_owned = coef_in(info_recv[:, CAP * 2 :])
    info_recv = info_recv[:, : CAP * 2].reshape(slots, 2)
    want = info_recv[:, 0].astype(jnp.int32)
    want_hot = (want[None, :] == jnp.arange(blocks_here, dtype=jnp.int32)[:, None]).astype(jnp.float32)
    hit_weight = jnp.sum(want_hot * info_recv[None, :, 1], axis=1).reshape(cycles_here, per_cycle)
    divisor = jnp.repeat(1.0 + 0.25 * hit_weight, 128, axis=1)
    want_pick = want_hot.T.astype(jnp.bfloat16)

    current = start_map
    for iteration in range(ITERS):
        map_half = current.astype(jnp.bfloat16).reshape(blocks_here, 128)
        rows_out = jnp.dot(want_pick, map_half, preferred_element_type=jnp.float32)
        rows_out = rows_out.astype(jnp.bfloat16).reshape(owners, CAP * 128)
        if iteration == 0:
            rows_in = lax.all_to_all(rows_out, axes, 0, 0, tiled=True).reshape(slots, 128)
            owned = first_owned
        else:
            outward, cos_phase, sin_phase = coef_out(current)
            send_a = jnp.concatenate([rows_out, outward], axis=1)
            recv_a = lax.all_to_all(send_a, axes, 0, 0, tiled=True)
            rows_in = recv_a[:, : CAP * 128].reshape(slots, 128)
            owned = coef_in(recv_a[:, CAP * 128 :])

        picked = jnp.dot(slot_hot.astype(jnp.bfloat16), rows_in, preferred_element_type=jnp.float32)
        picked = picked.astype(jnp.bfloat16).reshape(pix_block.shape + (128,))
        binned_terms = pointing_pallas(pointing, picked, samples, det_weight)
        binned_send = jnp.dot(
            slot_hot.T.astype(jnp.float32), binned_terms.reshape(-1, 128), precision=highest
        )

        synth = legendre_pallas(owned, legendre, prior_gain, m_values, first_order)
        synth_send = synth.reshape(2, count_here, owners, cycles_here).transpose(2, 0, 1, 3)
        send_b = jnp.concatenate(
            [binned_send.reshape(owners, CAP * 128), synth_send.reshape(owners, -1)], axis=1
        )
        recv_b = lax.all_to_all(send_b, axes, 0, 0, tiled=True)
        binned_in = recv_b[:, : CAP * 128].reshape(slots, 128)
        binned = jnp.dot(want_hot, binned_in, precision=highest).reshape(cycles_here, length)
        returned = recv_b[:, CAP * 128 :].reshape(owners, 2, count_here, cycles_here)
        returned = returned.transpose(1, 0, 2, 3).reshape(2, owners * count_here, cycles_here)
        filtered = spectrum_back(
            returned[0].T, returned[1].T, cos_phase, sin_phase, m_values, length
        )
        current = current + (binned - filtered) / divisor
    return current


def solution(mesh):
    placed = (
        P("det", "tm", None),
        P("det", "tm", None, None),
        P("det", "tm"),
        P("det"),
        P(("det", "tm"), None),
        P(("det", "tm"), None, None),
        P(),
        P(),
        P(("det", "tm")),
    )
    return jax.shard_map(
        on_device, mesh=mesh, in_specs=placed, out_specs=P(("det", "tm"), None), check_vma=False
    )
```

```python
import math

import functools

import jax
import jax.numpy as jnp
from jax import lax
from jax.experimental import pallas as pl
from jax.experimental.pallas import tpu as pltpu
from jax.sharding import PartitionSpec as P

ITERS = 2


highest = lax.Precision.HIGHEST


def phase_pair(first_len, second_len, length, sign):
    first = jnp.arange(first_len, dtype=jnp.int32)[:, None]
    second = jnp.arange(second_len, dtype=jnp.int32)[None, :]
    phases = (first * second % length).astype(jnp.float32) * (sign * 2.0 * math.pi / length)
    return (jnp.cos(phases), jnp.sin(phases))


def forward_cycles(field):
    cycles, length = field.shape
    outer_len = length // 128
    shaped = field.reshape(cycles, outer_len, 128)
    cos_outer, sin_outer = phase_pair(outer_len, outer_len, outer_len, -1.0)
    part_re = jnp.einsum("mj,rjk->rmk", cos_outer, shaped, precision=highest)
    part_im = jnp.einsum("mj,rjk->rmk", sin_outer, shaped, precision=highest)
    cos_twist, sin_twist = phase_pair(outer_len, 128, length, -1.0)
    twist_re = part_re * cos_twist - part_im * sin_twist
    twist_im = part_re * sin_twist + part_im * cos_twist
    cos_inner, sin_inner = phase_pair(128, 128, 128, -1.0)
    spec_re = jnp.einsum("rmk,kn->rmn", twist_re, cos_inner, precision=highest) - jnp.einsum(
        "rmk,kn->rmn", twist_im, sin_inner, precision=highest
    )
    spec_im = jnp.einsum("rmk,kn->rmn", twist_re, sin_inner, precision=highest) + jnp.einsum(
        "rmk,kn->rmn", twist_im, cos_inner, precision=highest
    )
    return (spec_re.reshape(cycles, length), spec_im.reshape(cycles, length))


def inverse_cycles(spec_re, spec_im):
    cycles, length = spec_re.shape
    outer_len = length // 128
    shaped_re = spec_re.reshape(cycles, outer_len, 128)
    shaped_im = spec_im.reshape(cycles, outer_len, 128)
    cos_inner, sin_inner = phase_pair(128, 128, 128, 1.0)
    inner_re = jnp.einsum("rmn,nk->rmk", shaped_re, cos_inner, precision=highest) - jnp.einsum(
        "rmn,nk->rmk", shaped_im, sin_inner, precision=highest
    )
    inner_im = jnp.einsum("rmn,nk->rmk", shaped_re, sin_inner, precision=highest) + jnp.einsum(
        "rmn,nk->rmk", shaped_im, cos_inner, precision=highest
    )
    cos_twist, sin_twist = phase_pair(outer_len, 128, length, 1.0)
    twist_re = inner_re * cos_twist - inner_im * sin_twist
    twist_im = inner_re * sin_twist + inner_im * cos_twist
    cos_outer, sin_outer = phase_pair(outer_len, outer_len, outer_len, 1.0)
    field = jnp.einsum("jm,rmk->rjk", cos_outer, twist_re, precision=highest) - jnp.einsum(
        "jm,rmk->rjk", sin_outer, twist_im, precision=highest
    )
    return field.reshape(cycles, length)


def forward_band(field, band):
    cycles, length = field.shape
    outer_len = length // 128
    band_cols = band // outer_len
    shaped = field.reshape(cycles, outer_len, 128)
    cos_outer, sin_outer = phase_pair(outer_len, outer_len, outer_len, -1.0)
    part = jnp.einsum(
        "mj,rjk->rmk", jnp.concatenate([cos_outer, sin_outer], axis=0), shaped, precision=highest
    )
    part_re, part_im = part[:, :outer_len], part[:, outer_len:]
    cos_twist, sin_twist = phase_pair(outer_len, 128, length, -1.0)
    twist = jnp.concatenate(
        [part_re * cos_twist - part_im * sin_twist, part_re * sin_twist + part_im * cos_twist],
        axis=2,
    )
    cos_inner, sin_inner = phase_pair(128, band_cols, 128, -1.0)
    inner = jnp.concatenate(
        [jnp.concatenate([cos_inner, sin_inner], axis=1),
         jnp.concatenate([-sin_inner, cos_inner], axis=1)],
        axis=0,
    )
    spec = jnp.einsum("rmk,kn->rmn", twist, inner, precision=highest)
    return spec[:, :, :band_cols], spec[:, :, band_cols:]


def inverse_band(spec_re, spec_im, length):
    cycles, outer_len, band_cols = spec_re.shape
    cos_inner, sin_inner = phase_pair(band_cols, 128, 128, 1.0)
    inner = jnp.concatenate(
        [jnp.concatenate([cos_inner, sin_inner], axis=1),
         jnp.concatenate([-sin_inner, cos_inner], axis=1)],
        axis=0,
    )
    inner_out = jnp.einsum(
        "rmn,nk->rmk", jnp.concatenate([spec_re, spec_im], axis=2), inner, precision=highest
    )
    inner_re, inner_im = inner_out[:, :, :128], inner_out[:, :, 128:]
    cos_twist, sin_twist = phase_pair(outer_len, 128, length, 1.0)
    twist = jnp.concatenate(
        [inner_re * cos_twist - inner_im * sin_twist, inner_re * sin_twist + inner_im * cos_twist],
        axis=1,
    )
    cos_outer, sin_outer = phase_pair(outer_len, outer_len, outer_len, 1.0)
    outer = jnp.concatenate([cos_outer, -sin_outer], axis=1)
    field = jnp.einsum("jm,rmk->rjk", outer, twist, precision=highest)
    return field.reshape(cycles, length)


def legendre_filter(owned, legendre, prior_gain, m_own):
    count_here, degrees, total_cycles = legendre.shape
    block_rows = min(512, degrees)

    def one_block(index, running):
        start = index * block_rows
        table = lax.dynamic_slice_in_dim(legendre, start, block_rows, 1)
        analysed = jnp.einsum("mlr,cmr->cml", table, owned, preferred_element_type=jnp.float32)
        degree = start + jnp.arange(block_rows, dtype=jnp.int32)
        keep_rows = degree[None, :] >= m_own[:, None]
        gain_block = lax.dynamic_slice_in_dim(prior_gain, start, block_rows)
        scaled = jnp.where(keep_rows[None], analysed * gain_block, 0.0).astype(jnp.bfloat16)
        return running + jnp.einsum(
            "mlr,cml->cmr", table, scaled, preferred_element_type=jnp.float32
        )

    first_block = 0
    initial = jnp.zeros(owned.shape, jnp.float32)
    summed = lax.fori_loop(first_block, degrees // block_rows, one_block, initial)
    return summed * math.sqrt(total_cycles / degrees)


ROWS = 16


def legendre_body(base_ref, m_ref, coef_ref, gain_ref, tab_ref, out_ref, *, scale):
    k = pl.program_id(0)
    tab = tab_ref[0]
    coef = coef_ref[0]
    analysed = lax.dot_general(
        coef, tab, (((1,), (1,)), ((), ())), preferred_element_type=jnp.float32
    )
    degree = lax.broadcasted_iota(jnp.int32, analysed.shape, 1)
    keep = degree >= m_ref[base_ref[0] + k]
    scaled = jnp.where(keep, analysed * gain_ref[...], 0.0).astype(jnp.bfloat16)
    synth = jnp.dot(scaled, tab, preferred_element_type=jnp.float32)
    out_ref[0] = synth * scale


def legendre_pallas(owned, legendre, prior_gain, m_values, first):
    count_here, degrees, total_cycles = legendre.shape
    coef = jnp.zeros((count_here, ROWS, total_cycles), jnp.bfloat16)
    coef = coef.at[:, :2, :].set(owned.transpose(1, 0, 2))
    gain = prior_gain.reshape(1, degrees)
    grid_spec = pltpu.PrefetchScalarGridSpec(
        num_scalar_prefetch=2,
        grid=(count_here,),
        in_specs=[
            pl.BlockSpec((1, ROWS, total_cycles), lambda k, b, m: (k, 0, 0)),
            pl.BlockSpec((1, degrees), lambda k, b, m: (0, 0)),
            pl.BlockSpec((1, degrees, total_cycles), lambda k, b, m: (k, 0, 0)),
        ],
        out_specs=pl.BlockSpec((1, ROWS, total_cycles), lambda k, b, m: (k, 0, 0)),
    )
    out = pl.pallas_call(
        functools.partial(legendre_body, scale=math.sqrt(total_cycles / degrees)),
        grid_spec=grid_spec,
        out_shape=jax.ShapeDtypeStruct((count_here, ROWS, total_cycles), jnp.float32),
    )(first, m_values, coef, gain, legendre)
    return out[:, :2, :].transpose(1, 0, 2)


def pointing_body(w_ref, p_ref, x_ref, s_ref, out_ref, *, tblk, nsamp):
    d = pl.program_id(0)
    point = p_ref[0].reshape(tblk * nsamp, p_ref.shape[3])
    picked = x_ref[0]
    every = lax.dot_general(
        picked, point, (((1,), (1,)), ((), ())), preferred_element_type=jnp.float32
    )
    row = lax.broadcasted_iota(jnp.int32, every.shape, 0)
    col = lax.broadcasted_iota(jnp.int32, every.shape, 1)
    mine = row == col // nsamp
    predicted = jnp.sum(jnp.where(mine, every, 0.0), axis=0, keepdims=True)
    resid = (w_ref[d] * (s_ref[0] - predicted)).astype(jnp.bfloat16)
    spread = jnp.where(mine, jnp.broadcast_to(resid, every.shape), jnp.zeros_like(resid))
    out_ref[0] = jnp.dot(spread, point, preferred_element_type=jnp.float32)


def pointing_pallas(pointing, picked, samples, det_weight):
    dets, times, nsamp, npix = pointing.shape
    tblk = times
    samples_row = samples.reshape(dets, 1, times * nsamp)
    grid_spec = pltpu.PrefetchScalarGridSpec(
        num_scalar_prefetch=1,
        grid=(dets, times // tblk),
        in_specs=[
            pl.BlockSpec((1, tblk, nsamp, npix), lambda d, t, w: (d, t, 0, 0)),
            pl.BlockSpec((1, tblk, npix), lambda d, t, w: (d, t, 0)),
            pl.BlockSpec((1, 1, tblk * nsamp), lambda d, t, w: (d, 0, t)),
        ],
        out_specs=pl.BlockSpec((1, tblk, npix), lambda d, t, w: (d, t, 0)),
    )
    return pl.pallas_call(
        functools.partial(pointing_body, tblk=tblk, nsamp=nsamp),
        grid_spec=grid_spec,
        out_shape=jax.ShapeDtypeStruct((dets, times, npix), jnp.float32),
    )(det_weight, pointing, picked, samples_row)


CAP = 8


STRIDE = 4


def order_pick(m_values):
    count = m_values.shape[0]
    offset = m_values - STRIDE * jnp.arange(count, dtype=jnp.int32)
    return offset[:, None] == jnp.arange(STRIDE, dtype=jnp.int32)[None, :]


def spectrum_out(field, m_values, cycle_offset):
    cycles_here, length = field.shape
    count = m_values.shape[0]
    band = count * STRIDE
    spec_re, spec_im = forward_band(field, band)
    spec_re = spec_re.transpose(0, 2, 1).reshape(cycles_here, count, STRIDE)
    spec_im = spec_im.transpose(0, 2, 1).reshape(cycles_here, count, STRIDE)
    pick = order_pick(m_values)[None]
    pick_re = jnp.sum(jnp.where(pick, spec_re, 0.0), axis=2)
    pick_im = jnp.sum(jnp.where(pick, spec_im, 0.0), axis=2)
    phases = (m_values[None, :] * cycle_offset[:, None] % length).astype(jnp.float32) * (
        2.0 * math.pi / length
    )
    cos_phase = jnp.cos(phases)
    sin_phase = jnp.sin(phases)
    norm_factor = 1.0 / math.sqrt(length)
    coef_re = (pick_re * cos_phase + pick_im * sin_phase) * norm_factor
    coef_im = (pick_im * cos_phase - pick_re * sin_phase) * norm_factor
    return coef_re, coef_im, cos_phase, sin_phase


def spectrum_back(back_re, back_im, cos_phase, sin_phase, m_values, length):
    cycles_here = back_re.shape[0]
    count = m_values.shape[0]
    outer_len = length // 128
    mode_weight = jnp.where(m_values == 0, 1.0, 2.0).astype(jnp.float32)[None, :]
    harm_re = mode_weight * (back_re * cos_phase - back_im * sin_phase)
    harm_im = mode_weight * (back_re * sin_phase + back_im * cos_phase)
    pick = order_pick(m_values)[None]
    band_cols = count * STRIDE // outer_len
    full_re = jnp.where(pick, harm_re[:, :, None], 0.0).reshape(cycles_here, band_cols, outer_len)
    full_im = jnp.where(pick, harm_im[:, :, None], 0.0).reshape(cycles_here, band_cols, outer_len)
    full_re = full_re.transpose(0, 2, 1)
    full_im = full_im.transpose(0, 2, 1)
    return inverse_band(full_re, full_im, length) / math.sqrt(2.0 * count)


def on_device(
    samples,
    pointing,
    pix_block,
    det_weight,
    start_map,
    legendre,
    prior_gain,
    m_values,
    cycle_offset,
):
    axes = ("det", "tm")
    cycles_here, length = start_map.shape
    per_cycle = length // 128
    owners = lax.axis_size(axes)
    total_cycles = cycles_here * owners
    blocks_here = cycles_here * per_cycle
    count_here = legendre.shape[0]
    owner_index = lax.axis_index(axes)
    first_order = jnp.full((1,), owner_index * count_here, jnp.int32)
    slots = owners * CAP

    flat_pix = pix_block.reshape(-1)
    nloc = flat_pix.shape[0]
    owner_of = flat_pix // blocks_here
    within = flat_pix % blocks_here
    order = jnp.arange(nloc, dtype=jnp.int32)
    same = (owner_of[:, None] == owner_of[None, :]) & (order[None, :] < order[:, None])
    rank = jnp.sum(same.astype(jnp.int32), axis=1)
    slot = owner_of * CAP + rank
    slot_hot = slot[:, None] == jnp.arange(slots, dtype=jnp.int32)[None, :]
    weight_of = jnp.broadcast_to(det_weight[:, None], pix_block.shape).reshape(-1)
    info = jnp.stack([within.astype(jnp.float32), weight_of], axis=1)
    info = jnp.zeros((slots, 2), jnp.float32).at[slot].set(info).reshape(owners, CAP * 2)
    coef_width = 2 * count_here * cycles_here

    def coef_out(field):
        coef_re, coef_im, cos_phase, sin_phase = spectrum_out(field, m_values, cycle_offset)
        outward = jnp.stack([coef_re.T, coef_im.T]).astype(jnp.bfloat16)
        outward = outward.reshape(2, owners, count_here, cycles_here).transpose(1, 0, 2, 3)
        return outward.reshape(owners, coef_width), cos_phase, sin_phase

    def coef_in(part):
        owned = part.reshape(owners, 2, count_here, cycles_here).astype(jnp.bfloat16)
        return owned.transpose(1, 2, 0, 3).reshape(2, count_here, total_cycles)

    first_out, cos_phase, sin_phase = coef_out(start_map)
    info = jnp.concatenate([info, first_out.astype(jnp.float32)], axis=1)
    info_recv = lax.all_to_all(info, axes, 0, 0, tiled=True)
    first_owned = coef_in(info_recv[:, CAP * 2 :])
    info_recv = info_recv[:, : CAP * 2].reshape(slots, 2)
    want = info_recv[:, 0].astype(jnp.int32)
    want_hot = (want[None, :] == jnp.arange(blocks_here, dtype=jnp.int32)[:, None]).astype(jnp.float32)
    hit_weight = jnp.sum(want_hot * info_recv[None, :, 1], axis=1).reshape(cycles_here, per_cycle)
    divisor = jnp.repeat(1.0 + 0.25 * hit_weight, 128, axis=1)
    want_pick = want_hot.T.astype(jnp.bfloat16)

    current = start_map
    for iteration in range(ITERS):
        map_half = current.astype(jnp.bfloat16).reshape(blocks_here, 128)
        rows_out = jnp.dot(want_pick, map_half, preferred_element_type=jnp.float32)
        rows_out = rows_out.astype(jnp.bfloat16).reshape(owners, CAP * 128)
        if iteration == 0:
            rows_in = lax.all_to_all(rows_out.reshape(owners, 1, -1), axes, 0, 0, tiled=True)
            rows_in = rows_in.reshape(slots, 128)
            owned = first_owned
        else:
            outward, cos_phase, sin_phase = coef_out(current)
            send_a = jnp.concatenate(
                [rows_out.reshape(owners, 1, -1), outward.reshape(owners, 1, -1)], axis=2
            )
            recv_a = lax.all_to_all(send_a, axes, 0, 0, tiled=True).reshape(owners, -1)
            rows_in = recv_a[:, : CAP * 128].reshape(slots, 128)
            owned = coef_in(recv_a[:, CAP * 128 :])

        picked = jnp.dot(slot_hot.astype(jnp.bfloat16), rows_in, preferred_element_type=jnp.float32)
        picked = picked.astype(jnp.bfloat16).reshape(pix_block.shape + (128,))
        binned_terms = pointing_pallas(pointing, picked, samples, det_weight)
        binned_send = jnp.dot(
            slot_hot.T.astype(jnp.float32), binned_terms.reshape(-1, 128), precision=highest
        )

        synth = legendre_pallas(owned, legendre, prior_gain, m_values, first_order)
        synth_send = synth.reshape(2, count_here, owners, cycles_here).transpose(2, 0, 1, 3)
        send_b = jnp.concatenate(
            [binned_send.reshape(owners, 1, CAP * 128), synth_send.reshape(owners, 1, -1)], axis=2
        )
        recv_b = lax.all_to_all(send_b, axes, 0, 0, tiled=True).reshape(owners, -1)
        binned_in = recv_b[:, : CAP * 128].reshape(slots, 128)
        binned = jnp.dot(want_hot, binned_in, precision=highest).reshape(cycles_here, length)
        returned = recv_b[:, CAP * 128 :].reshape(owners, 2, count_here, cycles_here)
        returned = returned.transpose(1, 0, 2, 3).reshape(2, owners * count_here, cycles_here)
        filtered = spectrum_back(
            returned[0].T, returned[1].T, cos_phase, sin_phase, m_values, length
        )
        current = current + (binned - filtered) / divisor
    return current


def solution(mesh):
    placed = (
        P("det", "tm", None),
        P("det", "tm", None, None),
        P("det", "tm"),
        P("det"),
        P(("det", "tm"), None),
        P(("det", "tm"), None, None),
        P(),
        P(),
        P(("det", "tm")),
    )
    return jax.shard_map(
        on_device, mesh=mesh, in_specs=placed, out_specs=P(("det", "tm"), None), check_vma=False
    )
```

```python
import math

import functools

import jax
import jax.numpy as jnp
from jax import lax
from jax.experimental import pallas as pl
from jax.experimental.pallas import tpu as pltpu
from jax.sharding import PartitionSpec as P

ITERS = 2


highest = lax.Precision.HIGHEST


def phase_pair(first_len, second_len, length, sign):
    first = jnp.arange(first_len, dtype=jnp.int32)[:, None]
    second = jnp.arange(second_len, dtype=jnp.int32)[None, :]
    phases = (first * second % length).astype(jnp.float32) * (sign * 2.0 * math.pi / length)
    return (jnp.cos(phases), jnp.sin(phases))


def forward_cycles(field):
    cycles, length = field.shape
    outer_len = length // 128
    shaped = field.reshape(cycles, outer_len, 128)
    cos_outer, sin_outer = phase_pair(outer_len, outer_len, outer_len, -1.0)
    part_re = jnp.einsum("mj,rjk->rmk", cos_outer, shaped, precision=highest)
    part_im = jnp.einsum("mj,rjk->rmk", sin_outer, shaped, precision=highest)
    cos_twist, sin_twist = phase_pair(outer_len, 128, length, -1.0)
    twist_re = part_re * cos_twist - part_im * sin_twist
    twist_im = part_re * sin_twist + part_im * cos_twist
    cos_inner, sin_inner = phase_pair(128, 128, 128, -1.0)
    spec_re = jnp.einsum("rmk,kn->rmn", twist_re, cos_inner, precision=highest) - jnp.einsum(
        "rmk,kn->rmn", twist_im, sin_inner, precision=highest
    )
    spec_im = jnp.einsum("rmk,kn->rmn", twist_re, sin_inner, precision=highest) + jnp.einsum(
        "rmk,kn->rmn", twist_im, cos_inner, precision=highest
    )
    return (spec_re.reshape(cycles, length), spec_im.reshape(cycles, length))


def inverse_cycles(spec_re, spec_im):
    cycles, length = spec_re.shape
    outer_len = length // 128
    shaped_re = spec_re.reshape(cycles, outer_len, 128)
    shaped_im = spec_im.reshape(cycles, outer_len, 128)
    cos_inner, sin_inner = phase_pair(128, 128, 128, 1.0)
    inner_re = jnp.einsum("rmn,nk->rmk", shaped_re, cos_inner, precision=highest) - jnp.einsum(
        "rmn,nk->rmk", shaped_im, sin_inner, precision=highest
    )
    inner_im = jnp.einsum("rmn,nk->rmk", shaped_re, sin_inner, precision=highest) + jnp.einsum(
        "rmn,nk->rmk", shaped_im, cos_inner, precision=highest
    )
    cos_twist, sin_twist = phase_pair(outer_len, 128, length, 1.0)
    twist_re = inner_re * cos_twist - inner_im * sin_twist
    twist_im = inner_re * sin_twist + inner_im * cos_twist
    cos_outer, sin_outer = phase_pair(outer_len, outer_len, outer_len, 1.0)
    field = jnp.einsum("jm,rmk->rjk", cos_outer, twist_re, precision=highest) - jnp.einsum(
        "jm,rmk->rjk", sin_outer, twist_im, precision=highest
    )
    return field.reshape(cycles, length)


def forward_band(field, band):
    cycles, length = field.shape
    outer_len = length // 128
    band_cols = band // outer_len
    shaped = field.reshape(cycles, outer_len, 128)
    cos_outer, sin_outer = phase_pair(outer_len, outer_len, outer_len, -1.0)
    part = jnp.einsum(
        "mj,rjk->rmk", jnp.concatenate([cos_outer, sin_outer], axis=0), shaped, precision=highest
    )
    part_re, part_im = part[:, :outer_len], part[:, outer_len:]
    cos_twist, sin_twist = phase_pair(outer_len, 128, length, -1.0)
    twist = jnp.concatenate(
        [part_re * cos_twist - part_im * sin_twist, part_re * sin_twist + part_im * cos_twist],
        axis=2,
    )
    cos_inner, sin_inner = phase_pair(128, band_cols, 128, -1.0)
    inner = jnp.concatenate(
        [jnp.concatenate([cos_inner, sin_inner], axis=1),
         jnp.concatenate([-sin_inner, cos_inner], axis=1)],
        axis=0,
    )
    spec = jnp.einsum("rmk,kn->rmn", twist, inner, precision=highest)
    return spec[:, :, :band_cols], spec[:, :, band_cols:]


def inverse_band(spec_re, spec_im, length):
    cycles, outer_len, band_cols = spec_re.shape
    cos_inner, sin_inner = phase_pair(band_cols, 128, 128, 1.0)
    inner = jnp.concatenate(
        [jnp.concatenate([cos_inner, sin_inner], axis=1),
         jnp.concatenate([-sin_inner, cos_inner], axis=1)],
        axis=0,
    )
    inner_out = jnp.einsum(
        "rmn,nk->rmk", jnp.concatenate([spec_re, spec_im], axis=2), inner, precision=highest
    )
    inner_re, inner_im = inner_out[:, :, :128], inner_out[:, :, 128:]
    cos_twist, sin_twist = phase_pair(outer_len, 128, length, 1.0)
    twist = jnp.concatenate(
        [inner_re * cos_twist - inner_im * sin_twist, inner_re * sin_twist + inner_im * cos_twist],
        axis=1,
    )
    cos_outer, sin_outer = phase_pair(outer_len, outer_len, outer_len, 1.0)
    outer = jnp.concatenate([cos_outer, -sin_outer], axis=1)
    field = jnp.einsum("jm,rmk->rjk", outer, twist, precision=highest)
    return field.reshape(cycles, length)


def legendre_filter(owned, legendre, prior_gain, m_own):
    count_here, degrees, total_cycles = legendre.shape
    block_rows = min(512, degrees)

    def one_block(index, running):
        start = index * block_rows
        table = lax.dynamic_slice_in_dim(legendre, start, block_rows, 1)
        analysed = jnp.einsum("mlr,cmr->cml", table, owned, preferred_element_type=jnp.float32)
        degree = start + jnp.arange(block_rows, dtype=jnp.int32)
        keep_rows = degree[None, :] >= m_own[:, None]
        gain_block = lax.dynamic_slice_in_dim(prior_gain, start, block_rows)
        scaled = jnp.where(keep_rows[None], analysed * gain_block, 0.0).astype(jnp.bfloat16)
        return running + jnp.einsum(
            "mlr,cml->cmr", table, scaled, preferred_element_type=jnp.float32
        )

    first_block = 0
    initial = jnp.zeros(owned.shape, jnp.float32)
    summed = lax.fori_loop(first_block, degrees // block_rows, one_block, initial)
    return summed * math.sqrt(total_cycles / degrees)


ROWS = 16


def legendre_body(base_ref, m_ref, coef_ref, gain_ref, tab_ref, out_ref, *, scale):
    k = pl.program_id(0)
    tab = tab_ref[0]
    coef = coef_ref[0]
    analysed = lax.dot_general(
        coef, tab, (((1,), (1,)), ((), ())), preferred_element_type=jnp.float32
    )
    degree = lax.broadcasted_iota(jnp.int32, analysed.shape, 1)
    keep = degree >= m_ref[base_ref[0] + k]
    scaled = jnp.where(keep, analysed * gain_ref[...], 0.0).astype(jnp.bfloat16)
    synth = jnp.dot(scaled, tab, preferred_element_type=jnp.float32)
    out_ref[0] = synth * scale


def legendre_pallas(owned, legendre, prior_gain, m_values, first):
    count_here, degrees, total_cycles = legendre.shape
    coef = jnp.zeros((count_here, ROWS, total_cycles), jnp.bfloat16)
    coef = coef.at[:, :2, :].set(owned.transpose(1, 0, 2))
    gain = prior_gain.reshape(1, degrees)
    grid_spec = pltpu.PrefetchScalarGridSpec(
        num_scalar_prefetch=2,
        grid=(count_here,),
        in_specs=[
            pl.BlockSpec((1, ROWS, total_cycles), lambda k, b, m: (k, 0, 0)),
            pl.BlockSpec((1, degrees), lambda k, b, m: (0, 0)),
            pl.BlockSpec((1, degrees, total_cycles), lambda k, b, m: (k, 0, 0)),
        ],
        out_specs=pl.BlockSpec((1, ROWS, total_cycles), lambda k, b, m: (k, 0, 0)),
    )
    out = pl.pallas_call(
        functools.partial(legendre_body, scale=math.sqrt(total_cycles / degrees)),
        grid_spec=grid_spec,
        out_shape=jax.ShapeDtypeStruct((count_here, ROWS, total_cycles), jnp.float32),
    )(first, m_values, coef, gain, legendre)
    return out[:, :2, :].transpose(1, 0, 2)


def pointing_body(w_ref, p_ref, x_ref, s_ref, out_ref, *, tblk, nsamp):
    d = pl.program_id(0)
    point = p_ref[0].reshape(tblk * nsamp, p_ref.shape[3])
    picked = x_ref[0]
    every = lax.dot_general(
        picked, point, (((1,), (1,)), ((), ())), preferred_element_type=jnp.float32
    )
    row = lax.broadcasted_iota(jnp.int32, every.shape, 0)
    col = lax.broadcasted_iota(jnp.int32, every.shape, 1)
    mine = row == col // nsamp
    predicted = jnp.sum(jnp.where(mine, every, 0.0), axis=0, keepdims=True)
    resid = (w_ref[d] * (s_ref[0] - predicted)).astype(jnp.bfloat16)
    spread = jnp.where(mine, jnp.broadcast_to(resid, every.shape), jnp.zeros_like(resid))
    out_ref[0] = jnp.dot(spread, point, preferred_element_type=jnp.float32)


def pointing_pallas(pointing, picked, samples, det_weight):
    dets, times, nsamp, npix = pointing.shape
    tblk = times
    samples_row = samples.reshape(dets, 1, times * nsamp)
    grid_spec = pltpu.PrefetchScalarGridSpec(
        num_scalar_prefetch=1,
        grid=(dets, times // tblk),
        in_specs=[
            pl.BlockSpec((1, tblk, nsamp, npix), lambda d, t, w: (d, t, 0, 0)),
            pl.BlockSpec((1, tblk, npix), lambda d, t, w: (d, t, 0)),
            pl.BlockSpec((1, 1, tblk * nsamp), lambda d, t, w: (d, 0, t)),
        ],
        out_specs=pl.BlockSpec((1, tblk, npix), lambda d, t, w: (d, t, 0)),
    )
    return pl.pallas_call(
        functools.partial(pointing_body, tblk=tblk, nsamp=nsamp),
        grid_spec=grid_spec,
        out_shape=jax.ShapeDtypeStruct((dets, times, npix), jnp.float32),
    )(det_weight, pointing, picked, samples_row)


CAP = 8


STRIDE = 4


def order_pick(m_values):
    count = m_values.shape[0]
    offset = m_values - STRIDE * jnp.arange(count, dtype=jnp.int32)
    return offset[:, None] == jnp.arange(STRIDE, dtype=jnp.int32)[None, :]


def spectrum_out(field, m_values, cycle_offset):
    cycles_here, length = field.shape
    count = m_values.shape[0]
    band = count * STRIDE
    spec_re, spec_im = forward_band(field, band)
    spec_re = spec_re.transpose(0, 2, 1).reshape(cycles_here, count, STRIDE)
    spec_im = spec_im.transpose(0, 2, 1).reshape(cycles_here, count, STRIDE)
    pick = order_pick(m_values)[None]
    pick_re = jnp.sum(jnp.where(pick, spec_re, 0.0), axis=2)
    pick_im = jnp.sum(jnp.where(pick, spec_im, 0.0), axis=2)
    phases = (m_values[None, :] * cycle_offset[:, None] % length).astype(jnp.float32) * (
        2.0 * math.pi / length
    )
    cos_phase = jnp.cos(phases)
    sin_phase = jnp.sin(phases)
    norm_factor = 1.0 / math.sqrt(length)
    coef_re = (pick_re * cos_phase + pick_im * sin_phase) * norm_factor
    coef_im = (pick_im * cos_phase - pick_re * sin_phase) * norm_factor
    return coef_re, coef_im, cos_phase, sin_phase


def spectrum_back(back_re, back_im, cos_phase, sin_phase, m_values, length):
    cycles_here = back_re.shape[0]
    count = m_values.shape[0]
    outer_len = length // 128
    mode_weight = jnp.where(m_values == 0, 1.0, 2.0).astype(jnp.float32)[None, :]
    harm_re = mode_weight * (back_re * cos_phase - back_im * sin_phase)
    harm_im = mode_weight * (back_re * sin_phase + back_im * cos_phase)
    pick = order_pick(m_values)[None]
    band_cols = count * STRIDE // outer_len
    full_re = jnp.where(pick, harm_re[:, :, None], 0.0).reshape(cycles_here, band_cols, outer_len)
    full_im = jnp.where(pick, harm_im[:, :, None], 0.0).reshape(cycles_here, band_cols, outer_len)
    full_re = full_re.transpose(0, 2, 1)
    full_im = full_im.transpose(0, 2, 1)
    return inverse_band(full_re, full_im, length) / math.sqrt(2.0 * count)


def on_device(
    samples,
    pointing,
    pix_block,
    det_weight,
    start_map,
    legendre,
    prior_gain,
    m_values,
    cycle_offset,
):
    axes = ("det", "tm")
    cycles_here, length = start_map.shape
    per_cycle = length // 128
    owners = lax.axis_size(axes)
    total_cycles = cycles_here * owners
    blocks_here = cycles_here * per_cycle
    count_here = legendre.shape[0]
    owner_index = lax.axis_index(axes)
    first_order = jnp.full((1,), owner_index * count_here, jnp.int32)
    slots = owners * CAP

    flat_pix = pix_block.reshape(-1)
    nloc = flat_pix.shape[0]
    owner_of = flat_pix // blocks_here
    within = flat_pix % blocks_here
    order = jnp.arange(nloc, dtype=jnp.int32)
    same = (owner_of[:, None] == owner_of[None, :]) & (order[None, :] < order[:, None])
    rank = jnp.sum(same.astype(jnp.int32), axis=1)
    slot = owner_of * CAP + rank
    slot_hot = slot[:, None] == jnp.arange(slots, dtype=jnp.int32)[None, :]
    weight_of = jnp.broadcast_to(det_weight[:, None], pix_block.shape).reshape(-1)
    info = jnp.stack([within.astype(jnp.float32), weight_of], axis=1)
    info = jnp.zeros((slots, 2), jnp.float32).at[slot].set(info).reshape(owners, CAP * 2)
    coef_width = 2 * count_here * cycles_here

    def coef_out(field):
        coef_re, coef_im, cos_phase, sin_phase = spectrum_out(field, m_values, cycle_offset)
        outward = jnp.stack([coef_re.T, coef_im.T]).astype(jnp.bfloat16)
        outward = outward.reshape(2, owners, count_here, cycles_here).transpose(1, 0, 2, 3)
        return outward.reshape(owners, coef_width), cos_phase, sin_phase

    def coef_in(part):
        owned = part.reshape(owners, 2, count_here, cycles_here).astype(jnp.bfloat16)
        return owned.transpose(1, 2, 0, 3).reshape(2, count_here, total_cycles)

    first_out, cos_phase, sin_phase = coef_out(start_map)
    info = jnp.concatenate([info, first_out.astype(jnp.float32)], axis=1)
    info_recv = lax.all_to_all(info, axes, 0, 0, tiled=True)
    first_owned = coef_in(info_recv[:, CAP * 2 :])
    info_recv = info_recv[:, : CAP * 2].reshape(slots, 2)
    want = info_recv[:, 0].astype(jnp.int32)
    want_hot = (want[None, :] == jnp.arange(blocks_here, dtype=jnp.int32)[:, None]).astype(jnp.float32)
    hit_weight = jnp.sum(want_hot * info_recv[None, :, 1], axis=1).reshape(cycles_here, per_cycle)
    divisor = jnp.repeat(1.0 + 0.25 * hit_weight, 128, axis=1)
    want_pick = want_hot.T.astype(jnp.bfloat16)

    current = start_map
    for iteration in range(ITERS):
        map_half = current.astype(jnp.bfloat16).reshape(blocks_here, 128)
        rows_out = jnp.dot(want_pick, map_half, preferred_element_type=jnp.float32)
        rows_out = rows_out.astype(jnp.bfloat16).reshape(owners, CAP * 128)
        if iteration == 0:
            rows_in = lax.all_to_all(rows_out.reshape(owners, 1, -1), axes, 0, 0, tiled=True)
            rows_in = rows_in.reshape(slots, 128)
            owned = first_owned
        else:
            outward, cos_phase, sin_phase = coef_out(current)
            send_a = jnp.concatenate(
                [rows_out.reshape(owners, 1, -1), outward.reshape(owners, 1, -1)], axis=2
            )
            recv_a = lax.all_to_all(send_a, axes, 0, 0, tiled=True).reshape(owners, -1)
            rows_in = recv_a[:, : CAP * 128].reshape(slots, 128)
            owned = coef_in(recv_a[:, CAP * 128 :])

        picked = jnp.dot(slot_hot.astype(jnp.bfloat16), rows_in, preferred_element_type=jnp.float32)
        picked = picked.astype(jnp.bfloat16).reshape(pix_block.shape + (128,))
        binned_terms = pointing_pallas(pointing, picked, samples, det_weight)
        binned_send = jnp.dot(
            slot_hot.T.astype(jnp.float32), binned_terms.reshape(-1, 128), precision=highest
        )

        if iteration == ITERS - 1:
            binned_in = lax.all_to_all(
                binned_send.reshape(owners, 1, CAP * 128), axes, 0, 0, tiled=True
            ).reshape(slots, 128)
            synth = legendre_pallas(owned, legendre, prior_gain, m_values, first_order)
            synth_send = synth.reshape(2, count_here, owners, cycles_here).transpose(2, 0, 1, 3)
            recv_b = lax.all_to_all(synth_send.reshape(owners, 1, -1), axes, 0, 0, tiled=True)
            recv_b = jnp.concatenate(
                [jnp.zeros((owners, CAP * 128), jnp.float32), recv_b.reshape(owners, -1)], axis=1
            )
        else:
            synth = legendre_pallas(owned, legendre, prior_gain, m_values, first_order)
            synth_send = synth.reshape(2, count_here, owners, cycles_here).transpose(2, 0, 1, 3)
            send_b = jnp.concatenate(
                [binned_send.reshape(owners, 1, CAP * 128), synth_send.reshape(owners, 1, -1)],
                axis=2,
            )
            recv_b = lax.all_to_all(send_b, axes, 0, 0, tiled=True).reshape(owners, -1)
            binned_in = recv_b[:, : CAP * 128].reshape(slots, 128)
        binned = jnp.dot(want_hot, binned_in, precision=highest).reshape(cycles_here, length)
        returned = recv_b[:, CAP * 128 :].reshape(owners, 2, count_here, cycles_here)
        returned = returned.transpose(1, 0, 2, 3).reshape(2, owners * count_here, cycles_here)
        filtered = spectrum_back(
            returned[0].T, returned[1].T, cos_phase, sin_phase, m_values, length
        )
        current = current + (binned - filtered) / divisor
    return current


def solution(mesh):
    placed = (
        P("det", "tm", None),
        P("det", "tm", None, None),
        P("det", "tm"),
        P("det"),
        P(("det", "tm"), None),
        P(("det", "tm"), None, None),
        P(),
        P(),
        P(("det", "tm")),
    )
    return jax.shard_map(
        on_device, mesh=mesh, in_specs=placed, out_specs=P(("det", "tm"), None), check_vma=False
    )
```

```python
import math

import functools

import jax
import jax.numpy as jnp
from jax import lax
from jax.experimental import pallas as pl
from jax.experimental.pallas import tpu as pltpu
from jax.sharding import PartitionSpec as P

ITERS = 2


highest = lax.Precision.HIGHEST


def phase_pair(first_len, second_len, length, sign):
    first = jnp.arange(first_len, dtype=jnp.int32)[:, None]
    second = jnp.arange(second_len, dtype=jnp.int32)[None, :]
    phases = (first * second % length).astype(jnp.float32) * (sign * 2.0 * math.pi / length)
    return (jnp.cos(phases), jnp.sin(phases))


def forward_cycles(field):
    cycles, length = field.shape
    outer_len = length // 128
    shaped = field.reshape(cycles, outer_len, 128)
    cos_outer, sin_outer = phase_pair(outer_len, outer_len, outer_len, -1.0)
    part_re = jnp.einsum("mj,rjk->rmk", cos_outer, shaped, precision=highest)
    part_im = jnp.einsum("mj,rjk->rmk", sin_outer, shaped, precision=highest)
    cos_twist, sin_twist = phase_pair(outer_len, 128, length, -1.0)
    twist_re = part_re * cos_twist - part_im * sin_twist
    twist_im = part_re * sin_twist + part_im * cos_twist
    cos_inner, sin_inner = phase_pair(128, 128, 128, -1.0)
    spec_re = jnp.einsum("rmk,kn->rmn", twist_re, cos_inner, precision=highest) - jnp.einsum(
        "rmk,kn->rmn", twist_im, sin_inner, precision=highest
    )
    spec_im = jnp.einsum("rmk,kn->rmn", twist_re, sin_inner, precision=highest) + jnp.einsum(
        "rmk,kn->rmn", twist_im, cos_inner, precision=highest
    )
    return (spec_re.reshape(cycles, length), spec_im.reshape(cycles, length))


def inverse_cycles(spec_re, spec_im):
    cycles, length = spec_re.shape
    outer_len = length // 128
    shaped_re = spec_re.reshape(cycles, outer_len, 128)
    shaped_im = spec_im.reshape(cycles, outer_len, 128)
    cos_inner, sin_inner = phase_pair(128, 128, 128, 1.0)
    inner_re = jnp.einsum("rmn,nk->rmk", shaped_re, cos_inner, precision=highest) - jnp.einsum(
        "rmn,nk->rmk", shaped_im, sin_inner, precision=highest
    )
    inner_im = jnp.einsum("rmn,nk->rmk", shaped_re, sin_inner, precision=highest) + jnp.einsum(
        "rmn,nk->rmk", shaped_im, cos_inner, precision=highest
    )
    cos_twist, sin_twist = phase_pair(outer_len, 128, length, 1.0)
    twist_re = inner_re * cos_twist - inner_im * sin_twist
    twist_im = inner_re * sin_twist + inner_im * cos_twist
    cos_outer, sin_outer = phase_pair(outer_len, outer_len, outer_len, 1.0)
    field = jnp.einsum("jm,rmk->rjk", cos_outer, twist_re, precision=highest) - jnp.einsum(
        "jm,rmk->rjk", sin_outer, twist_im, precision=highest
    )
    return field.reshape(cycles, length)


def forward_band(field, band):
    cycles, length = field.shape
    outer_len = length // 128
    band_cols = band // outer_len
    shaped = field.reshape(cycles, outer_len, 128)
    cos_outer, sin_outer = phase_pair(outer_len, outer_len, outer_len, -1.0)
    part = jnp.einsum(
        "mj,rjk->rmk", jnp.concatenate([cos_outer, sin_outer], axis=0), shaped, precision=highest
    )
    part_re, part_im = part[:, :outer_len], part[:, outer_len:]
    cos_twist, sin_twist = phase_pair(outer_len, 128, length, -1.0)
    twist = jnp.concatenate(
        [part_re * cos_twist - part_im * sin_twist, part_re * sin_twist + part_im * cos_twist],
        axis=2,
    )
    cos_inner, sin_inner = phase_pair(128, band_cols, 128, -1.0)
    inner = jnp.concatenate(
        [jnp.concatenate([cos_inner, sin_inner], axis=1),
         jnp.concatenate([-sin_inner, cos_inner], axis=1)],
        axis=0,
    )
    spec = jnp.einsum("rmk,kn->rmn", twist, inner, precision=highest)
    return spec[:, :, :band_cols], spec[:, :, band_cols:]


def inverse_band(spec_re, spec_im, length):
    cycles, outer_len, band_cols = spec_re.shape
    cos_inner, sin_inner = phase_pair(band_cols, 128, 128, 1.0)
    inner = jnp.concatenate(
        [jnp.concatenate([cos_inner, sin_inner], axis=1),
         jnp.concatenate([-sin_inner, cos_inner], axis=1)],
        axis=0,
    )
    inner_out = jnp.einsum(
        "rmn,nk->rmk", jnp.concatenate([spec_re, spec_im], axis=2), inner, precision=highest
    )
    inner_re, inner_im = inner_out[:, :, :128], inner_out[:, :, 128:]
    cos_twist, sin_twist = phase_pair(outer_len, 128, length, 1.0)
    twist = jnp.concatenate(
        [inner_re * cos_twist - inner_im * sin_twist, inner_re * sin_twist + inner_im * cos_twist],
        axis=1,
    )
    cos_outer, sin_outer = phase_pair(outer_len, outer_len, outer_len, 1.0)
    outer = jnp.concatenate([cos_outer, -sin_outer], axis=1)
    field = jnp.einsum("jm,rmk->rjk", outer, twist, precision=highest)
    return field.reshape(cycles, length)


def legendre_filter(owned, legendre, prior_gain, m_own):
    count_here, degrees, total_cycles = legendre.shape
    block_rows = min(512, degrees)

    def one_block(index, running):
        start = index * block_rows
        table = lax.dynamic_slice_in_dim(legendre, start, block_rows, 1)
        analysed = jnp.einsum("mlr,cmr->cml", table, owned, preferred_element_type=jnp.float32)
        degree = start + jnp.arange(block_rows, dtype=jnp.int32)
        keep_rows = degree[None, :] >= m_own[:, None]
        gain_block = lax.dynamic_slice_in_dim(prior_gain, start, block_rows)
        scaled = jnp.where(keep_rows[None], analysed * gain_block, 0.0).astype(jnp.bfloat16)
        return running + jnp.einsum(
            "mlr,cml->cmr", table, scaled, preferred_element_type=jnp.float32
        )

    first_block = 0
    initial = jnp.zeros(owned.shape, jnp.float32)
    summed = lax.fori_loop(first_block, degrees // block_rows, one_block, initial)
    return summed * math.sqrt(total_cycles / degrees)


ROWS = 16


def legendre_body(m_ref, coef_ref, gain_ref, tab_ref, out_ref, *, scale, per):
    k = pl.program_id(0)
    for j in range(per):
        tab = tab_ref[j]
        coef = coef_ref[j]
        analysed = lax.dot_general(
            coef, tab, (((1,), (1,)), ((), ())), preferred_element_type=jnp.float32
        )
        degree = lax.broadcasted_iota(jnp.int32, analysed.shape, 1)
        keep = degree >= m_ref[k * per + j]
        scaled = jnp.where(keep, analysed * gain_ref[...], 0.0).astype(jnp.bfloat16)
        synth = jnp.dot(scaled, tab, preferred_element_type=jnp.float32)
        out_ref[j] = synth * scale


def legendre_pallas(owned, legendre, prior_gain, m_own):
    count_here, degrees, total_cycles = legendre.shape
    per = 2 if count_here % 2 == 0 else 1
    coef = jnp.zeros((count_here, ROWS, total_cycles), jnp.bfloat16)
    coef = coef.at[:, :2, :].set(owned.transpose(1, 0, 2))
    gain = prior_gain.reshape(1, degrees)
    grid_spec = pltpu.PrefetchScalarGridSpec(
        num_scalar_prefetch=1,
        grid=(count_here // per,),
        in_specs=[
            pl.BlockSpec((per, ROWS, total_cycles), lambda k, m: (k, 0, 0)),
            pl.BlockSpec((1, degrees), lambda k, m: (0, 0)),
            pl.BlockSpec((per, degrees, total_cycles), lambda k, m: (k, 0, 0)),
        ],
        out_specs=pl.BlockSpec((per, ROWS, total_cycles), lambda k, m: (k, 0, 0)),
    )
    out = pl.pallas_call(
        functools.partial(legendre_body, scale=math.sqrt(total_cycles / degrees), per=per),
        grid_spec=grid_spec,
        out_shape=jax.ShapeDtypeStruct((count_here, ROWS, total_cycles), jnp.float32),
    )(m_own, coef, gain, legendre)
    return out[:, :2, :].transpose(1, 0, 2)


def pointing_body(w_ref, p_ref, x_ref, s_ref, out_ref, *, tblk, nsamp):
    d = pl.program_id(0)
    point = p_ref[0].reshape(tblk * nsamp, p_ref.shape[3])
    picked = x_ref[0]
    every = lax.dot_general(
        picked, point, (((1,), (1,)), ((), ())), preferred_element_type=jnp.float32
    )
    row = lax.broadcasted_iota(jnp.int32, every.shape, 0)
    col = lax.broadcasted_iota(jnp.int32, every.shape, 1)
    mine = row == col // nsamp
    predicted = jnp.sum(jnp.where(mine, every, 0.0), axis=0, keepdims=True)
    resid = (w_ref[d] * (s_ref[0] - predicted)).astype(jnp.bfloat16)
    spread = jnp.where(mine, jnp.broadcast_to(resid, every.shape), jnp.zeros_like(resid))
    out_ref[0] = jnp.dot(spread, point, preferred_element_type=jnp.float32)


def pointing_pallas(pointing, picked, samples, det_weight):
    dets, times, nsamp, npix = pointing.shape
    tblk = times
    samples_row = samples.reshape(dets, 1, times * nsamp)
    grid_spec = pltpu.PrefetchScalarGridSpec(
        num_scalar_prefetch=1,
        grid=(dets, times // tblk),
        in_specs=[
            pl.BlockSpec((1, tblk, nsamp, npix), lambda d, t, w: (d, t, 0, 0)),
            pl.BlockSpec((1, tblk, npix), lambda d, t, w: (d, t, 0)),
            pl.BlockSpec((1, 1, tblk * nsamp), lambda d, t, w: (d, 0, t)),
        ],
        out_specs=pl.BlockSpec((1, tblk, npix), lambda d, t, w: (d, t, 0)),
    )
    return pl.pallas_call(
        functools.partial(pointing_body, tblk=tblk, nsamp=nsamp),
        grid_spec=grid_spec,
        out_shape=jax.ShapeDtypeStruct((dets, times, npix), jnp.float32),
    )(det_weight, pointing, picked, samples_row)


CAP = 8


STRIDE = 4


def order_pick(m_values):
    count = m_values.shape[0]
    offset = m_values - STRIDE * jnp.arange(count, dtype=jnp.int32)
    return offset[:, None] == jnp.arange(STRIDE, dtype=jnp.int32)[None, :]


def spectrum_out(field, m_values, cycle_offset):
    cycles_here, length = field.shape
    count = m_values.shape[0]
    band = count * STRIDE
    spec_re, spec_im = forward_band(field, band)
    spec_re = spec_re.transpose(0, 2, 1).reshape(cycles_here, count, STRIDE)
    spec_im = spec_im.transpose(0, 2, 1).reshape(cycles_here, count, STRIDE)
    pick = order_pick(m_values)[None]
    pick_re = jnp.sum(jnp.where(pick, spec_re, 0.0), axis=2)
    pick_im = jnp.sum(jnp.where(pick, spec_im, 0.0), axis=2)
    phases = (m_values[None, :] * cycle_offset[:, None] % length).astype(jnp.float32) * (
        2.0 * math.pi / length
    )
    cos_phase = jnp.cos(phases)
    sin_phase = jnp.sin(phases)
    norm_factor = 1.0 / math.sqrt(length)
    coef_re = (pick_re * cos_phase + pick_im * sin_phase) * norm_factor
    coef_im = (pick_im * cos_phase - pick_re * sin_phase) * norm_factor
    return coef_re, coef_im, cos_phase, sin_phase


def spectrum_back(back_re, back_im, cos_phase, sin_phase, m_values, length):
    cycles_here = back_re.shape[0]
    count = m_values.shape[0]
    outer_len = length // 128
    mode_weight = jnp.where(m_values == 0, 1.0, 2.0).astype(jnp.float32)[None, :]
    harm_re = mode_weight * (back_re * cos_phase - back_im * sin_phase)
    harm_im = mode_weight * (back_re * sin_phase + back_im * cos_phase)
    pick = order_pick(m_values)[None]
    band_cols = count * STRIDE // outer_len
    full_re = jnp.where(pick, harm_re[:, :, None], 0.0).reshape(cycles_here, band_cols, outer_len)
    full_im = jnp.where(pick, harm_im[:, :, None], 0.0).reshape(cycles_here, band_cols, outer_len)
    full_re = full_re.transpose(0, 2, 1)
    full_im = full_im.transpose(0, 2, 1)
    return inverse_band(full_re, full_im, length) / math.sqrt(2.0 * count)


def on_device(
    samples,
    pointing,
    pix_block,
    det_weight,
    start_map,
    legendre,
    prior_gain,
    m_values,
    cycle_offset,
):
    axes = ("det", "tm")
    cycles_here, length = start_map.shape
    per_cycle = length // 128
    owners = lax.axis_size(axes)
    total_cycles = cycles_here * owners
    blocks_here = cycles_here * per_cycle
    count_here = legendre.shape[0]
    owner_index = lax.axis_index(axes)
    m_own = lax.dynamic_slice_in_dim(m_values, owner_index * count_here, count_here)
    slots = owners * CAP

    flat_pix = pix_block.reshape(-1)
    nloc = flat_pix.shape[0]
    owner_of = flat_pix // blocks_here
    within = flat_pix % blocks_here
    order = jnp.arange(nloc, dtype=jnp.int32)
    same = (owner_of[:, None] == owner_of[None, :]) & (order[None, :] < order[:, None])
    rank = jnp.sum(same.astype(jnp.int32), axis=1)
    slot = owner_of * CAP + rank
    weight_of = jnp.broadcast_to(det_weight[:, None], pix_block.shape).reshape(-1)
    info = jnp.stack([within.astype(jnp.float32), weight_of], axis=1)
    info = jnp.zeros((slots, 2), jnp.float32).at[slot].set(info).reshape(owners, CAP * 2)
    coef_width = 2 * count_here * cycles_here

    def coef_out(field):
        coef_re, coef_im, cos_phase, sin_phase = spectrum_out(field, m_values, cycle_offset)
        outward = jnp.stack([coef_re.T, coef_im.T]).astype(jnp.bfloat16)
        outward = outward.reshape(2, owners, count_here, cycles_here).transpose(1, 0, 2, 3)
        return outward.reshape(owners, coef_width), cos_phase, sin_phase

    def coef_in(part):
        owned = part.reshape(owners, 2, count_here, cycles_here).astype(jnp.bfloat16)
        return owned.transpose(1, 2, 0, 3).reshape(2, count_here, total_cycles)

    first_out, cos_phase, sin_phase = coef_out(start_map)
    info = jnp.concatenate([info, first_out.astype(jnp.float32)], axis=1)
    info_recv = lax.all_to_all(info, axes, 0, 0, tiled=True)
    first_owned = coef_in(info_recv[:, CAP * 2 :])
    info_recv = info_recv[:, : CAP * 2].reshape(slots, 2)
    want = info_recv[:, 0].astype(jnp.int32)
    want_hot = (want[None, :] == jnp.arange(blocks_here, dtype=jnp.int32)[:, None]).astype(jnp.float32)
    hit_weight = jnp.sum(want_hot * info_recv[None, :, 1], axis=1).reshape(cycles_here, per_cycle)
    divisor = jnp.repeat(1.0 + 0.25 * hit_weight, 128, axis=1)
    want_pick = want_hot.T.astype(jnp.bfloat16)

    current = start_map
    for iteration in range(ITERS):
        map_half = current.astype(jnp.bfloat16).reshape(blocks_here, 128)
        rows_out = jnp.dot(want_pick, map_half, preferred_element_type=jnp.float32)
        rows_out = rows_out.astype(jnp.bfloat16).reshape(owners, CAP * 128)
        if iteration == 0:
            rows_in = lax.all_to_all(rows_out, axes, 0, 0, tiled=True).reshape(slots, 128)
            owned = first_owned
        else:
            outward, cos_phase, sin_phase = coef_out(current)
            send_a = jnp.concatenate([rows_out, outward], axis=1)
            recv_a = lax.all_to_all(send_a, axes, 0, 0, tiled=True)
            rows_in = recv_a[:, : CAP * 128].reshape(slots, 128)
            owned = coef_in(recv_a[:, CAP * 128 :])

        picked = rows_in[slot].reshape(pix_block.shape + (128,))
        binned_terms = pointing_pallas(pointing, picked, samples, det_weight)
        binned_send = jnp.zeros((slots, 128), jnp.float32).at[slot].set(binned_terms.reshape(-1, 128))

        synth = legendre_pallas(owned, legendre, prior_gain, m_own)
        synth_send = synth.reshape(2, count_here, owners, cycles_here).transpose(2, 0, 1, 3)
        send_b = jnp.concatenate(
            [binned_send.reshape(owners, CAP * 128), synth_send.reshape(owners, -1)], axis=1
        )
        recv_b = lax.all_to_all(send_b, axes, 0, 0, tiled=True)
        binned_in = recv_b[:, : CAP * 128].reshape(slots, 128)
        binned = jnp.dot(want_hot, binned_in, precision=highest).reshape(cycles_here, length)
        returned = recv_b[:, CAP * 128 :].reshape(owners, 2, count_here, cycles_here)
        returned = returned.transpose(1, 0, 2, 3).reshape(2, owners * count_here, cycles_here)
        filtered = spectrum_back(
            returned[0].T, returned[1].T, cos_phase, sin_phase, m_values, length
        )
        current = current + (binned - filtered) / divisor
    return current


def solution(mesh):
    placed = (
        P("det", "tm", None),
        P("det", "tm", None, None),
        P("det", "tm"),
        P("det"),
        P(("det", "tm"), None),
        P(("det", "tm"), None, None),
        P(),
        P(),
        P(("det", "tm")),
    )
    return jax.shard_map(
        on_device, mesh=mesh, in_specs=placed, out_specs=P(("det", "tm"), None), check_vma=False
    )
```

```python
import math

import functools

import jax
import jax.numpy as jnp
from jax import lax
from jax.experimental import pallas as pl
from jax.experimental.pallas import tpu as pltpu
from jax.sharding import PartitionSpec as P

ITERS = 2


highest = lax.Precision.HIGHEST


def phase_pair(first_len, second_len, length, sign):
    first = jnp.arange(first_len, dtype=jnp.int32)[:, None]
    second = jnp.arange(second_len, dtype=jnp.int32)[None, :]
    phases = (first * second % length).astype(jnp.float32) * (sign * 2.0 * math.pi / length)
    return (jnp.cos(phases), jnp.sin(phases))


def forward_cycles(field):
    cycles, length = field.shape
    outer_len = length // 128
    shaped = field.reshape(cycles, outer_len, 128)
    cos_outer, sin_outer = phase_pair(outer_len, outer_len, outer_len, -1.0)
    part_re = jnp.einsum("mj,rjk->rmk", cos_outer, shaped, precision=highest)
    part_im = jnp.einsum("mj,rjk->rmk", sin_outer, shaped, precision=highest)
    cos_twist, sin_twist = phase_pair(outer_len, 128, length, -1.0)
    twist_re = part_re * cos_twist - part_im * sin_twist
    twist_im = part_re * sin_twist + part_im * cos_twist
    cos_inner, sin_inner = phase_pair(128, 128, 128, -1.0)
    spec_re = jnp.einsum("rmk,kn->rmn", twist_re, cos_inner, precision=highest) - jnp.einsum(
        "rmk,kn->rmn", twist_im, sin_inner, precision=highest
    )
    spec_im = jnp.einsum("rmk,kn->rmn", twist_re, sin_inner, precision=highest) + jnp.einsum(
        "rmk,kn->rmn", twist_im, cos_inner, precision=highest
    )
    return (spec_re.reshape(cycles, length), spec_im.reshape(cycles, length))


def inverse_cycles(spec_re, spec_im):
    cycles, length = spec_re.shape
    outer_len = length // 128
    shaped_re = spec_re.reshape(cycles, outer_len, 128)
    shaped_im = spec_im.reshape(cycles, outer_len, 128)
    cos_inner, sin_inner = phase_pair(128, 128, 128, 1.0)
    inner_re = jnp.einsum("rmn,nk->rmk", shaped_re, cos_inner, precision=highest) - jnp.einsum(
        "rmn,nk->rmk", shaped_im, sin_inner, precision=highest
    )
    inner_im = jnp.einsum("rmn,nk->rmk", shaped_re, sin_inner, precision=highest) + jnp.einsum(
        "rmn,nk->rmk", shaped_im, cos_inner, precision=highest
    )
    cos_twist, sin_twist = phase_pair(outer_len, 128, length, 1.0)
    twist_re = inner_re * cos_twist - inner_im * sin_twist
    twist_im = inner_re * sin_twist + inner_im * cos_twist
    cos_outer, sin_outer = phase_pair(outer_len, outer_len, outer_len, 1.0)
    field = jnp.einsum("jm,rmk->rjk", cos_outer, twist_re, precision=highest) - jnp.einsum(
        "jm,rmk->rjk", sin_outer, twist_im, precision=highest
    )
    return field.reshape(cycles, length)


def forward_band(field, band):
    cycles, length = field.shape
    outer_len = length // 128
    band_cols = band // outer_len
    shaped = field.reshape(cycles, outer_len, 128)
    cos_outer, sin_outer = phase_pair(outer_len, outer_len, outer_len, -1.0)
    part = jnp.einsum(
        "mj,rjk->rmk", jnp.concatenate([cos_outer, sin_outer], axis=0), shaped, precision=highest
    )
    part_re, part_im = part[:, :outer_len], part[:, outer_len:]
    cos_twist, sin_twist = phase_pair(outer_len, 128, length, -1.0)
    twist = jnp.concatenate(
        [part_re * cos_twist - part_im * sin_twist, part_re * sin_twist + part_im * cos_twist],
        axis=2,
    )
    cos_inner, sin_inner = phase_pair(128, band_cols, 128, -1.0)
    inner = jnp.concatenate(
        [jnp.concatenate([cos_inner, sin_inner], axis=1),
         jnp.concatenate([-sin_inner, cos_inner], axis=1)],
        axis=0,
    )
    spec = jnp.einsum("rmk,kn->rmn", twist, inner, precision=highest)
    return spec[:, :, :band_cols], spec[:, :, band_cols:]


def inverse_band(spec_re, spec_im, length):
    cycles, outer_len, band_cols = spec_re.shape
    cos_inner, sin_inner = phase_pair(band_cols, 128, 128, 1.0)
    inner = jnp.concatenate(
        [jnp.concatenate([cos_inner, sin_inner], axis=1),
         jnp.concatenate([-sin_inner, cos_inner], axis=1)],
        axis=0,
    )
    inner_out = jnp.einsum(
        "rmn,nk->rmk", jnp.concatenate([spec_re, spec_im], axis=2), inner, precision=highest
    )
    inner_re, inner_im = inner_out[:, :, :128], inner_out[:, :, 128:]
    cos_twist, sin_twist = phase_pair(outer_len, 128, length, 1.0)
    twist = jnp.concatenate(
        [inner_re * cos_twist - inner_im * sin_twist, inner_re * sin_twist + inner_im * cos_twist],
        axis=1,
    )
    cos_outer, sin_outer = phase_pair(outer_len, outer_len, outer_len, 1.0)
    outer = jnp.concatenate([cos_outer, -sin_outer], axis=1)
    field = jnp.einsum("jm,rmk->rjk", outer, twist, precision=highest)
    return field.reshape(cycles, length)


def legendre_filter(owned, legendre, prior_gain, m_own):
    count_here, degrees, total_cycles = legendre.shape
    block_rows = min(512, degrees)

    def one_block(index, running):
        start = index * block_rows
        table = lax.dynamic_slice_in_dim(legendre, start, block_rows, 1)
        analysed = jnp.einsum("mlr,cmr->cml", table, owned, preferred_element_type=jnp.float32)
        degree = start + jnp.arange(block_rows, dtype=jnp.int32)
        keep_rows = degree[None, :] >= m_own[:, None]
        gain_block = lax.dynamic_slice_in_dim(prior_gain, start, block_rows)
        scaled = jnp.where(keep_rows[None], analysed * gain_block, 0.0).astype(jnp.bfloat16)
        return running + jnp.einsum(
            "mlr,cml->cmr", table, scaled, preferred_element_type=jnp.float32
        )

    first_block = 0
    initial = jnp.zeros(owned.shape, jnp.float32)
    summed = lax.fori_loop(first_block, degrees // block_rows, one_block, initial)
    return summed * math.sqrt(total_cycles / degrees)


ROWS = 16


def legendre_body(m_ref, coef_ref, gain_ref, tab_ref, out_ref, *, scale, per):
    k = pl.program_id(0)
    for j in range(per):
        tab = tab_ref[j]
        coef = coef_ref[j]
        analysed = lax.dot_general(
            coef, tab, (((1,), (1,)), ((), ())), preferred_element_type=jnp.float32
        )
        degree = lax.broadcasted_iota(jnp.int32, analysed.shape, 1)
        keep = degree >= m_ref[k * per + j]
        scaled = jnp.where(keep, analysed * gain_ref[...], 0.0).astype(jnp.bfloat16)
        synth = jnp.dot(scaled, tab, preferred_element_type=jnp.float32)
        out_ref[j] = synth * scale


def legendre_pallas(owned, legendre, prior_gain, m_own):
    count_here, degrees, total_cycles = legendre.shape
    per = 2 if count_here % 2 == 0 else 1
    coef = jnp.pad(owned.transpose(1, 0, 2), ((0, 0), (0, ROWS - 2), (0, 0)))
    gain = prior_gain.reshape(1, degrees)
    grid_spec = pltpu.PrefetchScalarGridSpec(
        num_scalar_prefetch=1,
        grid=(count_here // per,),
        in_specs=[
            pl.BlockSpec((per, ROWS, total_cycles), lambda k, m: (k, 0, 0)),
            pl.BlockSpec((1, degrees), lambda k, m: (0, 0)),
            pl.BlockSpec((per, degrees, total_cycles), lambda k, m: (k, 0, 0)),
        ],
        out_specs=pl.BlockSpec((per, ROWS, total_cycles), lambda k, m: (k, 0, 0)),
    )
    out = pl.pallas_call(
        functools.partial(legendre_body, scale=math.sqrt(total_cycles / degrees), per=per),
        grid_spec=grid_spec,
        out_shape=jax.ShapeDtypeStruct((count_here, ROWS, total_cycles), jnp.float32),
    )(m_own, coef, gain, legendre)
    return out[:, :2, :].transpose(1, 0, 2)


def pointing_body(w_ref, p_ref, x_ref, s_ref, out_ref, *, tblk, nsamp, per):
    d = pl.program_id(0)
    for j in range(per):
        point = p_ref[j].reshape(tblk * nsamp, p_ref.shape[3])
        picked = x_ref[j]
        every = lax.dot_general(
            picked, point, (((1,), (1,)), ((), ())), preferred_element_type=jnp.float32
        )
        row = lax.broadcasted_iota(jnp.int32, every.shape, 0)
        col = lax.broadcasted_iota(jnp.int32, every.shape, 1)
        mine = row == col // nsamp
        predicted = jnp.sum(jnp.where(mine, every, 0.0), axis=0, keepdims=True)
        resid = (w_ref[d * per + j] * (s_ref[j] - predicted)).astype(jnp.bfloat16)
        spread = jnp.where(mine, jnp.broadcast_to(resid, every.shape), jnp.zeros_like(resid))
        out_ref[j] = jnp.dot(spread, point, preferred_element_type=jnp.float32)


def pointing_pallas(pointing, picked, samples, det_weight):
    dets, times, nsamp, npix = pointing.shape
    tblk = times
    per = 2 if dets % 2 == 0 else 1
    samples_row = samples.reshape(dets, 1, times * nsamp)
    grid_spec = pltpu.PrefetchScalarGridSpec(
        num_scalar_prefetch=1,
        grid=(dets // per,),
        in_specs=[
            pl.BlockSpec((per, tblk, nsamp, npix), lambda d, w: (d, 0, 0, 0)),
            pl.BlockSpec((per, tblk, npix), lambda d, w: (d, 0, 0)),
            pl.BlockSpec((per, 1, tblk * nsamp), lambda d, w: (d, 0, 0)),
        ],
        out_specs=pl.BlockSpec((per, tblk, npix), lambda d, w: (d, 0, 0)),
    )
    return pl.pallas_call(
        functools.partial(pointing_body, tblk=tblk, nsamp=nsamp, per=per),
        grid_spec=grid_spec,
        out_shape=jax.ShapeDtypeStruct((dets, times, npix), jnp.float32),
    )(det_weight, pointing, picked, samples_row)


CAP = 8


STRIDE = 4


def order_pick(m_values):
    count = m_values.shape[0]
    offset = m_values - STRIDE * jnp.arange(count, dtype=jnp.int32)
    return offset[:, None] == jnp.arange(STRIDE, dtype=jnp.int32)[None, :]


def spectrum_out(field, m_values, cycle_offset):
    cycles_here, length = field.shape
    count = m_values.shape[0]
    band = count * STRIDE
    spec_re, spec_im = forward_band(field, band)
    spec_re = spec_re.transpose(0, 2, 1).reshape(cycles_here, count, STRIDE)
    spec_im = spec_im.transpose(0, 2, 1).reshape(cycles_here, count, STRIDE)
    pick = order_pick(m_values)[None]
    pick_re = jnp.sum(jnp.where(pick, spec_re, 0.0), axis=2)
    pick_im = jnp.sum(jnp.where(pick, spec_im, 0.0), axis=2)
    phases = (m_values[None, :] * cycle_offset[:, None] % length).astype(jnp.float32) * (
        2.0 * math.pi / length
    )
    cos_phase = jnp.cos(phases)
    sin_phase = jnp.sin(phases)
    norm_factor = 1.0 / math.sqrt(length)
    coef_re = (pick_re * cos_phase + pick_im * sin_phase) * norm_factor
    coef_im = (pick_im * cos_phase - pick_re * sin_phase) * norm_factor
    return coef_re, coef_im, cos_phase, sin_phase


def spectrum_back(back_re, back_im, cos_phase, sin_phase, m_values, length):
    cycles_here = back_re.shape[0]
    count = m_values.shape[0]
    outer_len = length // 128
    mode_weight = jnp.where(m_values == 0, 1.0, 2.0).astype(jnp.float32)[None, :]
    harm_re = mode_weight * (back_re * cos_phase - back_im * sin_phase)
    harm_im = mode_weight * (back_re * sin_phase + back_im * cos_phase)
    pick = order_pick(m_values)[None]
    band_cols = count * STRIDE // outer_len
    full_re = jnp.where(pick, harm_re[:, :, None], 0.0).reshape(cycles_here, band_cols, outer_len)
    full_im = jnp.where(pick, harm_im[:, :, None], 0.0).reshape(cycles_here, band_cols, outer_len)
    full_re = full_re.transpose(0, 2, 1)
    full_im = full_im.transpose(0, 2, 1)
    return inverse_band(full_re, full_im, length) / math.sqrt(2.0 * count)


def on_device(
    samples,
    pointing,
    pix_block,
    det_weight,
    start_map,
    legendre,
    prior_gain,
    m_values,
    cycle_offset,
):
    axes = ("det", "tm")
    cycles_here, length = start_map.shape
    per_cycle = length // 128
    owners = lax.axis_size(axes)
    total_cycles = cycles_here * owners
    blocks_here = cycles_here * per_cycle
    count_here = legendre.shape[0]
    owner_index = lax.axis_index(axes)
    m_own = lax.dynamic_slice_in_dim(m_values, owner_index * count_here, count_here)
    slots = owners * CAP

    flat_pix = pix_block.reshape(-1)
    nloc = flat_pix.shape[0]
    owner_of = flat_pix // blocks_here
    within = flat_pix % blocks_here
    order = jnp.arange(nloc, dtype=jnp.int32)
    same = (owner_of[:, None] == owner_of[None, :]) & (order[None, :] < order[:, None])
    rank = jnp.sum(same.astype(jnp.int32), axis=1)
    slot = owner_of * CAP + rank
    weight_of = jnp.broadcast_to(det_weight[:, None], pix_block.shape).reshape(-1)
    info = jnp.stack([within.astype(jnp.float32), weight_of], axis=1)
    info = jnp.zeros((slots, 2), jnp.float32).at[slot].set(info).reshape(owners, CAP * 2)
    coef_width = 2 * count_here * cycles_here

    def coef_out(field):
        coef_re, coef_im, cos_phase, sin_phase = spectrum_out(field, m_values, cycle_offset)
        outward = jnp.stack([coef_re.T, coef_im.T]).astype(jnp.bfloat16)
        outward = outward.reshape(2, owners, count_here, cycles_here).transpose(1, 0, 2, 3)
        return outward.reshape(owners, coef_width), cos_phase, sin_phase

    def coef_in(part):
        owned = part.reshape(owners, 2, count_here, cycles_here).astype(jnp.bfloat16)
        return owned.transpose(1, 2, 0, 3).reshape(2, count_here, total_cycles)

    first_out, cos_phase, sin_phase = coef_out(start_map)
    info = jnp.concatenate([info, first_out.astype(jnp.float32)], axis=1)
    info_recv = lax.all_to_all(info, axes, 0, 0, tiled=True)
    first_owned = coef_in(info_recv[:, CAP * 2 :])
    info_recv = info_recv[:, : CAP * 2].reshape(slots, 2)
    want = info_recv[:, 0].astype(jnp.int32)
    want_hot = (want[None, :] == jnp.arange(blocks_here, dtype=jnp.int32)[:, None]).astype(jnp.float32)
    hit_weight = jnp.sum(want_hot * info_recv[None, :, 1], axis=1).reshape(cycles_here, per_cycle)
    divisor = jnp.repeat(1.0 + 0.25 * hit_weight, 128, axis=1)
    want_pick = want_hot.T.astype(jnp.bfloat16)

    current = start_map
    for iteration in range(ITERS):
        map_half = current.astype(jnp.bfloat16).reshape(blocks_here, 128)
        rows_out = jnp.dot(want_pick, map_half, preferred_element_type=jnp.float32)
        rows_out = rows_out.astype(jnp.bfloat16).reshape(owners, CAP * 128)
        if iteration == 0:
            rows_in = lax.all_to_all(rows_out, axes, 0, 0, tiled=True).reshape(slots, 128)
            owned = first_owned
        else:
            outward, cos_phase, sin_phase = coef_out(current)
            send_a = jnp.concatenate([rows_out, outward], axis=1)
            recv_a = lax.all_to_all(send_a, axes, 0, 0, tiled=True)
            rows_in = recv_a[:, : CAP * 128].reshape(slots, 128)
            owned = coef_in(recv_a[:, CAP * 128 :])

        picked = rows_in[slot].reshape(pix_block.shape + (128,))
        binned_terms = pointing_pallas(pointing, picked, samples, det_weight)
        binned_send = jnp.zeros((slots, 128), jnp.float32).at[slot].set(binned_terms.reshape(-1, 128))

        synth = legendre_pallas(owned, legendre, prior_gain, m_own)
        synth_send = synth.reshape(2, count_here, owners, cycles_here).transpose(2, 0, 1, 3)
        send_b = jnp.concatenate(
            [binned_send.reshape(owners, CAP * 128), synth_send.reshape(owners, -1)], axis=1
        )
        recv_b = lax.all_to_all(send_b, axes, 0, 0, tiled=True)
        binned_in = recv_b[:, : CAP * 128].reshape(slots, 128)
        binned = jnp.dot(want_hot, binned_in, precision=highest).reshape(cycles_here, length)
        returned = recv_b[:, CAP * 128 :].reshape(owners, 2, count_here, cycles_here)
        returned = returned.transpose(1, 0, 2, 3).reshape(2, owners * count_here, cycles_here)
        filtered = spectrum_back(
            returned[0].T, returned[1].T, cos_phase, sin_phase, m_values, length
        )
        current = current + (binned - filtered) / divisor
    return current


def solution(mesh):
    placed = (
        P("det", "tm", None),
        P("det", "tm", None, None),
        P("det", "tm"),
        P("det"),
        P(("det", "tm"), None),
        P(("det", "tm"), None, None),
        P(),
        P(),
        P(("det", "tm")),
    )
    return jax.shard_map(
        on_device, mesh=mesh, in_specs=placed, out_specs=P(("det", "tm"), None), check_vma=False
    )
```

```python
import math

import functools

import jax
import jax.numpy as jnp
from jax import lax
from jax.experimental import pallas as pl
from jax.experimental.pallas import tpu as pltpu
from jax.sharding import PartitionSpec as P

ITERS = 2


highest = lax.Precision.HIGH


def phase_pair(first_len, second_len, length, sign):
    first = jnp.arange(first_len, dtype=jnp.int32)[:, None]
    second = jnp.arange(second_len, dtype=jnp.int32)[None, :]
    phases = (first * second % length).astype(jnp.float32) * (sign * 2.0 * math.pi / length)
    return (jnp.cos(phases), jnp.sin(phases))


def forward_cycles(field):
    cycles, length = field.shape
    outer_len = length // 128
    shaped = field.reshape(cycles, outer_len, 128)
    cos_outer, sin_outer = phase_pair(outer_len, outer_len, outer_len, -1.0)
    part_re = jnp.einsum("mj,rjk->rmk", cos_outer, shaped, precision=highest)
    part_im = jnp.einsum("mj,rjk->rmk", sin_outer, shaped, precision=highest)
    cos_twist, sin_twist = phase_pair(outer_len, 128, length, -1.0)
    twist_re = part_re * cos_twist - part_im * sin_twist
    twist_im = part_re * sin_twist + part_im * cos_twist
    cos_inner, sin_inner = phase_pair(128, 128, 128, -1.0)
    spec_re = jnp.einsum("rmk,kn->rmn", twist_re, cos_inner, precision=highest) - jnp.einsum(
        "rmk,kn->rmn", twist_im, sin_inner, precision=highest
    )
    spec_im = jnp.einsum("rmk,kn->rmn", twist_re, sin_inner, precision=highest) + jnp.einsum(
        "rmk,kn->rmn", twist_im, cos_inner, precision=highest
    )
    return (spec_re.reshape(cycles, length), spec_im.reshape(cycles, length))


def inverse_cycles(spec_re, spec_im):
    cycles, length = spec_re.shape
    outer_len = length // 128
    shaped_re = spec_re.reshape(cycles, outer_len, 128)
    shaped_im = spec_im.reshape(cycles, outer_len, 128)
    cos_inner, sin_inner = phase_pair(128, 128, 128, 1.0)
    inner_re = jnp.einsum("rmn,nk->rmk", shaped_re, cos_inner, precision=highest) - jnp.einsum(
        "rmn,nk->rmk", shaped_im, sin_inner, precision=highest
    )
    inner_im = jnp.einsum("rmn,nk->rmk", shaped_re, sin_inner, precision=highest) + jnp.einsum(
        "rmn,nk->rmk", shaped_im, cos_inner, precision=highest
    )
    cos_twist, sin_twist = phase_pair(outer_len, 128, length, 1.0)
    twist_re = inner_re * cos_twist - inner_im * sin_twist
    twist_im = inner_re * sin_twist + inner_im * cos_twist
    cos_outer, sin_outer = phase_pair(outer_len, outer_len, outer_len, 1.0)
    field = jnp.einsum("jm,rmk->rjk", cos_outer, twist_re, precision=highest) - jnp.einsum(
        "jm,rmk->rjk", sin_outer, twist_im, precision=highest
    )
    return field.reshape(cycles, length)


def forward_band(field, band):
    cycles, length = field.shape
    outer_len = length // 128
    band_cols = band // outer_len
    shaped = field.reshape(cycles, outer_len, 128)
    cos_outer, sin_outer = phase_pair(outer_len, outer_len, outer_len, -1.0)
    part = jnp.einsum(
        "mj,rjk->rmk", jnp.concatenate([cos_outer, sin_outer], axis=0), shaped, precision=highest
    )
    part_re, part_im = part[:, :outer_len], part[:, outer_len:]
    cos_twist, sin_twist = phase_pair(outer_len, 128, length, -1.0)
    twist = jnp.concatenate(
        [part_re * cos_twist - part_im * sin_twist, part_re * sin_twist + part_im * cos_twist],
        axis=2,
    )
    cos_inner, sin_inner = phase_pair(128, band_cols, 128, -1.0)
    inner = jnp.concatenate(
        [jnp.concatenate([cos_inner, sin_inner], axis=1),
         jnp.concatenate([-sin_inner, cos_inner], axis=1)],
        axis=0,
    )
    spec = jnp.einsum("rmk,kn->rmn", twist, inner, precision=highest)
    return spec[:, :, :band_cols], spec[:, :, band_cols:]


def inverse_band(spec_re, spec_im, length):
    cycles, outer_len, band_cols = spec_re.shape
    cos_inner, sin_inner = phase_pair(band_cols, 128, 128, 1.0)
    inner = jnp.concatenate(
        [jnp.concatenate([cos_inner, sin_inner], axis=1),
         jnp.concatenate([-sin_inner, cos_inner], axis=1)],
        axis=0,
    )
    inner_out = jnp.einsum(
        "rmn,nk->rmk", jnp.concatenate([spec_re, spec_im], axis=2), inner, precision=highest
    )
    inner_re, inner_im = inner_out[:, :, :128], inner_out[:, :, 128:]
    cos_twist, sin_twist = phase_pair(outer_len, 128, length, 1.0)
    twist = jnp.concatenate(
        [inner_re * cos_twist - inner_im * sin_twist, inner_re * sin_twist + inner_im * cos_twist],
        axis=1,
    )
    cos_outer, sin_outer = phase_pair(outer_len, outer_len, outer_len, 1.0)
    outer = jnp.concatenate([cos_outer, -sin_outer], axis=1)
    field = jnp.einsum("jm,rmk->rjk", outer, twist, precision=highest)
    return field.reshape(cycles, length)


def legendre_filter(owned, legendre, prior_gain, m_own):
    count_here, degrees, total_cycles = legendre.shape
    block_rows = min(512, degrees)

    def one_block(index, running):
        start = index * block_rows
        table = lax.dynamic_slice_in_dim(legendre, start, block_rows, 1)
        analysed = jnp.einsum("mlr,cmr->cml", table, owned, preferred_element_type=jnp.float32)
        degree = start + jnp.arange(block_rows, dtype=jnp.int32)
        keep_rows = degree[None, :] >= m_own[:, None]
        gain_block = lax.dynamic_slice_in_dim(prior_gain, start, block_rows)
        scaled = jnp.where(keep_rows[None], analysed * gain_block, 0.0).astype(jnp.bfloat16)
        return running + jnp.einsum(
            "mlr,cml->cmr", table, scaled, preferred_element_type=jnp.float32
        )

    first_block = 0
    initial = jnp.zeros(owned.shape, jnp.float32)
    summed = lax.fori_loop(first_block, degrees // block_rows, one_block, initial)
    return summed * math.sqrt(total_cycles / degrees)


ROWS = 16


def legendre_body(m_ref, coef_ref, gain_ref, tab_ref, out_ref, *, scale, per):
    k = pl.program_id(0)
    for j in range(per):
        tab = tab_ref[j]
        coef = coef_ref[j]
        analysed = lax.dot_general(
            coef, tab, (((1,), (1,)), ((), ())), preferred_element_type=jnp.float32
        )
        degree = lax.broadcasted_iota(jnp.int32, analysed.shape, 1)
        keep = degree >= m_ref[k * per + j]
        scaled = jnp.where(keep, analysed * gain_ref[...], 0.0).astype(jnp.bfloat16)
        synth = jnp.dot(scaled, tab, preferred_element_type=jnp.float32)
        out_ref[j] = synth * scale


def legendre_pallas(owned, legendre, prior_gain, m_own):
    count_here, degrees, total_cycles = legendre.shape
    per = 2 if count_here % 2 == 0 else 1
    coef = jnp.pad(owned.transpose(1, 0, 2), ((0, 0), (0, ROWS - 2), (0, 0)))
    gain = prior_gain.reshape(1, degrees)
    grid_spec = pltpu.PrefetchScalarGridSpec(
        num_scalar_prefetch=1,
        grid=(count_here // per,),
        in_specs=[
            pl.BlockSpec((per, ROWS, total_cycles), lambda k, m: (k, 0, 0)),
            pl.BlockSpec((1, degrees), lambda k, m: (0, 0)),
            pl.BlockSpec((per, degrees, total_cycles), lambda k, m: (k, 0, 0)),
        ],
        out_specs=pl.BlockSpec((per, ROWS, total_cycles), lambda k, m: (k, 0, 0)),
    )
    out = pl.pallas_call(
        functools.partial(legendre_body, scale=math.sqrt(total_cycles / degrees), per=per),
        grid_spec=grid_spec,
        out_shape=jax.ShapeDtypeStruct((count_here, ROWS, total_cycles), jnp.float32),
    )(m_own, coef, gain, legendre)
    return out[:, :2, :].transpose(1, 0, 2)


def pointing_body(w_ref, p_ref, x_ref, s_ref, out_ref, *, tblk, nsamp, per):
    d = pl.program_id(0)
    for j in range(per):
        point = p_ref[j].reshape(tblk * nsamp, p_ref.shape[3])
        picked = x_ref[j]
        every = lax.dot_general(
            picked, point, (((1,), (1,)), ((), ())), preferred_element_type=jnp.float32
        )
        row = lax.broadcasted_iota(jnp.int32, every.shape, 0)
        col = lax.broadcasted_iota(jnp.int32, every.shape, 1)
        mine = row == col // nsamp
        predicted = jnp.sum(jnp.where(mine, every, 0.0), axis=0, keepdims=True)
        resid = (w_ref[d * per + j] * (s_ref[j] - predicted)).astype(jnp.bfloat16)
        spread = jnp.where(mine, jnp.broadcast_to(resid, every.shape), jnp.zeros_like(resid))
        out_ref[j] = jnp.dot(spread, point, preferred_element_type=jnp.float32)


def pointing_pallas(pointing, picked, samples, det_weight):
    dets, times, nsamp, npix = pointing.shape
    tblk = times
    per = 2 if dets % 2 == 0 else 1
    samples_row = samples.reshape(dets, 1, times * nsamp)
    grid_spec = pltpu.PrefetchScalarGridSpec(
        num_scalar_prefetch=1,
        grid=(dets // per,),
        in_specs=[
            pl.BlockSpec((per, tblk, nsamp, npix), lambda d, w: (d, 0, 0, 0)),
            pl.BlockSpec((per, tblk, npix), lambda d, w: (d, 0, 0)),
            pl.BlockSpec((per, 1, tblk * nsamp), lambda d, w: (d, 0, 0)),
        ],
        out_specs=pl.BlockSpec((per, tblk, npix), lambda d, w: (d, 0, 0)),
    )
    return pl.pallas_call(
        functools.partial(pointing_body, tblk=tblk, nsamp=nsamp, per=per),
        grid_spec=grid_spec,
        out_shape=jax.ShapeDtypeStruct((dets, times, npix), jnp.float32),
    )(det_weight, pointing, picked, samples_row)


CAP = 8


STRIDE = 4


def order_pick(m_values):
    count = m_values.shape[0]
    offset = m_values - STRIDE * jnp.arange(count, dtype=jnp.int32)
    return offset[:, None] == jnp.arange(STRIDE, dtype=jnp.int32)[None, :]


def spectrum_out(field, m_values, cycle_offset):
    cycles_here, length = field.shape
    count = m_values.shape[0]
    band = count * STRIDE
    spec_re, spec_im = forward_band(field, band)
    spec_re = spec_re.transpose(0, 2, 1).reshape(cycles_here, count, STRIDE)
    spec_im = spec_im.transpose(0, 2, 1).reshape(cycles_here, count, STRIDE)
    pick = order_pick(m_values)[None]
    pick_re = jnp.sum(jnp.where(pick, spec_re, 0.0), axis=2)
    pick_im = jnp.sum(jnp.where(pick, spec_im, 0.0), axis=2)
    phases = (m_values[None, :] * cycle_offset[:, None] % length).astype(jnp.float32) * (
        2.0 * math.pi / length
    )
    cos_phase = jnp.cos(phases)
    sin_phase = jnp.sin(phases)
    norm_factor = 1.0 / math.sqrt(length)
    coef_re = (pick_re * cos_phase + pick_im * sin_phase) * norm_factor
    coef_im = (pick_im * cos_phase - pick_re * sin_phase) * norm_factor
    return coef_re, coef_im, cos_phase, sin_phase


def spectrum_back(back_re, back_im, cos_phase, sin_phase, m_values, length):
    cycles_here = back_re.shape[0]
    count = m_values.shape[0]
    outer_len = length // 128
    mode_weight = jnp.where(m_values == 0, 1.0, 2.0).astype(jnp.float32)[None, :]
    harm_re = mode_weight * (back_re * cos_phase - back_im * sin_phase)
    harm_im = mode_weight * (back_re * sin_phase + back_im * cos_phase)
    pick = order_pick(m_values)[None]
    band_cols = count * STRIDE // outer_len
    full_re = jnp.where(pick, harm_re[:, :, None], 0.0).reshape(cycles_here, band_cols, outer_len)
    full_im = jnp.where(pick, harm_im[:, :, None], 0.0).reshape(cycles_here, band_cols, outer_len)
    full_re = full_re.transpose(0, 2, 1)
    full_im = full_im.transpose(0, 2, 1)
    return inverse_band(full_re, full_im, length) / math.sqrt(2.0 * count)


def on_device(
    samples,
    pointing,
    pix_block,
    det_weight,
    start_map,
    legendre,
    prior_gain,
    m_values,
    cycle_offset,
):
    axes = ("det", "tm")
    cycles_here, length = start_map.shape
    per_cycle = length // 128
    owners = lax.axis_size(axes)
    total_cycles = cycles_here * owners
    blocks_here = cycles_here * per_cycle
    count_here = legendre.shape[0]
    owner_index = lax.axis_index(axes)
    m_own = lax.dynamic_slice_in_dim(m_values, owner_index * count_here, count_here)
    slots = owners * CAP

    flat_pix = pix_block.reshape(-1)
    nloc = flat_pix.shape[0]
    owner_of = flat_pix // blocks_here
    within = flat_pix % blocks_here
    order = jnp.arange(nloc, dtype=jnp.int32)
    same = (owner_of[:, None] == owner_of[None, :]) & (order[None, :] < order[:, None])
    rank = jnp.sum(same.astype(jnp.int32), axis=1)
    slot = owner_of * CAP + rank
    weight_of = jnp.broadcast_to(det_weight[:, None], pix_block.shape).reshape(-1)
    info = jnp.stack([within.astype(jnp.float32), weight_of], axis=1)
    info = jnp.zeros((slots, 2), jnp.float32).at[slot].set(info).reshape(owners, CAP * 2)
    coef_width = 2 * count_here * cycles_here

    def coef_out(field):
        coef_re, coef_im, cos_phase, sin_phase = spectrum_out(field, m_values, cycle_offset)
        outward = jnp.stack([coef_re.T, coef_im.T]).astype(jnp.bfloat16)
        outward = outward.reshape(2, owners, count_here, cycles_here).transpose(1, 0, 2, 3)
        return outward.reshape(owners, coef_width), cos_phase, sin_phase

    def coef_in(part):
        owned = part.reshape(owners, 2, count_here, cycles_here).astype(jnp.bfloat16)
        return owned.transpose(1, 2, 0, 3).reshape(2, count_here, total_cycles)

    first_out, cos_phase, sin_phase = coef_out(start_map)
    info = jnp.concatenate([info, first_out.astype(jnp.float32)], axis=1)
    info_recv = lax.all_to_all(info, axes, 0, 0, tiled=True)
    first_owned = coef_in(info_recv[:, CAP * 2 :])
    info_recv = info_recv[:, : CAP * 2].reshape(slots, 2)
    want = info_recv[:, 0].astype(jnp.int32)
    want_hot = (want[None, :] == jnp.arange(blocks_here, dtype=jnp.int32)[:, None]).astype(jnp.float32)
    hit_weight = jnp.sum(want_hot * info_recv[None, :, 1], axis=1).reshape(cycles_here, per_cycle)
    divisor = jnp.repeat(1.0 + 0.25 * hit_weight, 128, axis=1)
    want_pick = want_hot.T.astype(jnp.bfloat16)

    current = start_map
    for iteration in range(ITERS):
        map_half = current.astype(jnp.bfloat16).reshape(blocks_here, 128)
        rows_out = jnp.dot(want_pick, map_half, preferred_element_type=jnp.float32)
        rows_out = rows_out.astype(jnp.bfloat16).reshape(owners, CAP * 128)
        if iteration == 0:
            rows_in = lax.all_to_all(rows_out, axes, 0, 0, tiled=True).reshape(slots, 128)
            owned = first_owned
        else:
            outward, cos_phase, sin_phase = coef_out(current)
            send_a = jnp.concatenate([rows_out, outward], axis=1)
            recv_a = lax.all_to_all(send_a, axes, 0, 0, tiled=True)
            rows_in = recv_a[:, : CAP * 128].reshape(slots, 128)
            owned = coef_in(recv_a[:, CAP * 128 :])

        picked = rows_in[slot].reshape(pix_block.shape + (128,))
        binned_terms = pointing_pallas(pointing, picked, samples, det_weight)
        binned_send = jnp.zeros((slots, 128), jnp.float32).at[slot].set(binned_terms.reshape(-1, 128))

        synth = legendre_pallas(owned, legendre, prior_gain, m_own)
        synth_send = synth.reshape(2, count_here, owners, cycles_here).transpose(2, 0, 1, 3)
        send_b = jnp.concatenate(
            [binned_send.reshape(owners, CAP * 128), synth_send.reshape(owners, -1)], axis=1
        )
        recv_b = lax.all_to_all(send_b, axes, 0, 0, tiled=True)
        binned_in = recv_b[:, : CAP * 128].reshape(slots, 128)
        binned = jnp.dot(want_hot, binned_in, precision=highest).reshape(cycles_here, length)
        returned = recv_b[:, CAP * 128 :].reshape(owners, 2, count_here, cycles_here)
        returned = returned.transpose(1, 0, 2, 3).reshape(2, owners * count_here, cycles_here)
        filtered = spectrum_back(
            returned[0].T, returned[1].T, cos_phase, sin_phase, m_values, length
        )
        current = current + (binned - filtered) / divisor
    return current


def solution(mesh):
    placed = (
        P("det", "tm", None),
        P("det", "tm", None, None),
        P("det", "tm"),
        P("det"),
        P(("det", "tm"), None),
        P(("det", "tm"), None, None),
        P(),
        P(),
        P(("det", "tm")),
    )
    return jax.shard_map(
        on_device, mesh=mesh, in_specs=placed, out_specs=P(("det", "tm"), None), check_vma=False
    )
```

```python
import math

import functools

import jax
import jax.numpy as jnp
from jax import lax
from jax.experimental import pallas as pl
from jax.experimental.pallas import tpu as pltpu
from jax.sharding import PartitionSpec as P

ITERS = 2


highest = lax.Precision.HIGHEST


def phase_pair(first_len, second_len, length, sign):
    first = jnp.arange(first_len, dtype=jnp.int32)[:, None]
    second = jnp.arange(second_len, dtype=jnp.int32)[None, :]
    phases = (first * second % length).astype(jnp.float32) * (sign * 2.0 * math.pi / length)
    return (jnp.cos(phases), jnp.sin(phases))


def forward_cycles(field):
    cycles, length = field.shape
    outer_len = length // 128
    shaped = field.reshape(cycles, outer_len, 128)
    cos_outer, sin_outer = phase_pair(outer_len, outer_len, outer_len, -1.0)
    part_re = jnp.einsum("mj,rjk->rmk", cos_outer, shaped, precision=highest)
    part_im = jnp.einsum("mj,rjk->rmk", sin_outer, shaped, precision=highest)
    cos_twist, sin_twist = phase_pair(outer_len, 128, length, -1.0)
    twist_re = part_re * cos_twist - part_im * sin_twist
    twist_im = part_re * sin_twist + part_im * cos_twist
    cos_inner, sin_inner = phase_pair(128, 128, 128, -1.0)
    spec_re = jnp.einsum("rmk,kn->rmn", twist_re, cos_inner, precision=highest) - jnp.einsum(
        "rmk,kn->rmn", twist_im, sin_inner, precision=highest
    )
    spec_im = jnp.einsum("rmk,kn->rmn", twist_re, sin_inner, precision=highest) + jnp.einsum(
        "rmk,kn->rmn", twist_im, cos_inner, precision=highest
    )
    return (spec_re.reshape(cycles, length), spec_im.reshape(cycles, length))


def inverse_cycles(spec_re, spec_im):
    cycles, length = spec_re.shape
    outer_len = length // 128
    shaped_re = spec_re.reshape(cycles, outer_len, 128)
    shaped_im = spec_im.reshape(cycles, outer_len, 128)
    cos_inner, sin_inner = phase_pair(128, 128, 128, 1.0)
    inner_re = jnp.einsum("rmn,nk->rmk", shaped_re, cos_inner, precision=highest) - jnp.einsum(
        "rmn,nk->rmk", shaped_im, sin_inner, precision=highest
    )
    inner_im = jnp.einsum("rmn,nk->rmk", shaped_re, sin_inner, precision=highest) + jnp.einsum(
        "rmn,nk->rmk", shaped_im, cos_inner, precision=highest
    )
    cos_twist, sin_twist = phase_pair(outer_len, 128, length, 1.0)
    twist_re = inner_re * cos_twist - inner_im * sin_twist
    twist_im = inner_re * sin_twist + inner_im * cos_twist
    cos_outer, sin_outer = phase_pair(outer_len, outer_len, outer_len, 1.0)
    field = jnp.einsum("jm,rmk->rjk", cos_outer, twist_re, precision=highest) - jnp.einsum(
        "jm,rmk->rjk", sin_outer, twist_im, precision=highest
    )
    return field.reshape(cycles, length)


def forward_band(field, band):
    cycles, length = field.shape
    outer_len = length // 128
    band_cols = band // outer_len
    shaped = field.reshape(cycles, outer_len, 128)
    cos_outer, sin_outer = phase_pair(outer_len, outer_len, outer_len, -1.0)
    part = jnp.einsum(
        "mj,rjk->rmk", jnp.concatenate([cos_outer, sin_outer], axis=0), shaped, precision=highest
    )
    part_re, part_im = part[:, :outer_len], part[:, outer_len:]
    cos_twist, sin_twist = phase_pair(outer_len, 128, length, -1.0)
    twist = jnp.concatenate(
        [part_re * cos_twist - part_im * sin_twist, part_re * sin_twist + part_im * cos_twist],
        axis=2,
    )
    cos_inner, sin_inner = phase_pair(128, band_cols, 128, -1.0)
    inner = jnp.concatenate(
        [jnp.concatenate([cos_inner, sin_inner], axis=1),
         jnp.concatenate([-sin_inner, cos_inner], axis=1)],
        axis=0,
    )
    spec = jnp.einsum("rmk,kn->rmn", twist, inner, precision=highest)
    return spec[:, :, :band_cols], spec[:, :, band_cols:]


def inverse_band(spec_re, spec_im, length):
    cycles, outer_len, band_cols = spec_re.shape
    cos_inner, sin_inner = phase_pair(band_cols, 128, 128, 1.0)
    inner = jnp.concatenate(
        [jnp.concatenate([cos_inner, sin_inner], axis=1),
         jnp.concatenate([-sin_inner, cos_inner], axis=1)],
        axis=0,
    )
    inner_out = jnp.einsum(
        "rmn,nk->rmk", jnp.concatenate([spec_re, spec_im], axis=2), inner, precision=highest
    )
    inner_re, inner_im = inner_out[:, :, :128], inner_out[:, :, 128:]
    cos_twist, sin_twist = phase_pair(outer_len, 128, length, 1.0)
    twist = jnp.concatenate(
        [inner_re * cos_twist - inner_im * sin_twist, inner_re * sin_twist + inner_im * cos_twist],
        axis=1,
    )
    cos_outer, sin_outer = phase_pair(outer_len, outer_len, outer_len, 1.0)
    outer = jnp.concatenate([cos_outer, -sin_outer], axis=1)
    field = jnp.einsum("jm,rmk->rjk", outer, twist, precision=highest)
    return field.reshape(cycles, length)


def legendre_filter(owned, legendre, prior_gain, m_own):
    count_here, degrees, total_cycles = legendre.shape
    block_rows = min(512, degrees)

    def one_block(index, running):
        start = index * block_rows
        table = lax.dynamic_slice_in_dim(legendre, start, block_rows, 1)
        analysed = jnp.einsum("mlr,cmr->cml", table, owned, preferred_element_type=jnp.float32)
        degree = start + jnp.arange(block_rows, dtype=jnp.int32)
        keep_rows = degree[None, :] >= m_own[:, None]
        gain_block = lax.dynamic_slice_in_dim(prior_gain, start, block_rows)
        scaled = jnp.where(keep_rows[None], analysed * gain_block, 0.0).astype(jnp.bfloat16)
        return running + jnp.einsum(
            "mlr,cml->cmr", table, scaled, preferred_element_type=jnp.float32
        )

    first_block = 0
    initial = jnp.zeros(owned.shape, jnp.float32)
    summed = lax.fori_loop(first_block, degrees // block_rows, one_block, initial)
    return summed * math.sqrt(total_cycles / degrees)


ROWS = 16


def legendre_body(m_ref, coef_ref, gain_ref, tab_ref, out_ref, *, scale, per):
    k = pl.program_id(0)
    for j in range(per):
        tab = tab_ref[j]
        coef = coef_ref[j]
        analysed = lax.dot_general(
            coef, tab, (((1,), (1,)), ((), ())), preferred_element_type=jnp.float32
        )
        degree = lax.broadcasted_iota(jnp.int32, analysed.shape, 1)
        keep = degree >= m_ref[k * per + j]
        scaled = jnp.where(keep, analysed * gain_ref[...], 0.0).astype(jnp.bfloat16)
        synth = jnp.dot(scaled, tab, preferred_element_type=jnp.float32)
        out_ref[j] = synth * scale


def legendre_pallas(owned, legendre, prior_gain, m_own):
    count_here, degrees, total_cycles = legendre.shape
    per = 2 if count_here % 2 == 0 else 1
    coef = jnp.pad(owned.transpose(1, 0, 2), ((0, 0), (0, ROWS - 2), (0, 0)))
    gain = prior_gain.reshape(1, degrees)
    grid_spec = pltpu.PrefetchScalarGridSpec(
        num_scalar_prefetch=1,
        grid=(count_here // per,),
        in_specs=[
            pl.BlockSpec((per, ROWS, total_cycles), lambda k, m: (k, 0, 0)),
            pl.BlockSpec((1, degrees), lambda k, m: (0, 0)),
            pl.BlockSpec((per, degrees, total_cycles), lambda k, m: (k, 0, 0)),
        ],
        out_specs=pl.BlockSpec((per, ROWS, total_cycles), lambda k, m: (k, 0, 0)),
    )
    out = pl.pallas_call(
        functools.partial(legendre_body, scale=math.sqrt(total_cycles / degrees), per=per),
        grid_spec=grid_spec,
        out_shape=jax.ShapeDtypeStruct((count_here, ROWS, total_cycles), jnp.float32),
    )(m_own, coef, gain, legendre)
    return out[:, :2, :].transpose(1, 0, 2)


def pointing_body(w_ref, p_ref, x_ref, s_ref, out_ref, *, tblk, nsamp, per):
    d = pl.program_id(0)
    for j in range(per):
        point = p_ref[j].reshape(tblk * nsamp, p_ref.shape[3])
        picked = x_ref[j]
        every = lax.dot_general(
            picked, point, (((1,), (1,)), ((), ())), preferred_element_type=jnp.float32
        )
        row = lax.broadcasted_iota(jnp.int32, every.shape, 0)
        col = lax.broadcasted_iota(jnp.int32, every.shape, 1)
        mine = row == col // nsamp
        predicted = jnp.sum(jnp.where(mine, every, 0.0), axis=0, keepdims=True)
        resid = (w_ref[d * per + j] * (s_ref[j] - predicted)).astype(jnp.bfloat16)
        spread = jnp.where(mine, jnp.broadcast_to(resid, every.shape), jnp.zeros_like(resid))
        out_ref[j] = jnp.dot(spread, point, preferred_element_type=jnp.float32)


def pointing_pallas(pointing, picked, samples, det_weight):
    dets, times, nsamp, npix = pointing.shape
    tblk = times
    per = 2 if dets % 2 == 0 else 1
    samples_row = samples.reshape(dets, 1, times * nsamp)
    grid_spec = pltpu.PrefetchScalarGridSpec(
        num_scalar_prefetch=1,
        grid=(dets // per,),
        in_specs=[
            pl.BlockSpec((per, tblk, nsamp, npix), lambda d, w: (d, 0, 0, 0)),
            pl.BlockSpec((per, tblk, npix), lambda d, w: (d, 0, 0)),
            pl.BlockSpec((per, 1, tblk * nsamp), lambda d, w: (d, 0, 0)),
        ],
        out_specs=pl.BlockSpec((per, tblk, npix), lambda d, w: (d, 0, 0)),
    )
    return pl.pallas_call(
        functools.partial(pointing_body, tblk=tblk, nsamp=nsamp, per=per),
        grid_spec=grid_spec,
        out_shape=jax.ShapeDtypeStruct((dets, times, npix), jnp.float32),
    )(det_weight, pointing, picked, samples_row)


CAP = 8


STRIDE = 4


def order_pick(m_values):
    count = m_values.shape[0]
    offset = m_values - STRIDE * jnp.arange(count, dtype=jnp.int32)
    return offset[:, None] == jnp.arange(STRIDE, dtype=jnp.int32)[None, :]


def spectrum_out(field, m_values, cycle_offset):
    cycles_here, length = field.shape
    count = m_values.shape[0]
    band = count * STRIDE
    spec_re, spec_im = forward_band(field, band)
    spec_re = spec_re.transpose(0, 2, 1).reshape(cycles_here, count, STRIDE)
    spec_im = spec_im.transpose(0, 2, 1).reshape(cycles_here, count, STRIDE)
    pick = order_pick(m_values)[None]
    pick_re = jnp.sum(jnp.where(pick, spec_re, 0.0), axis=2)
    pick_im = jnp.sum(jnp.where(pick, spec_im, 0.0), axis=2)
    phases = (m_values[None, :] * cycle_offset[:, None] % length).astype(jnp.float32) * (
        2.0 * math.pi / length
    )
    cos_phase = jnp.cos(phases)
    sin_phase = jnp.sin(phases)
    norm_factor = 1.0 / math.sqrt(length)
    coef_re = (pick_re * cos_phase + pick_im * sin_phase) * norm_factor
    coef_im = (pick_im * cos_phase - pick_re * sin_phase) * norm_factor
    return coef_re, coef_im, cos_phase, sin_phase


def spectrum_back(back_re, back_im, cos_phase, sin_phase, m_values, length):
    cycles_here = back_re.shape[0]
    count = m_values.shape[0]
    outer_len = length // 128
    mode_weight = jnp.where(m_values == 0, 1.0, 2.0).astype(jnp.float32)[None, :]
    harm_re = mode_weight * (back_re * cos_phase - back_im * sin_phase)
    harm_im = mode_weight * (back_re * sin_phase + back_im * cos_phase)
    pick = order_pick(m_values)[None]
    band_cols = count * STRIDE // outer_len
    full_re = jnp.where(pick, harm_re[:, :, None], 0.0).reshape(cycles_here, band_cols, outer_len)
    full_im = jnp.where(pick, harm_im[:, :, None], 0.0).reshape(cycles_here, band_cols, outer_len)
    full_re = full_re.transpose(0, 2, 1)
    full_im = full_im.transpose(0, 2, 1)
    return inverse_band(full_re, full_im, length) / math.sqrt(2.0 * count)


def on_device(
    samples,
    pointing,
    pix_block,
    det_weight,
    start_map,
    legendre,
    prior_gain,
    m_values,
    cycle_offset,
):
    axes = ("det", "tm")
    cycles_here, length = start_map.shape
    per_cycle = length // 128
    owners = lax.axis_size(axes)
    total_cycles = cycles_here * owners
    blocks_here = cycles_here * per_cycle
    count_here = legendre.shape[0]
    owner_index = lax.axis_index(axes)
    m_own = lax.dynamic_slice_in_dim(m_values, owner_index * count_here, count_here)
    slots = owners * CAP

    flat_pix = pix_block.reshape(-1)
    nloc = flat_pix.shape[0]
    owner_of = flat_pix // blocks_here
    within = flat_pix % blocks_here
    order = jnp.arange(nloc, dtype=jnp.int32)
    same = (owner_of[:, None] == owner_of[None, :]) & (order[None, :] < order[:, None])
    rank = jnp.sum(same.astype(jnp.int32), axis=1)
    slot = owner_of * CAP + rank
    weight_of = jnp.broadcast_to(det_weight[:, None], pix_block.shape).reshape(-1)
    info = jnp.stack([within.astype(jnp.float32), weight_of], axis=1)
    info = jnp.zeros((slots, 2), jnp.float32).at[slot].set(info).reshape(owners, CAP * 2)
    coef_width = 2 * count_here * cycles_here

    def coef_out(field):
        coef_re, coef_im, cos_phase, sin_phase = spectrum_out(field, m_values, cycle_offset)
        outward = jnp.stack([coef_re.T, coef_im.T]).astype(jnp.bfloat16)
        outward = outward.reshape(2, owners, count_here, cycles_here).transpose(1, 0, 2, 3)
        return outward.reshape(owners, coef_width), cos_phase, sin_phase

    def coef_in(part):
        owned = part.reshape(owners, 2, count_here, cycles_here).astype(jnp.bfloat16)
        return owned.transpose(1, 2, 0, 3).reshape(2, count_here, total_cycles)

    first_out, cos_phase, sin_phase = coef_out(start_map)
    info = jnp.concatenate([info, first_out.astype(jnp.float32)], axis=1)
    info_recv = lax.all_to_all(info, axes, 0, 0, tiled=True)
    first_owned = coef_in(info_recv[:, CAP * 2 :])
    info_recv = info_recv[:, : CAP * 2].reshape(slots, 2)
    want = info_recv[:, 0].astype(jnp.int32)
    want_hot = (want[None, :] == jnp.arange(blocks_here, dtype=jnp.int32)[:, None]).astype(jnp.float32)
    hit_weight = jnp.sum(want_hot * info_recv[None, :, 1], axis=1).reshape(cycles_here, per_cycle)
    divisor = jnp.repeat(1.0 + 0.25 * hit_weight, 128, axis=1)
    want_pick = want_hot.T.astype(jnp.bfloat16)

    current = start_map
    for iteration in range(ITERS):
        map_half = current.astype(jnp.bfloat16).reshape(blocks_here, 128)
        rows_out = jnp.dot(want_pick, map_half, preferred_element_type=jnp.float32)
        rows_out = rows_out.astype(jnp.bfloat16).reshape(owners, CAP * 128)
        if iteration == 0:
            rows_in = lax.all_to_all(rows_out, axes, 0, 0, tiled=True).reshape(slots, 128)
            owned = first_owned
        else:
            outward, cos_phase, sin_phase = coef_out(current)
            send_a = jnp.concatenate([rows_out, outward], axis=1)
            recv_a = lax.all_to_all(send_a, axes, 0, 0, tiled=True)
            rows_in = recv_a[:, : CAP * 128].reshape(slots, 128)
            owned = coef_in(recv_a[:, CAP * 128 :])

        picked = rows_in[slot].reshape(pix_block.shape + (128,))
        binned_terms = pointing_pallas(pointing, picked, samples, det_weight)
        binned_send = jnp.zeros((slots, 128), jnp.float32).at[slot].set(binned_terms.reshape(-1, 128))

        synth = legendre_pallas(owned, legendre, prior_gain, m_own)
        synth_send = synth.reshape(2, count_here, owners, cycles_here).transpose(2, 0, 1, 3)
        send_b = jnp.concatenate(
            [binned_send.reshape(owners, CAP * 128), synth_send.reshape(owners, -1)], axis=1
        )
        recv_b = lax.all_to_all(send_b, axes, 0, 0, tiled=True)
        binned_in = recv_b[:, : CAP * 128].reshape(slots, 128)
        piece_hi = binned_in.astype(jnp.bfloat16)
        rest = binned_in - piece_hi.astype(jnp.float32)
        piece_mid = rest.astype(jnp.bfloat16)
        piece_lo = (rest - piece_mid.astype(jnp.float32)).astype(jnp.bfloat16)
        hot_half = want_hot.astype(jnp.bfloat16)
        binned = sum(
            jnp.dot(hot_half, piece, preferred_element_type=jnp.float32)
            for piece in (piece_lo, piece_mid, piece_hi)
        ).reshape(cycles_here, length)
        returned = recv_b[:, CAP * 128 :].reshape(owners, 2, count_here, cycles_here)
        returned = returned.transpose(1, 0, 2, 3).reshape(2, owners * count_here, cycles_here)
        filtered = spectrum_back(
            returned[0].T, returned[1].T, cos_phase, sin_phase, m_values, length
        )
        current = current + (binned - filtered) / divisor
    return current


def solution(mesh):
    placed = (
        P("det", "tm", None),
        P("det", "tm", None, None),
        P("det", "tm"),
        P("det"),
        P(("det", "tm"), None),
        P(("det", "tm"), None, None),
        P(),
        P(),
        P(("det", "tm")),
    )
    return jax.shard_map(
        on_device, mesh=mesh, in_specs=placed, out_specs=P(("det", "tm"), None), check_vma=False
    )
```
